32 devices in a mesh: groups: 2 (over y), tensor: 4 (over z), store: 4 (over x, core).
Axes of the slice: x: 2, y: 2, z: 4, core: 2. Of those that a mesh axis runs over, the one named last changes fastest.
Arguments:
- x_new: bfloat16 [128, 8192], P('groups', 'store'), parts along dimension 0, may hold values from -6 to 6
- kv_pages: bfloat16 [8, 160, 128, 2048], P(('groups', 'store'), 'tensor'), parts along dimension 0, may hold values from -6 to 6
- w_query: bfloat16 [8192, 8192], P('store', 'tensor'), may hold values from -3 to 3
- w_keyval: bfloat16 [8192, 2048], P('store'), may hold values from -0.0625 to 0.0625
- w_out: bfloat16 [8192, 8192], P('tensor', 'store'), may hold values from -0.0625 to 0.0625
- lengths: int32 [2], P('groups'), parts along dimension 0, may hold values from 4096 to 32768, as said below
- page_store: int32 [512, 1], P('groups'), parts along dimension 0, may hold values from 0 to 3; in each aligned block of 256 rows (0 to 255, 256 to 511, ...) at most 160 rows name the same one
- offsets: int32 [2], P('groups'), parts along dimension 0, may hold values from 0 to 8191
Outputs:
- attn_out: bfloat16 [128, 8192], P(('groups', 'tensor'), 'store'), parts along dimension 0
The draws below stay inside these ranges and needn't reach their ends.
There are 2 independent parts, one for each index of `groups`. The reference program is written for one: setup_inputs(seed, part) draws one part's arguments, and reference() takes and returns one part's arrays. A program takes and returns all parts, laid end to end along the dimension named above; an argument that names none is the same for every part. Nothing has to cross between parts.
Inputs may be any that keep to these rules, and one draw needn't show every extreme that they name: `lengths`: one session in every draw has exactly 32768 tokens. `page_store`: at most 160 pages of a group lie on one store shard, and some shard holds exactly 160.
All inputs are finite; a program needn't handle non-finite values.
Results may differ from the reference program's by a relative error of at most 0.019.
The reference program's roundings to bfloat16 on the way count: a program that leaves them out, or rounds other values in their place, can miss the bound.
Values may be sent and summed in bfloat16 or wider, within the bound.
No kernel may reach another device: no remote copies, remote signals or barrier semaphores. Data moves between devices by JAX's collectives and lax.ppermute only.
A program may use at most 192 MiB of HBM per device.

```python
import math
import jax
import jax.numpy as jnp
import numpy as np
from jax import lax

D = 8192
HQ = 64
KVH = 8
HD = 128
PAGE = 128
TURN = 64
MAXPAGES = 256
SESS = 1
TOK = 64
CAP = 160
N_STORE = 4


def draw_lengths(key, part):
    longest = MAXPAGES * PAGE
    base_len = jax.random.randint(jax.random.fold_in(key, 11), (SESS,), longest // 8, longest + 1)
    chosen = jax.random.randint(jax.random.fold_in(key, 12), (), 0, SESS)
    return jnp.where(jnp.arange(SESS) == chosen, longest, base_len).astype(jnp.int32)


def draw_w_query(key, part):
    base_vals = jax.random.truncated_normal(jax.random.fold_in(key, 21), -3.0, 3.0, (D, HQ * HD), jnp.float32) * D ** (-0.5)
    return jnp.clip(base_vals, -3.0, 3.0).astype(jnp.bfloat16)


def level_of(stream_key, dims, pieces, smallest, top_value):
    level = 1.0
    for axis_at, shards_of in pieces:
        steps = jax.random.uniform(jax.random.fold_in(jax.random.fold_in(stream_key, 6), axis_at), (shards_of,), jnp.float32, smallest / len(pieces), top_value / len(pieces))
        level = level * jnp.repeat(jnp.exp(steps), dims[axis_at] // shards_of).reshape((-1,) + (1,) * (len(dims) - 1 - axis_at))
    return level


def shared_out(key, own, number, rows, number_of, top, limit, skew):
    sequence = jax.random.permutation(key, number_of)
    packed, ordinary = shares(number_of, rows * top, limit, skew, True), shares(number_of, rows * top, limit, skew, False)
    places = jnp.arange(number_of)

    def named(sizes, rotation):
        used = int((sizes > 0).sum())
        fixed = max(1, used // 4)
        passed = fixed + (places - fixed + rotation * (used - fixed)) % max(1, number_of - fixed)
        return jnp.zeros((number_of,), jnp.int32).at[sequence[jnp.where(places < fixed, places, passed)]].set(jnp.asarray(sizes, jnp.int32))

    sizes = jnp.where(number % 4 == 0, named(packed, number // 4), named(ordinary, number - number // 4 - 1))
    mixed = jax.random.permutation(jax.random.fold_in(own, 3), number_of)
    giver, sink = mixed[0:number_of // 2 * 2:2], mixed[1:number_of // 2 * 2:2]
    margin = jnp.minimum(sizes[giver] - 1, limit - sizes[sink]) // 2
    margin = jnp.where((giver == sequence[0]) | (sink == sequence[0]) | (sizes[sink] == 0), 0, jnp.maximum(margin, 0))
    passed = jax.random.randint(jax.random.fold_in(own, 4), (number_of // 2,), 0, 1 << 20) % (margin + 1)
    sizes = sizes.at[giver].add(-passed).at[sink].add(passed)
    labels = jnp.searchsorted(jnp.cumsum(sizes), jnp.arange(rows * top), side="right").astype(jnp.int32)
    table = labels.reshape(top, rows).T
    table = table[jax.random.permutation(jax.random.fold_in(own, 1), rows)]
    rotation = jax.random.randint(jax.random.fold_in(own, 2), (rows, 1), 0, top)
    return jnp.take_along_axis(table, (jnp.arange(top)[None, :] + rotation) % top, axis=1)


def shares(count, total, bound, skew, full):
    loads = [(1 << 20) // math.isqrt(grade ** skew) + 1 for grade in range(1, count + 1)]
    largest = bound if full else min(bound, max(-(-total // count), total * loads[0] // sum(loads)))
    least = 1 if total - largest >= count - 1 else 0
    counts, spare = [largest] + [least] * (count - 1), total - largest - least * (count - 1)
    while spare > 0:
        movable = [i for i in range(1, count) if counts[i] < largest] or [i for i in range(1, count) if counts[i] < bound]
        whole, left = sum([loads[i] for i in movable]), spare
        for i in movable:
            more = min(bound - counts[i], max(1, left * loads[i] // whole), spare)
            counts[i] = counts[i] + more
            spare = spare - more
    return np.array(counts)


def centred(own_key, dims, deviation, most, cuts=(), kind=jnp.bfloat16):
    drawn = deviation * jax.random.normal(own_key, dims, jnp.float32)
    if cuts:
        drawn = drawn * level_of(own_key, dims, cuts, -0.22, 0.18)
    return jnp.clip(drawn, -most, most).astype(kind)


def setup_inputs(seed: int = 0, part: int = 0) -> dict:
    streams_of = jax.random.split(jax.random.key(seed), 9)
    part_keys = jax.random.split(jax.random.fold_in(streams_of[8], part), 9)
    x_new = centred(part_keys[0], (TOK, D), 1.0, 6.0, ((1, 4),))
    kv_pages = centred(part_keys[1], (N_STORE, CAP, PAGE, 2 * KVH * HD), 1.0, 6.0, ((0, 4), (1, 4)))
    w_query = draw_w_query(jax.random.fold_in(streams_of[8], 71), part)
    w_keyval = centred(streams_of[3], (D, 2 * KVH * HD), D ** -0.5, 0.0625, ((0, 4),))
    w_out = centred(streams_of[4], (HQ * HD, D), (HQ * HD) ** -0.5, 0.0625, ((0, 4), (1, 4)))
    lengths = draw_lengths(jax.random.fold_in(jax.random.fold_in(streams_of[8], part), 71), part)
    page_store_keys = jax.random.split(jax.random.fold_in(part_keys[6], 1), (SESS * MAXPAGES) // (SESS * MAXPAGES))
    page_store_turns = jax.random.permutation(jax.random.fold_in(part_keys[6], 3), (SESS * MAXPAGES) // (SESS * MAXPAGES))
    page_store = jax.vmap(lambda own, number: shared_out(jax.random.fold_in(part_keys[6], 2), own, number, SESS * MAXPAGES, N_STORE, 1, CAP, 2))(page_store_keys, page_store_turns).reshape((SESS * MAXPAGES, 1))
    offsets = jax.random.randint(part_keys[7], (SESS,), 0, 8192).astype(jnp.int32)
    return dict(x_new=x_new, kv_pages=kv_pages, w_query=w_query, w_keyval=w_keyval, w_out=w_out, lengths=lengths, page_store=page_store, offsets=offsets)


THETA = 500000.0
NEG_FILL = -1.0e30
ROPE_FACTOR = 8.0
LOW_FACTOR = 1.0
HIGH_FACTOR = 4.0
INITIAL_CONTEXT = 8192.0


def inverse_freq(width):
    steps_half = jnp.arange(width // 2, dtype=jnp.float32)
    base_freq = jnp.exp(-(steps_half * (2.0 / width)) * jnp.log(jnp.float32(THETA)))
    wavelength = (2.0 * math.pi) / base_freq
    low_wave = INITIAL_CONTEXT / LOW_FACTOR
    high_wave = INITIAL_CONTEXT / HIGH_FACTOR
    smooth = (INITIAL_CONTEXT / wavelength - LOW_FACTOR) / (HIGH_FACTOR - LOW_FACTOR)
    blended = (1.0 - smooth) * base_freq / ROPE_FACTOR + smooth * base_freq
    scaled = jnp.where(wavelength > low_wave, base_freq / ROPE_FACTOR, blended)
    return jnp.where(wavelength < high_wave, base_freq, scaled)


def rotate(values, rot_angle):
    half_width = values.shape[-1] // 2
    first_half = values[..., :half_width]
    second_half = values[..., half_width:]
    cosine = jnp.cos(rot_angle)
    sine_part = jnp.sin(rot_angle)
    return jnp.concatenate([first_half * cosine - second_half * sine_part, second_half * cosine + first_half * sine_part], axis=-1)


def to_half(values):
    return lax.optimization_barrier(values.astype(jnp.bfloat16))


def page_positions(page_store, shards, capacity):
    store_of = page_store[:, 0]
    onehot = (store_of[:, None] == jnp.arange(shards, dtype=jnp.int32)[None, :]).astype(jnp.int32)
    ranks = jnp.sum((jnp.cumsum(onehot, axis=0) - onehot) * onehot, axis=1)
    return (store_of * capacity + ranks).astype(jnp.int32)


def reference(x_new, kv_pages, w_query, w_keyval, w_out, lengths, page_store, offsets):
    score_scale = 1.0 / (HD ** 0.5)
    freq_table = inverse_freq(HD)
    group_size = HQ // KVH
    query_all = jnp.dot(x_new, w_query, preferred_element_type=jnp.float32).reshape(TOK, HQ, HD)
    keyval_all = jnp.dot(x_new, w_keyval, preferred_element_type=jnp.float32).reshape(TOK, KVH, 2, HD)
    tok_ids = jnp.arange(TOK, dtype=jnp.int32)
    tok_sess = tok_ids // TURN
    tok_pos = lengths[tok_sess] + tok_ids % TURN
    tok_angle = tok_pos.astype(jnp.float32)[:, None, None] * freq_table
    query_rot = to_half(rotate(query_all, tok_angle))
    key_new = to_half(rotate(keyval_all[:, :, 0], tok_angle))
    value_new = to_half(keyval_all[:, :, 1])
    positions = page_positions(page_store, N_STORE, CAP)
    pool = kv_pages.reshape(N_STORE * CAP, PAGE, KVH, 2, HD)
    hist_len = MAXPAGES * PAGE
    causal = jnp.arange(TURN)[None, :] <= jnp.arange(TURN)[:, None]
    outputs = []
    for session in range(SESS):
        page_rows = jnp.take(pool, positions[session * MAXPAGES:(session + 1) * MAXPAGES], axis=0)
        page_rows = page_rows.reshape(hist_len, KVH, 2, HD)
        hist_angle = offsets[session].astype(jnp.float32) * freq_table
        key_hist = to_half(rotate(page_rows[:, :, 0].astype(jnp.float32), hist_angle))
        value_hist = page_rows[:, :, 1]
        hist_valid = jnp.arange(hist_len) < lengths[session]
        allowed = jnp.concatenate([jnp.broadcast_to(hist_valid[None, :], (TURN, hist_len)), causal], axis=1)
        key_every = jnp.concatenate([key_hist, key_new[session * TURN:(session + 1) * TURN]], axis=0)
        value_every = jnp.concatenate([value_hist, value_new[session * TURN:(session + 1) * TURN]], axis=0)
        query_sess = query_rot[session * TURN:(session + 1) * TURN].reshape(TURN, KVH, group_size, HD)

        def one_head(head_idx):
            query_head = lax.dynamic_index_in_dim(query_sess, head_idx, 1, False)
            key_head = lax.dynamic_index_in_dim(key_every, head_idx, 1, False)
            value_head = lax.dynamic_index_in_dim(value_every, head_idx, 1, False)
            scores = jnp.einsum('tgd,nd->gtn', query_head.astype(jnp.float32), key_head.astype(jnp.float32)) * score_scale
            scores = jnp.where(allowed[None], scores, NEG_FILL)
            row_top = jnp.max(scores, axis=-1, keepdims=True)
            weights = jnp.where(allowed[None], jnp.exp(scores - row_top), 0.0)
            weight_sum = jnp.sum(weights, axis=-1)
            rounded = to_half(weights).astype(jnp.float32)
            head_mix = jnp.einsum('gtn,nd->tgd', rounded, value_head.astype(jnp.float32))
            return head_mix / jnp.transpose(weight_sum)[:, :, None]

        per_head = lax.map(one_head, jnp.arange(KVH, dtype=jnp.int32))
        outputs.append(jnp.transpose(per_head, (1, 0, 2, 3)).reshape(TURN, HQ * HD))
    attended = jnp.concatenate(outputs, axis=0).astype(jnp.bfloat16)
    return jnp.dot(attended, w_out, preferred_element_type=jnp.float32).astype(jnp.bfloat16)
```

```python
import math

import jax
import jax.numpy as jnp
import numpy as np
from jax import lax
from jax.sharding import PartitionSpec as P
from jax.experimental import pallas as pl
from jax.experimental.pallas import tpu as pltpu
import functools

HQ = 64
KVH = 8
HD = 128
TURN = 64
MAXPAGES = 256


THETA = 500000.0
NEG_FILL = -1e30
ROPE_FACTOR = 8.0
LOW_FACTOR = 1.0
HIGH_FACTOR = 4.0
INITIAL_CONTEXT = 8192.0


def joined(x, axis, combine):
    everything = jax.tree.map(lambda part: lax.all_gather(part, axis), x)
    first = jax.tree.map(lambda part: part[0], everything)

    def step(k, so_far):
        return combine(so_far, jax.tree.map(lambda part: part[k], everything))

    return lax.fori_loop(1, lax.axis_size(axis), step, first)


def inverse_freq(width):
    steps_half = jnp.arange(width // 2, dtype=jnp.float32)
    base_freq = jnp.exp(-(steps_half * (2.0 / width)) * jnp.log(jnp.float32(THETA)))
    wavelength = 2.0 * math.pi / base_freq
    low_wave = INITIAL_CONTEXT / LOW_FACTOR
    high_wave = INITIAL_CONTEXT / HIGH_FACTOR
    smooth = (INITIAL_CONTEXT / wavelength - LOW_FACTOR) / (HIGH_FACTOR - LOW_FACTOR)
    blended = (1.0 - smooth) * base_freq / ROPE_FACTOR + smooth * base_freq
    scaled = jnp.where(wavelength > low_wave, base_freq / ROPE_FACTOR, blended)
    return jnp.where(wavelength < high_wave, base_freq, scaled)


def rotate(values, rot_angle):
    half_width = values.shape[-1] // 2
    first_half = values[..., :half_width]
    second_half = values[..., half_width:]
    cosine = jnp.cos(rot_angle)
    sine_part = jnp.sin(rot_angle)
    return jnp.concatenate(
        [
            first_half * cosine - second_half * sine_part,
            second_half * cosine + first_half * sine_part,
        ],
        axis=-1,
    )


def to_half(values):
    return values.astype(jnp.bfloat16)


def table_lookup(table, index):
    hits = index[..., None] == jnp.arange(table.shape[0], dtype=jnp.int32)
    return jnp.sum(jnp.where(hits, table, 0), axis=-1)


def page_positions(page_store, shards, capacity):
    store_of = page_store[:, 0]
    onehot = (store_of[:, None] == jnp.arange(shards, dtype=jnp.int32)[None, :]).astype(jnp.int32)
    ranks = jnp.sum((jnp.cumsum(onehot, axis=0) - onehot) * onehot, axis=1)
    return store_of * capacity + ranks


def slot_meta(page_store, lengths, offsets, shards, capacity, first_slot, slot_count, page_len):
    positions = page_positions(page_store, shards, capacity)
    wanted = first_slot + jnp.arange(slot_count, dtype=jnp.int32)
    matches = (positions[:, None] == wanted[None, :]).astype(jnp.int32)
    page_ids = jnp.sum(matches * jnp.arange(positions.shape[0], dtype=jnp.int32)[:, None], axis=0)
    filled = jnp.sum(matches, axis=0) > 0
    slot_sess = page_ids // MAXPAGES
    slot_page = page_ids % MAXPAGES
    key_pos = slot_page[:, None] * page_len + jnp.arange(page_len, dtype=jnp.int32)[None, :]
    key_ok = filled[:, None] & (key_pos < table_lookup(lengths, slot_sess)[:, None])
    key_sess = jnp.broadcast_to(slot_sess[:, None], (slot_count, page_len))
    key_off = jnp.broadcast_to(table_lookup(offsets, slot_sess)[:, None], (slot_count, page_len))
    return (key_sess.reshape(-1), key_ok.reshape(-1), key_off.reshape(-1))


def attend(query, key_rows, value_rows, allowed):
    score_scale = 1.0 / query.shape[-1] ** 0.5
    scores = (
        jnp.einsum("tkgd,nkd->tkgn", query, key_rows, preferred_element_type=jnp.float32)
        * score_scale
    )
    wide_mask = allowed[:, None, None, :]
    scores = jnp.where(wide_mask, scores, NEG_FILL)
    row_top = jnp.max(scores, axis=-1)
    weights = jnp.where(wide_mask, jnp.exp(scores - row_top[..., None]), 0.0)
    weight_sum = jnp.sum(weights, axis=-1)
    head_mix = jnp.einsum(
        "tkgn,nkd->tkgd",
        weights.astype(jnp.bfloat16),
        value_rows,
        preferred_element_type=jnp.float32,
    )
    return (row_top, weight_sum, head_mix)


def combine(first_part, second_part):
    new_top = jnp.maximum(first_part[0], second_part[0])
    first_factor = jnp.exp(first_part[0] - new_top)
    second_factor = jnp.exp(second_part[0] - new_top)
    summed = first_part[1] * first_factor + second_part[1] * second_factor
    mixed_sum = first_part[2] * first_factor[..., None] + second_part[2] * second_factor[..., None]
    return (new_top, summed, mixed_sum)


MASK_FILL = -3e30


def hist_kernel(q_ref, kv_ref, bias_ref, cos_ref, sin_ref, acc_out, m_out, l_out, m_sc, l_sc, acc_sc, *, scale, blocks):
    j = pl.program_id(1)

    @pl.when(j == 0)
    def _():
        m_sc[...] = jnp.full(m_sc.shape, NEG_FILL, jnp.float32)
        l_sc[...] = jnp.zeros(l_sc.shape, jnp.float32)
        acc_sc[...] = jnp.zeros(acc_sc.shape, jnp.float32)

    pages, page_len, width = kv_ref.shape
    hd = width // 2
    n = pages * page_len
    keys = kv_ref[:, :, :hd].reshape(n, hd).astype(jnp.float32)
    vals = kv_ref[:, :, hd:].reshape(n, hd)
    keys = (keys * cos_ref[...] + pltpu.roll(keys, hd // 2, 1) * sin_ref[...]).astype(jnp.bfloat16)
    scores = lax.dot_general(
        q_ref[0], keys, (((1,), (1,)), ((), ())), preferred_element_type=jnp.float32
    )
    scores = scores * scale + bias_ref[0]
    m_old = m_sc[...]
    m_new = jnp.maximum(m_old, jnp.max(scores, axis=1, keepdims=True))
    alpha = jnp.exp(m_old - m_new)
    weights = jnp.exp(scores - m_new)
    l_sc[...] = alpha * l_sc[...] + jnp.sum(weights, axis=1, keepdims=True)
    acc_sc[...] = alpha * acc_sc[...] + jnp.dot(
        weights.astype(jnp.bfloat16), vals, preferred_element_type=jnp.float32
    )
    m_sc[...] = m_new

    @pl.when(j == blocks - 1)
    def _():
        acc_out[0] = acc_sc[...]
        m_out[0] = m_sc[...]
        l_out[0] = l_sc[...]


def hist_attend(q_k, kv_local, bias, cos2, sin2, pb):
    kv_heads, rows, hd = q_k.shape
    slots, page_len, width = kv_local.shape
    blocks = slots // pb
    kernel = functools.partial(hist_kernel, scale=1.0 / hd ** 0.5, blocks=blocks)
    return pl.pallas_call(
        kernel,
        grid=(kv_heads, blocks),
        in_specs=[
            pl.BlockSpec((1, rows, hd), lambda h, j: (h, 0, 0)),
            pl.BlockSpec((pb, page_len, 2 * hd), lambda h, j: (j, 0, h)),
            pl.BlockSpec((1, 1, pb * page_len), lambda h, j: (j, 0, 0)),
            pl.BlockSpec((1, hd), lambda h, j: (0, 0)),
            pl.BlockSpec((1, hd), lambda h, j: (0, 0)),
        ],
        out_specs=[
            pl.BlockSpec((1, rows, hd), lambda h, j: (h, 0, 0)),
            pl.BlockSpec((1, rows, 1), lambda h, j: (h, 0, 0)),
            pl.BlockSpec((1, rows, 1), lambda h, j: (h, 0, 0)),
        ],
        out_shape=[
            jax.ShapeDtypeStruct((kv_heads, rows, hd), jnp.float32),
            jax.ShapeDtypeStruct((kv_heads, rows, 1), jnp.float32),
            jax.ShapeDtypeStruct((kv_heads, rows, 1), jnp.float32),
        ],
        scratch_shapes=[
            pltpu.VMEM((rows, 1), jnp.float32),
            pltpu.VMEM((rows, 1), jnp.float32),
            pltpu.VMEM((rows, hd), jnp.float32),
        ],
        compiler_params=pltpu.CompilerParams(dimension_semantics=("parallel", "arbitrary")),
    )(q_k, kv_local, bias, cos2, sin2)


def body(x_new, kv_pages, w_query, w_keyval, w_out, lengths, page_store, offsets):
    tensors = lax.axis_size("tensor")
    shards = lax.axis_size("store")
    tensor_idx = lax.axis_index("tensor")
    store_idx = lax.axis_index("store")
    tok_count = x_new.shape[0]
    assert tok_count == TURN and lengths.shape[0] == 1
    local_slots = kv_pages.shape[1]
    capacity = local_slots * tensors
    page_len = kv_pages.shape[2]
    kv_heads = kv_pages.shape[3] // (2 * HD)
    group_size = HQ // KVH
    local_heads = w_query.shape[1] // HD
    local_kv = max(1, local_heads // group_size)
    local_group = local_heads // local_kv
    freq_table = inverse_freq(HD)
    kv_first = tensor_idx * local_heads // group_size
    keyval_cols = lax.dynamic_slice_in_dim(w_keyval, kv_first * (2 * HD), local_kv * 2 * HD, 1)
    query_part = jnp.dot(x_new, w_query, preferred_element_type=jnp.float32)
    keyval_part = jnp.dot(x_new, keyval_cols, preferred_element_type=jnp.float32)
    query_sum, keyval_sum = lax.psum((query_part, keyval_part), "store")
    keyval_local = keyval_sum.reshape(tok_count, local_kv, 2, HD)
    tok_ids = jnp.arange(tok_count, dtype=jnp.int32)
    tok_sess = tok_ids // TURN
    tok_pos = table_lookup(lengths, tok_sess) + tok_ids % TURN
    tok_angle = tok_pos.astype(jnp.float32)[:, None, None] * freq_table
    query_rot = to_half(rotate(query_sum.reshape(tok_count, local_heads, HD), tok_angle))
    key_new = to_half(rotate(keyval_local[:, :, 0], tok_angle))
    value_new = to_half(keyval_local[:, :, 1])

    q_all = lax.all_gather(jnp.transpose(query_rot, (1, 0, 2)), "tensor", axis=0, tiled=True)
    q_k = q_all.reshape(kv_heads, group_size * tok_count, HD)

    first_slot = store_idx * capacity + tensor_idx * local_slots
    key_sess, key_ok, key_off = slot_meta(
        page_store, lengths, offsets, shards, capacity, first_slot, local_slots, page_len
    )
    pb = 8 if local_slots % 8 == 0 else local_slots
    bias = jnp.where(key_ok, 0.0, MASK_FILL).astype(jnp.float32)
    bias = bias.reshape(local_slots // pb, 1, pb * page_len)
    hist_angle = offsets[0].astype(jnp.float32) * freq_table
    cosine = jnp.cos(hist_angle)
    sine = jnp.sin(hist_angle)
    cos2 = jnp.concatenate([cosine, cosine])[None, :]
    sin2 = jnp.concatenate([-sine, sine])[None, :]
    kv_local = kv_pages.reshape(local_slots, page_len, kv_pages.shape[3])
    acc, top, total = hist_attend(q_k, kv_local, bias, cos2, sin2, pb)
    acc = acc.reshape(HQ, tok_count, HD)
    top = top.reshape(HQ, tok_count)
    total = total.reshape(HQ, tok_count)

    glob_top = lax.pmax(top, ("tensor", "store"))
    factor = jnp.exp(top - glob_top)
    acc = acc * factor[..., None]
    total = total * factor
    acc, total = lax.psum_scatter((acc, total), "tensor", scatter_dimension=0, tiled=True)
    acc, total = lax.psum((acc, total), "store")
    loc_top = lax.dynamic_slice_in_dim(glob_top, tensor_idx * local_heads, local_heads, 0)
    hist_part = (
        jnp.transpose(loc_top),
        jnp.transpose(total),
        jnp.transpose(acc, (1, 0, 2)),
    )

    query_local = query_rot.reshape(tok_count, local_kv, local_group, HD)
    new_allowed = (tok_sess[:, None] == tok_sess[None, :]) & (tok_ids[None, :] <= tok_ids[:, None])
    new_part = attend(query_local, key_new, value_new, new_allowed)
    new_flat = (
        new_part[0].reshape(tok_count, local_heads),
        new_part[1].reshape(tok_count, local_heads),
        new_part[2].reshape(tok_count, local_heads, HD),
    )
    combined = combine(hist_part, new_flat)
    attended = (
        (combined[2] / combined[1][..., None])
        .reshape(tok_count, local_heads * HD)
        .astype(jnp.bfloat16)
    )
    result = lax.psum_scatter(
        jnp.dot(attended, w_out, preferred_element_type=jnp.float32),
        "tensor",
        scatter_dimension=0,
        tiled=True,
    )
    return result.astype(jnp.bfloat16)


def solution(mesh):
    in_specs = (
        P("groups", "store"),
        P(("groups", "store"), "tensor", None, None),
        P("store", "tensor"),
        P("store", None),
        P("tensor", "store"),
        P("groups"),
        P("groups", None),
        P("groups"),
    )
    out_specs = P(("groups", "tensor"), "store")
    return jax.shard_map(body, mesh=mesh, in_specs=in_specs, out_specs=out_specs, check_vma=False)
```

```python
import math

import jax
import jax.numpy as jnp
import numpy as np
from jax import lax
from jax.sharding import PartitionSpec as P
from jax.experimental import pallas as pl
from jax.experimental.pallas import tpu as pltpu
import functools

HQ = 64
KVH = 8
HD = 128
TURN = 64
MAXPAGES = 256


THETA = 500000.0
NEG_FILL = -1e30
ROPE_FACTOR = 8.0
LOW_FACTOR = 1.0
HIGH_FACTOR = 4.0
INITIAL_CONTEXT = 8192.0


def joined(x, axis, combine):
    everything = jax.tree.map(lambda part: lax.all_gather(part, axis), x)
    first = jax.tree.map(lambda part: part[0], everything)

    def step(k, so_far):
        return combine(so_far, jax.tree.map(lambda part: part[k], everything))

    return lax.fori_loop(1, lax.axis_size(axis), step, first)


def inverse_freq(width):
    steps_half = jnp.arange(width // 2, dtype=jnp.float32)
    base_freq = jnp.exp(-(steps_half * (2.0 / width)) * jnp.log(jnp.float32(THETA)))
    wavelength = 2.0 * math.pi / base_freq
    low_wave = INITIAL_CONTEXT / LOW_FACTOR
    high_wave = INITIAL_CONTEXT / HIGH_FACTOR
    smooth = (INITIAL_CONTEXT / wavelength - LOW_FACTOR) / (HIGH_FACTOR - LOW_FACTOR)
    blended = (1.0 - smooth) * base_freq / ROPE_FACTOR + smooth * base_freq
    scaled = jnp.where(wavelength > low_wave, base_freq / ROPE_FACTOR, blended)
    return jnp.where(wavelength < high_wave, base_freq, scaled)


def rotate(values, rot_angle):
    half_width = values.shape[-1] // 2
    first_half = values[..., :half_width]
    second_half = values[..., half_width:]
    cosine = jnp.cos(rot_angle)
    sine_part = jnp.sin(rot_angle)
    return jnp.concatenate(
        [
            first_half * cosine - second_half * sine_part,
            second_half * cosine + first_half * sine_part,
        ],
        axis=-1,
    )


def to_half(values):
    return values.astype(jnp.bfloat16)


def table_lookup(table, index):
    hits = index[..., None] == jnp.arange(table.shape[0], dtype=jnp.int32)
    return jnp.sum(jnp.where(hits, table, 0), axis=-1)


def page_positions(page_store, shards, capacity):
    store_of = page_store[:, 0]
    onehot = (store_of[:, None] == jnp.arange(shards, dtype=jnp.int32)[None, :]).astype(jnp.int32)
    ranks = jnp.sum((jnp.cumsum(onehot, axis=0) - onehot) * onehot, axis=1)
    return store_of * capacity + ranks


def slot_meta(page_store, lengths, offsets, shards, capacity, first_slot, slot_count, page_len):
    positions = page_positions(page_store, shards, capacity)
    wanted = first_slot + jnp.arange(slot_count, dtype=jnp.int32)
    matches = (positions[:, None] == wanted[None, :]).astype(jnp.int32)
    page_ids = jnp.sum(matches * jnp.arange(positions.shape[0], dtype=jnp.int32)[:, None], axis=0)
    filled = jnp.sum(matches, axis=0) > 0
    slot_sess = page_ids // MAXPAGES
    slot_page = page_ids % MAXPAGES
    key_pos = slot_page[:, None] * page_len + jnp.arange(page_len, dtype=jnp.int32)[None, :]
    key_ok = filled[:, None] & (key_pos < table_lookup(lengths, slot_sess)[:, None])
    key_sess = jnp.broadcast_to(slot_sess[:, None], (slot_count, page_len))
    key_off = jnp.broadcast_to(table_lookup(offsets, slot_sess)[:, None], (slot_count, page_len))
    return (key_sess.reshape(-1), key_ok.reshape(-1), key_off.reshape(-1))


def attend(query, key_rows, value_rows, allowed):
    score_scale = 1.0 / query.shape[-1] ** 0.5
    scores = (
        jnp.einsum("tkgd,nkd->tkgn", query, key_rows, preferred_element_type=jnp.float32)
        * score_scale
    )
    wide_mask = allowed[:, None, None, :]
    scores = jnp.where(wide_mask, scores, NEG_FILL)
    row_top = jnp.max(scores, axis=-1)
    weights = jnp.where(wide_mask, jnp.exp(scores - row_top[..., None]), 0.0)
    weight_sum = jnp.sum(weights, axis=-1)
    head_mix = jnp.einsum(
        "tkgn,nkd->tkgd",
        weights.astype(jnp.bfloat16),
        value_rows,
        preferred_element_type=jnp.float32,
    )
    return (row_top, weight_sum, head_mix)


def combine(first_part, second_part):
    new_top = jnp.maximum(first_part[0], second_part[0])
    first_factor = jnp.exp(first_part[0] - new_top)
    second_factor = jnp.exp(second_part[0] - new_top)
    summed = first_part[1] * first_factor + second_part[1] * second_factor
    mixed_sum = first_part[2] * first_factor[..., None] + second_part[2] * second_factor[..., None]
    return (new_top, summed, mixed_sum)


MASK_FILL = -3e30


def hist_kernel(q_ref, kv_ref, bias_ref, cos_ref, sin_ref, acc_out, m_out, l_out, m_sc, l_sc, acc_sc, *, scale, blocks):
    j = pl.program_id(1)

    @pl.when(j == 0)
    def _():
        m_sc[...] = jnp.full(m_sc.shape, NEG_FILL, jnp.float32)
        l_sc[...] = jnp.zeros(l_sc.shape, jnp.float32)
        acc_sc[...] = jnp.zeros(acc_sc.shape, jnp.float32)

    pages, page_len, width = kv_ref.shape
    hd = width // 2
    n = pages * page_len
    keys = kv_ref[:, :, :hd].reshape(n, hd).astype(jnp.float32)
    vals = kv_ref[:, :, hd:].reshape(n, hd)
    keys = (keys * cos_ref[...] + pltpu.roll(keys, hd // 2, 1) * sin_ref[...]).astype(jnp.bfloat16)
    scores = lax.dot_general(
        q_ref[0], keys, (((1,), (1,)), ((), ())), preferred_element_type=jnp.float32
    )
    scores = scores * scale + bias_ref[0]
    m_old = m_sc[...]
    m_new = jnp.maximum(m_old, jnp.max(scores, axis=1, keepdims=True))
    alpha = jnp.exp(m_old - m_new)
    weights = jnp.exp(scores - m_new)
    l_sc[...] = alpha * l_sc[...] + jnp.sum(weights, axis=1, keepdims=True)
    acc_sc[...] = alpha * acc_sc[...] + jnp.dot(
        weights.astype(jnp.bfloat16), vals, preferred_element_type=jnp.float32
    )
    m_sc[...] = m_new

    @pl.when(j == blocks - 1)
    def _():
        acc_out[0] = acc_sc[...]
        m_out[0] = m_sc[...]
        l_out[0] = l_sc[...]


def hist_attend(q_k, kv_local, bias, cos2, sin2, pb):
    kv_heads, rows, hd = q_k.shape
    slots, page_len, width = kv_local.shape
    blocks = slots // pb
    kernel = functools.partial(hist_kernel, scale=1.0 / hd ** 0.5, blocks=blocks)
    return pl.pallas_call(
        kernel,
        grid=(kv_heads, blocks),
        in_specs=[
            pl.BlockSpec((1, rows, hd), lambda h, j: (h, 0, 0)),
            pl.BlockSpec((pb, page_len, 2 * hd), lambda h, j: (j, 0, h)),
            pl.BlockSpec((1, 1, pb * page_len), lambda h, j: (j, 0, 0)),
            pl.BlockSpec((1, hd), lambda h, j: (0, 0)),
            pl.BlockSpec((1, hd), lambda h, j: (0, 0)),
        ],
        out_specs=[
            pl.BlockSpec((1, rows, hd), lambda h, j: (h, 0, 0)),
            pl.BlockSpec((1, rows, 1), lambda h, j: (h, 0, 0)),
            pl.BlockSpec((1, rows, 1), lambda h, j: (h, 0, 0)),
        ],
        out_shape=[
            jax.ShapeDtypeStruct((kv_heads, rows, hd), jnp.float32),
            jax.ShapeDtypeStruct((kv_heads, rows, 1), jnp.float32),
            jax.ShapeDtypeStruct((kv_heads, rows, 1), jnp.float32),
        ],
        scratch_shapes=[
            pltpu.VMEM((rows, 1), jnp.float32),
            pltpu.VMEM((rows, 1), jnp.float32),
            pltpu.VMEM((rows, hd), jnp.float32),
        ],
        compiler_params=pltpu.CompilerParams(dimension_semantics=("parallel", "arbitrary")),
    )(q_k, kv_local, bias, cos2, sin2)


def body(x_new, kv_pages, w_query, w_keyval, w_out, lengths, page_store, offsets):
    tensors = lax.axis_size("tensor")
    shards = lax.axis_size("store")
    tensor_idx = lax.axis_index("tensor")
    store_idx = lax.axis_index("store")
    tok_count = x_new.shape[0]
    assert tok_count == TURN and lengths.shape[0] == 1
    local_slots = kv_pages.shape[1]
    capacity = local_slots * tensors
    page_len = kv_pages.shape[2]
    kv_heads = kv_pages.shape[3] // (2 * HD)
    group_size = HQ // KVH
    local_heads = w_query.shape[1] // HD
    local_kv = max(1, local_heads // group_size)
    local_group = local_heads // local_kv
    freq_table = inverse_freq(HD)
    kv_first = tensor_idx * local_heads // group_size
    keyval_cols = lax.dynamic_slice_in_dim(w_keyval, kv_first * (2 * HD), local_kv * 2 * HD, 1)
    query_part = jnp.dot(x_new, w_query, preferred_element_type=jnp.float32)
    keyval_part = jnp.dot(x_new, keyval_cols, preferred_element_type=jnp.float32)
    query_sum, keyval_sum = lax.psum((query_part, keyval_part), "store")
    keyval_local = keyval_sum.reshape(tok_count, local_kv, 2, HD)
    tok_ids = jnp.arange(tok_count, dtype=jnp.int32)
    tok_sess = tok_ids // TURN
    tok_pos = table_lookup(lengths, tok_sess) + tok_ids % TURN
    tok_angle = tok_pos.astype(jnp.float32)[:, None, None] * freq_table
    query_rot = to_half(rotate(query_sum.reshape(tok_count, local_heads, HD), tok_angle))
    key_new = to_half(rotate(keyval_local[:, :, 0], tok_angle))
    value_new = to_half(keyval_local[:, :, 1])

    q_all = lax.all_gather(jnp.transpose(query_rot, (1, 0, 2)), "tensor", axis=0, tiled=True)
    q_k = q_all.reshape(kv_heads, group_size * tok_count, HD)

    first_slot = store_idx * capacity + tensor_idx * local_slots
    key_sess, key_ok, key_off = slot_meta(
        page_store, lengths, offsets, shards, capacity, first_slot, local_slots, page_len
    )
    pb = 8 if local_slots % 8 == 0 else local_slots
    bias = jnp.where(key_ok, 0.0, MASK_FILL).astype(jnp.float32)
    bias = bias.reshape(local_slots // pb, 1, pb * page_len)
    hist_angle = offsets[0].astype(jnp.float32) * freq_table
    cosine = jnp.cos(hist_angle)
    sine = jnp.sin(hist_angle)
    cos2 = jnp.concatenate([cosine, cosine])[None, :]
    sin2 = jnp.concatenate([-sine, sine])[None, :]
    kv_local = kv_pages.reshape(local_slots, page_len, kv_pages.shape[3])
    acc, top, total = hist_attend(q_k, kv_local, bias, cos2, sin2, pb)
    acc = acc.reshape(HQ, tok_count, HD)
    top = top.reshape(HQ, tok_count)
    total = total.reshape(HQ, tok_count)

    glob_top = jnp.max(lax.all_gather(top, ("tensor", "store")), axis=0)
    factor = jnp.exp(top - glob_top)
    packed = jnp.concatenate(
        [(acc * factor[..., None]).reshape(HQ, tok_count * HD), total * factor], axis=1
    )
    packed = lax.psum_scatter(packed, "tensor", scatter_dimension=0, tiled=True)
    packed = lax.psum(packed, "store")
    acc = packed[:, : tok_count * HD].reshape(local_heads, tok_count, HD)
    total = packed[:, tok_count * HD :]
    loc_top = lax.dynamic_slice_in_dim(glob_top, tensor_idx * local_heads, local_heads, 0)
    hist_part = (
        jnp.transpose(loc_top),
        jnp.transpose(total),
        jnp.transpose(acc, (1, 0, 2)),
    )

    query_local = query_rot.reshape(tok_count, local_kv, local_group, HD)
    new_allowed = (tok_sess[:, None] == tok_sess[None, :]) & (tok_ids[None, :] <= tok_ids[:, None])
    new_part = attend(query_local, key_new, value_new, new_allowed)
    new_flat = (
        new_part[0].reshape(tok_count, local_heads),
        new_part[1].reshape(tok_count, local_heads),
        new_part[2].reshape(tok_count, local_heads, HD),
    )
    combined = combine(hist_part, new_flat)
    attended = (
        (combined[2] / combined[1][..., None])
        .reshape(tok_count, local_heads * HD)
        .astype(jnp.bfloat16)
    )
    result = lax.psum_scatter(
        jnp.dot(attended, w_out, preferred_element_type=jnp.float32),
        "tensor",
        scatter_dimension=0,
        tiled=True,
    )
    return result.astype(jnp.bfloat16)


def solution(mesh):
    in_specs = (
        P("groups", "store"),
        P(("groups", "store"), "tensor", None, None),
        P("store", "tensor"),
        P("store", None),
        P("tensor", "store"),
        P("groups"),
        P("groups", None),
        P("groups"),
    )
    out_specs = P(("groups", "tensor"), "store")
    return jax.shard_map(body, mesh=mesh, in_specs=in_specs, out_specs=out_specs, check_vma=False)
```

```python
import math

import jax
import jax.numpy as jnp
import numpy as np
from jax import lax
from jax.sharding import PartitionSpec as P
from jax.experimental import pallas as pl
from jax.experimental.pallas import tpu as pltpu
import functools

HQ = 64
KVH = 8
HD = 128
TURN = 64
MAXPAGES = 256


THETA = 500000.0
NEG_FILL = -1e30
ROPE_FACTOR = 8.0
LOW_FACTOR = 1.0
HIGH_FACTOR = 4.0
INITIAL_CONTEXT = 8192.0


def joined(x, axis, combine):
    everything = jax.tree.map(lambda part: lax.all_gather(part, axis), x)
    first = jax.tree.map(lambda part: part[0], everything)

    def step(k, so_far):
        return combine(so_far, jax.tree.map(lambda part: part[k], everything))

    return lax.fori_loop(1, lax.axis_size(axis), step, first)


def inverse_freq(width):
    steps_half = jnp.arange(width // 2, dtype=jnp.float32)
    base_freq = jnp.exp(-(steps_half * (2.0 / width)) * jnp.log(jnp.float32(THETA)))
    wavelength = 2.0 * math.pi / base_freq
    low_wave = INITIAL_CONTEXT / LOW_FACTOR
    high_wave = INITIAL_CONTEXT / HIGH_FACTOR
    smooth = (INITIAL_CONTEXT / wavelength - LOW_FACTOR) / (HIGH_FACTOR - LOW_FACTOR)
    blended = (1.0 - smooth) * base_freq / ROPE_FACTOR + smooth * base_freq
    scaled = jnp.where(wavelength > low_wave, base_freq / ROPE_FACTOR, blended)
    return jnp.where(wavelength < high_wave, base_freq, scaled)


def rotate(values, rot_angle):
    half_width = values.shape[-1] // 2
    first_half = values[..., :half_width]
    second_half = values[..., half_width:]
    cosine = jnp.cos(rot_angle)
    sine_part = jnp.sin(rot_angle)
    return jnp.concatenate(
        [
            first_half * cosine - second_half * sine_part,
            second_half * cosine + first_half * sine_part,
        ],
        axis=-1,
    )


def to_half(values):
    return values.astype(jnp.bfloat16)


def table_lookup(table, index):
    hits = index[..., None] == jnp.arange(table.shape[0], dtype=jnp.int32)
    return jnp.sum(jnp.where(hits, table, 0), axis=-1)


def page_positions(page_store, shards, capacity):
    store_of = page_store[:, 0]
    onehot = (store_of[:, None] == jnp.arange(shards, dtype=jnp.int32)[None, :]).astype(jnp.int32)
    ranks = jnp.sum((jnp.cumsum(onehot, axis=0) - onehot) * onehot, axis=1)
    return store_of * capacity + ranks


def slot_meta(page_store, lengths, offsets, shards, capacity, first_slot, slot_count, page_len):
    positions = page_positions(page_store, shards, capacity)
    wanted = first_slot + jnp.arange(slot_count, dtype=jnp.int32)
    matches = (positions[:, None] == wanted[None, :]).astype(jnp.int32)
    page_ids = jnp.sum(matches * jnp.arange(positions.shape[0], dtype=jnp.int32)[:, None], axis=0)
    filled = jnp.sum(matches, axis=0) > 0
    slot_sess = page_ids // MAXPAGES
    slot_page = page_ids % MAXPAGES
    key_pos = slot_page[:, None] * page_len + jnp.arange(page_len, dtype=jnp.int32)[None, :]
    key_ok = filled[:, None] & (key_pos < table_lookup(lengths, slot_sess)[:, None])
    key_sess = jnp.broadcast_to(slot_sess[:, None], (slot_count, page_len))
    key_off = jnp.broadcast_to(table_lookup(offsets, slot_sess)[:, None], (slot_count, page_len))
    return (key_sess.reshape(-1), key_ok.reshape(-1), key_off.reshape(-1))


def attend(query, key_rows, value_rows, allowed):
    score_scale = 1.0 / query.shape[-1] ** 0.5
    scores = (
        jnp.einsum("tkgd,nkd->tkgn", query, key_rows, preferred_element_type=jnp.float32)
        * score_scale
    )
    wide_mask = allowed[:, None, None, :]
    scores = jnp.where(wide_mask, scores, NEG_FILL)
    row_top = jnp.max(scores, axis=-1)
    weights = jnp.where(wide_mask, jnp.exp(scores - row_top[..., None]), 0.0)
    weight_sum = jnp.sum(weights, axis=-1)
    head_mix = jnp.einsum(
        "tkgn,nkd->tkgd",
        weights.astype(jnp.bfloat16),
        value_rows,
        preferred_element_type=jnp.float32,
    )
    return (row_top, weight_sum, head_mix)


def combine(first_part, second_part):
    new_top = jnp.maximum(first_part[0], second_part[0])
    first_factor = jnp.exp(first_part[0] - new_top)
    second_factor = jnp.exp(second_part[0] - new_top)
    summed = first_part[1] * first_factor + second_part[1] * second_factor
    mixed_sum = first_part[2] * first_factor[..., None] + second_part[2] * second_factor[..., None]
    return (new_top, summed, mixed_sum)


MASK_FILL = -3e30


def hist_kernel(kv0_ref, q_ref, k_ref, v_ref, bias_ref, acc_out, m_out, l_out, m_sc, l_sc, acc_sc, *, scale, blocks):
    j = pl.program_id(1)

    @pl.when(j == 0)
    def _():
        m_sc[...] = jnp.full(m_sc.shape, NEG_FILL, jnp.float32)
        l_sc[...] = jnp.zeros(l_sc.shape, jnp.float32)
        acc_sc[...] = jnp.zeros(acc_sc.shape, jnp.float32)

    pages, page_len, hd = k_ref.shape
    n = pages * page_len
    keys = k_ref[...].reshape(n, hd)
    vals = v_ref[...].reshape(n, hd)
    scores = lax.dot_general(
        q_ref[0], keys, (((1,), (1,)), ((), ())), preferred_element_type=jnp.float32
    )
    scores = scores * scale + bias_ref[0]
    m_old = m_sc[...]
    m_new = jnp.maximum(m_old, jnp.max(scores, axis=1, keepdims=True))
    alpha = jnp.exp(m_old - m_new)
    weights = jnp.exp(scores - m_new)
    l_sc[...] = alpha * l_sc[...] + jnp.sum(weights, axis=1, keepdims=True)
    acc_sc[...] = alpha * acc_sc[...] + jnp.dot(
        weights.astype(jnp.bfloat16), vals, preferred_element_type=jnp.float32
    )
    m_sc[...] = m_new

    @pl.when(j == blocks - 1)
    def _():
        acc_out[0] = acc_sc[...]
        m_out[0] = m_sc[...]
        l_out[0] = l_sc[...]


def hist_attend(kv0, q_k, keys_rot, kv_local, bias, pb):
    heads, rows, hd = q_k.shape
    slots, page_len, width = kv_local.shape
    kv_heads = width // (2 * hd)
    blocks = slots // pb
    kernel = functools.partial(hist_kernel, scale=1.0 / hd ** 0.5, blocks=blocks)

    def head_of(h, kv0_ref):
        return (kv0_ref[0] + h) % kv_heads

    grid_spec = pltpu.PrefetchScalarGridSpec(
        num_scalar_prefetch=1,
        grid=(heads, blocks),
        in_specs=[
            pl.BlockSpec((1, rows, hd), lambda h, j, r: (h, 0, 0)),
            pl.BlockSpec((pb, page_len, hd), lambda h, j, r: (j, 0, head_of(h, r))),
            pl.BlockSpec((pb, page_len, hd), lambda h, j, r: (j, 0, 2 * head_of(h, r) + 1)),
            pl.BlockSpec((1, 1, pb * page_len), lambda h, j, r: (j, 0, 0)),
        ],
        out_specs=[
            pl.BlockSpec((1, rows, hd), lambda h, j, r: (h, 0, 0)),
            pl.BlockSpec((1, rows, 1), lambda h, j, r: (h, 0, 0)),
            pl.BlockSpec((1, rows, 1), lambda h, j, r: (h, 0, 0)),
        ],
        scratch_shapes=[
            pltpu.VMEM((rows, 1), jnp.float32),
            pltpu.VMEM((rows, 1), jnp.float32),
            pltpu.VMEM((rows, hd), jnp.float32),
        ],
    )
    return pl.pallas_call(
        kernel,
        grid_spec=grid_spec,
        out_shape=[
            jax.ShapeDtypeStruct((heads, rows, hd), jnp.float32),
            jax.ShapeDtypeStruct((heads, rows, 1), jnp.float32),
            jax.ShapeDtypeStruct((heads, rows, 1), jnp.float32),
        ],
        compiler_params=pltpu.CompilerParams(dimension_semantics=("arbitrary", "arbitrary")),
    )(jnp.reshape(kv0, (1,)).astype(jnp.int32), q_k, keys_rot, kv_local, bias)


def body(x_new, kv_pages, w_query, w_keyval, w_out, lengths, page_store, offsets):
    tensors = lax.axis_size("tensor")
    shards = lax.axis_size("store")
    tensor_idx = lax.axis_index("tensor")
    store_idx = lax.axis_index("store")
    tok_count = x_new.shape[0]
    assert tok_count == TURN and lengths.shape[0] == 1
    local_slots = kv_pages.shape[1]
    capacity = local_slots * tensors
    page_len = kv_pages.shape[2]
    kv_heads = kv_pages.shape[3] // (2 * HD)
    group_size = HQ // KVH
    local_heads = w_query.shape[1] // HD
    local_kv = max(1, local_heads // group_size)
    local_group = local_heads // local_kv
    freq_table = inverse_freq(HD)
    kv_first = tensor_idx * local_heads // group_size
    keyval_cols = lax.dynamic_slice_in_dim(w_keyval, kv_first * (2 * HD), local_kv * 2 * HD, 1)
    query_part = jnp.dot(x_new, w_query, preferred_element_type=jnp.float32)
    keyval_part = jnp.dot(x_new, keyval_cols, preferred_element_type=jnp.float32)
    query_sum, keyval_sum = lax.psum((query_part, keyval_part), "store")
    keyval_local = keyval_sum.reshape(tok_count, local_kv, 2, HD)
    tok_ids = jnp.arange(tok_count, dtype=jnp.int32)
    tok_sess = tok_ids // TURN
    tok_pos = table_lookup(lengths, tok_sess) + tok_ids % TURN
    tok_angle = tok_pos.astype(jnp.float32)[:, None, None] * freq_table
    query_rot = to_half(rotate(query_sum.reshape(tok_count, local_heads, HD), tok_angle))
    key_new = to_half(rotate(keyval_local[:, :, 0], tok_angle))
    value_new = to_half(keyval_local[:, :, 1])

    first_slot = store_idx * capacity + tensor_idx * local_slots
    key_sess, key_ok, key_off = slot_meta(
        page_store, lengths, offsets, shards, capacity, first_slot, local_slots, page_len
    )
    pb = 8 if local_slots % 8 == 0 else local_slots
    bias = jnp.where(key_ok, 0.0, MASK_FILL).astype(jnp.float32)
    bias = bias.reshape(local_slots // pb, 1, pb * page_len)
    hist_angle = offsets[0].astype(jnp.float32) * freq_table
    kv_local = kv_pages.reshape(local_slots, page_len, kv_pages.shape[3])
    keys_rot = to_half(
        rotate(
            kv_local.reshape(local_slots, page_len, kv_heads, 2, HD)[:, :, :, 0].astype(jnp.float32),
            hist_angle,
        )
    ).reshape(local_slots, page_len, kv_heads * HD)

    q_heads = jnp.transpose(query_rot, (1, 0, 2))
    q_all = lax.all_gather(q_heads, "tensor", axis=0, tiled=True)
    q_k = q_all.reshape(kv_heads, group_size * tok_count, HD)
    if local_heads % group_size == 0:
        own = hist_attend(
            kv_first, q_heads.reshape(local_kv, group_size * tok_count, HD), keys_rot, kv_local, bias, pb
        )
        rest_first = kv_first + local_kv
        q_rest = lax.dynamic_slice_in_dim(
            jnp.concatenate([q_k, q_k], axis=0), rest_first % kv_heads, kv_heads - local_kv, 0
        )
        rest = hist_attend(rest_first % kv_heads, q_rest, keys_rot, kv_local, bias, pb)
        parts = []
        for first, second in zip(own, rest):
            rolled = jnp.concatenate([first, second, first, second], axis=0)
            parts.append(lax.dynamic_slice_in_dim(rolled, kv_heads - kv_first, kv_heads, 0))
        acc, top, total = parts
    else:
        acc, top, total = hist_attend(jnp.int32(0), q_k, keys_rot, kv_local, bias, pb)
    acc = acc.reshape(HQ, tok_count, HD)
    top = top.reshape(HQ, tok_count)
    total = total.reshape(HQ, tok_count)

    glob_top = jnp.max(lax.all_gather(top, ("tensor", "store")), axis=0)
    factor = jnp.exp(top - glob_top)
    packed = jnp.concatenate(
        [(acc * factor[..., None]).reshape(HQ, tok_count * HD), total * factor], axis=1
    )
    packed = lax.psum_scatter(packed, "tensor", scatter_dimension=0, tiled=True)
    packed = lax.psum(packed, "store")
    acc = packed[:, : tok_count * HD].reshape(local_heads, tok_count, HD)
    total = packed[:, tok_count * HD :]
    loc_top = lax.dynamic_slice_in_dim(glob_top, tensor_idx * local_heads, local_heads, 0)
    hist_part = (
        jnp.transpose(loc_top),
        jnp.transpose(total),
        jnp.transpose(acc, (1, 0, 2)),
    )

    query_local = query_rot.reshape(tok_count, local_kv, local_group, HD)
    new_allowed = (tok_sess[:, None] == tok_sess[None, :]) & (tok_ids[None, :] <= tok_ids[:, None])
    new_part = attend(query_local, key_new, value_new, new_allowed)
    new_flat = (
        new_part[0].reshape(tok_count, local_heads),
        new_part[1].reshape(tok_count, local_heads),
        new_part[2].reshape(tok_count, local_heads, HD),
    )
    combined = combine(hist_part, new_flat)
    attended = (
        (combined[2] / combined[1][..., None])
        .reshape(tok_count, local_heads * HD)
        .astype(jnp.bfloat16)
    )
    result = lax.psum_scatter(
        jnp.dot(attended, w_out, preferred_element_type=jnp.float32),
        "tensor",
        scatter_dimension=0,
        tiled=True,
    )
    return result.astype(jnp.bfloat16)


def solution(mesh):
    in_specs = (
        P("groups", "store"),
        P(("groups", "store"), "tensor", None, None),
        P("store", "tensor"),
        P("store", None),
        P("tensor", "store"),
        P("groups"),
        P("groups", None),
        P("groups"),
    )
    out_specs = P(("groups", "tensor"), "store")
    return jax.shard_map(body, mesh=mesh, in_specs=in_specs, out_specs=out_specs, check_vma=False)
```

```python
import math

import jax
import jax.numpy as jnp
import numpy as np
from jax import lax
from jax.sharding import PartitionSpec as P
from jax.experimental import pallas as pl
from jax.experimental.pallas import tpu as pltpu
import functools

HQ = 64
KVH = 8
HD = 128
TURN = 64
MAXPAGES = 256


THETA = 500000.0
NEG_FILL = -1e30
ROPE_FACTOR = 8.0
LOW_FACTOR = 1.0
HIGH_FACTOR = 4.0
INITIAL_CONTEXT = 8192.0


def joined(x, axis, combine):
    everything = jax.tree.map(lambda part: lax.all_gather(part, axis), x)
    first = jax.tree.map(lambda part: part[0], everything)

    def step(k, so_far):
        return combine(so_far, jax.tree.map(lambda part: part[k], everything))

    return lax.fori_loop(1, lax.axis_size(axis), step, first)


def inverse_freq(width):
    steps_half = jnp.arange(width // 2, dtype=jnp.float32)
    base_freq = jnp.exp(-(steps_half * (2.0 / width)) * jnp.log(jnp.float32(THETA)))
    wavelength = 2.0 * math.pi / base_freq
    low_wave = INITIAL_CONTEXT / LOW_FACTOR
    high_wave = INITIAL_CONTEXT / HIGH_FACTOR
    smooth = (INITIAL_CONTEXT / wavelength - LOW_FACTOR) / (HIGH_FACTOR - LOW_FACTOR)
    blended = (1.0 - smooth) * base_freq / ROPE_FACTOR + smooth * base_freq
    scaled = jnp.where(wavelength > low_wave, base_freq / ROPE_FACTOR, blended)
    return jnp.where(wavelength < high_wave, base_freq, scaled)


def rotate(values, rot_angle):
    half_width = values.shape[-1] // 2
    first_half = values[..., :half_width]
    second_half = values[..., half_width:]
    cosine = jnp.cos(rot_angle)
    sine_part = jnp.sin(rot_angle)
    return jnp.concatenate(
        [
            first_half * cosine - second_half * sine_part,
            second_half * cosine + first_half * sine_part,
        ],
        axis=-1,
    )


def to_half(values):
    return values.astype(jnp.bfloat16)


def table_lookup(table, index):
    hits = index[..., None] == jnp.arange(table.shape[0], dtype=jnp.int32)
    return jnp.sum(jnp.where(hits, table, 0), axis=-1)


def page_positions(page_store, shards, capacity):
    store_of = page_store[:, 0]
    onehot = (store_of[:, None] == jnp.arange(shards, dtype=jnp.int32)[None, :]).astype(jnp.int32)
    ranks = jnp.sum((jnp.cumsum(onehot, axis=0) - onehot) * onehot, axis=1)
    return store_of * capacity + ranks


def slot_meta(page_store, lengths, offsets, shards, capacity, first_slot, slot_count, page_len):
    positions = page_positions(page_store, shards, capacity)
    wanted = first_slot + jnp.arange(slot_count, dtype=jnp.int32)
    matches = (positions[:, None] == wanted[None, :]).astype(jnp.int32)
    page_ids = jnp.sum(matches * jnp.arange(positions.shape[0], dtype=jnp.int32)[:, None], axis=0)
    filled = jnp.sum(matches, axis=0) > 0
    slot_sess = page_ids // MAXPAGES
    slot_page = page_ids % MAXPAGES
    key_pos = slot_page[:, None] * page_len + jnp.arange(page_len, dtype=jnp.int32)[None, :]
    key_ok = filled[:, None] & (key_pos < table_lookup(lengths, slot_sess)[:, None])
    key_sess = jnp.broadcast_to(slot_sess[:, None], (slot_count, page_len))
    key_off = jnp.broadcast_to(table_lookup(offsets, slot_sess)[:, None], (slot_count, page_len))
    return (key_sess.reshape(-1), key_ok.reshape(-1), key_off.reshape(-1))


def attend(query, key_rows, value_rows, allowed):
    score_scale = 1.0 / query.shape[-1] ** 0.5
    scores = (
        jnp.einsum("tkgd,nkd->tkgn", query, key_rows, preferred_element_type=jnp.float32)
        * score_scale
    )
    wide_mask = allowed[:, None, None, :]
    scores = jnp.where(wide_mask, scores, NEG_FILL)
    row_top = jnp.max(scores, axis=-1)
    weights = jnp.where(wide_mask, jnp.exp(scores - row_top[..., None]), 0.0)
    weight_sum = jnp.sum(weights, axis=-1)
    head_mix = jnp.einsum(
        "tkgn,nkd->tkgd",
        weights.astype(jnp.bfloat16),
        value_rows,
        preferred_element_type=jnp.float32,
    )
    return (row_top, weight_sum, head_mix)


def combine(first_part, second_part):
    new_top = jnp.maximum(first_part[0], second_part[0])
    first_factor = jnp.exp(first_part[0] - new_top)
    second_factor = jnp.exp(second_part[0] - new_top)
    summed = first_part[1] * first_factor + second_part[1] * second_factor
    mixed_sum = first_part[2] * first_factor[..., None] + second_part[2] * second_factor[..., None]
    return (new_top, summed, mixed_sum)


MASK_FILL = -3e30


def hist_kernel(kv0_ref, q_ref, k_ref, v_ref, bias_ref, cos_ref, sin_ref, acc_out, m_out, l_out, m_sc, l_sc, acc_sc, *, scale, blocks):
    j = pl.program_id(1)

    @pl.when(j == 0)
    def _():
        m_sc[...] = jnp.full(m_sc.shape, NEG_FILL, jnp.float32)
        l_sc[...] = jnp.zeros(l_sc.shape, jnp.float32)
        acc_sc[...] = jnp.zeros(acc_sc.shape, jnp.float32)

    pages, page_len, hd = k_ref.shape
    n = pages * page_len
    keys = k_ref[...].reshape(n, hd).astype(jnp.float32)
    vals = v_ref[...].reshape(n, hd)
    keys = (keys * cos_ref[...] + pltpu.roll(keys, hd // 2, 1) * sin_ref[...]).astype(jnp.bfloat16)
    scores = lax.dot_general(
        q_ref[0], keys, (((1,), (1,)), ((), ())), preferred_element_type=jnp.float32
    )
    scores = scores * scale + bias_ref[0]
    m_old = m_sc[...]
    m_new = jnp.maximum(m_old, jnp.max(scores, axis=1, keepdims=True))
    alpha = jnp.exp(m_old - m_new)
    weights = jnp.exp(scores - m_new)
    l_sc[...] = alpha * l_sc[...] + jnp.sum(weights, axis=1, keepdims=True)
    acc_sc[...] = alpha * acc_sc[...] + jnp.dot(
        weights.astype(jnp.bfloat16), vals, preferred_element_type=jnp.float32
    )
    m_sc[...] = m_new

    @pl.when(j == blocks - 1)
    def _():
        acc_out[0] = acc_sc[...]
        m_out[0] = m_sc[...]
        l_out[0] = l_sc[...]


def hist_attend(kv0, q_k, kv_local, bias, cos2, sin2, pb):
    heads, rows, hd = q_k.shape
    slots, page_len, width = kv_local.shape
    kv_heads = width // (2 * hd)
    blocks = slots // pb
    kernel = functools.partial(hist_kernel, scale=1.0 / hd ** 0.5, blocks=blocks)

    def head_of(h, kv0_ref):
        return (kv0_ref[0] + h) % kv_heads

    grid_spec = pltpu.PrefetchScalarGridSpec(
        num_scalar_prefetch=1,
        grid=(heads, blocks),
        in_specs=[
            pl.BlockSpec((1, rows, hd), lambda h, j, r: (h, 0, 0)),
            pl.BlockSpec((pb, page_len, hd), lambda h, j, r: (j, 0, 2 * head_of(h, r))),
            pl.BlockSpec((pb, page_len, hd), lambda h, j, r: (j, 0, 2 * head_of(h, r) + 1)),
            pl.BlockSpec((1, 1, pb * page_len), lambda h, j, r: (j, 0, 0)),
            pl.BlockSpec((1, hd), lambda h, j, r: (0, 0)),
            pl.BlockSpec((1, hd), lambda h, j, r: (0, 0)),
        ],
        out_specs=[
            pl.BlockSpec((1, rows, hd), lambda h, j, r: (h, 0, 0)),
            pl.BlockSpec((1, rows, 1), lambda h, j, r: (h, 0, 0)),
            pl.BlockSpec((1, rows, 1), lambda h, j, r: (h, 0, 0)),
        ],
        scratch_shapes=[
            pltpu.VMEM((rows, 1), jnp.float32),
            pltpu.VMEM((rows, 1), jnp.float32),
            pltpu.VMEM((rows, hd), jnp.float32),
        ],
    )
    return pl.pallas_call(
        kernel,
        grid_spec=grid_spec,
        out_shape=[
            jax.ShapeDtypeStruct((heads, rows, hd), jnp.float32),
            jax.ShapeDtypeStruct((heads, rows, 1), jnp.float32),
            jax.ShapeDtypeStruct((heads, rows, 1), jnp.float32),
        ],
        compiler_params=pltpu.CompilerParams(dimension_semantics=("arbitrary", "arbitrary")),
    )(jnp.reshape(kv0, (1,)).astype(jnp.int32), q_k, kv_local, kv_local, bias, cos2, sin2)


def body(x_new, kv_pages, w_query, w_keyval, w_out, lengths, page_store, offsets):
    tensors = lax.axis_size("tensor")
    shards = lax.axis_size("store")
    tensor_idx = lax.axis_index("tensor")
    store_idx = lax.axis_index("store")
    tok_count = x_new.shape[0]
    assert tok_count == TURN and lengths.shape[0] == 1
    local_slots = kv_pages.shape[1]
    capacity = local_slots * tensors
    page_len = kv_pages.shape[2]
    kv_heads = kv_pages.shape[3] // (2 * HD)
    group_size = HQ // KVH
    local_heads = w_query.shape[1] // HD
    local_kv = max(1, local_heads // group_size)
    local_group = local_heads // local_kv
    freq_table = inverse_freq(HD)
    kv_first = tensor_idx * local_heads // group_size
    keyval_cols = lax.dynamic_slice_in_dim(w_keyval, kv_first * (2 * HD), local_kv * 2 * HD, 1)
    query_part = jnp.dot(x_new, w_query, preferred_element_type=jnp.float32)
    keyval_part = jnp.dot(x_new, keyval_cols, preferred_element_type=jnp.float32)
    query_sum, keyval_sum = lax.psum((query_part, keyval_part), "store")
    keyval_local = keyval_sum.reshape(tok_count, local_kv, 2, HD)
    tok_ids = jnp.arange(tok_count, dtype=jnp.int32)
    tok_sess = tok_ids // TURN
    tok_pos = table_lookup(lengths, tok_sess) + tok_ids % TURN
    tok_angle = tok_pos.astype(jnp.float32)[:, None, None] * freq_table
    query_rot = to_half(rotate(query_sum.reshape(tok_count, local_heads, HD), tok_angle))
    key_new = to_half(rotate(keyval_local[:, :, 0], tok_angle))
    value_new = to_half(keyval_local[:, :, 1])

    first_slot = store_idx * capacity + tensor_idx * local_slots
    key_sess, key_ok, key_off = slot_meta(
        page_store, lengths, offsets, shards, capacity, first_slot, local_slots, page_len
    )
    pb = max(d for d in range(1, min(local_slots, 20) + 1) if local_slots % d == 0)
    bias = jnp.where(key_ok, 0.0, MASK_FILL).astype(jnp.float32)
    bias = bias.reshape(local_slots // pb, 1, pb * page_len)
    hist_angle = offsets[0].astype(jnp.float32) * freq_table
    kv_local = kv_pages.reshape(local_slots, page_len, kv_pages.shape[3])
    cosine = jnp.cos(hist_angle)
    sine = jnp.sin(hist_angle)
    cos2 = jnp.concatenate([cosine, cosine])[None, :]
    sin2 = jnp.concatenate([-sine, sine])[None, :]

    q_heads = jnp.transpose(query_rot, (1, 0, 2))
    q_all = lax.all_gather(q_heads, "tensor", axis=0, tiled=True)
    q_k = q_all.reshape(kv_heads, group_size * tok_count, HD)
    if local_heads % group_size == 0:
        own = hist_attend(
            kv_first, q_heads.reshape(local_kv, group_size * tok_count, HD), kv_local, bias, cos2, sin2, pb
        )
        rest_first = kv_first + local_kv
        q_rest = lax.dynamic_slice_in_dim(
            jnp.concatenate([q_k, q_k], axis=0), rest_first % kv_heads, kv_heads - local_kv, 0
        )
        rest = hist_attend(rest_first % kv_heads, q_rest, kv_local, bias, cos2, sin2, pb)
        parts = []
        for first, second in zip(own, rest):
            rolled = jnp.concatenate([first, second, first, second], axis=0)
            parts.append(lax.dynamic_slice_in_dim(rolled, kv_heads - kv_first, kv_heads, 0))
        acc, top, total = parts
    else:
        acc, top, total = hist_attend(jnp.int32(0), q_k, kv_local, bias, cos2, sin2, pb)
    acc = acc.reshape(HQ, tok_count, HD)
    top = top.reshape(HQ, tok_count)
    total = total.reshape(HQ, tok_count)

    glob_top = jnp.max(lax.all_gather(top, ("tensor", "store")), axis=0)
    factor = jnp.exp(top - glob_top)
    packed = jnp.concatenate(
        [(acc * factor[..., None]).reshape(HQ, tok_count * HD), total * factor], axis=1
    )
    packed = lax.psum_scatter(packed, "tensor", scatter_dimension=0, tiled=True)
    packed = lax.psum(packed, "store")
    acc = packed[:, : tok_count * HD].reshape(local_heads, tok_count, HD)
    total = packed[:, tok_count * HD :]
    loc_top = lax.dynamic_slice_in_dim(glob_top, tensor_idx * local_heads, local_heads, 0)
    hist_part = (
        jnp.transpose(loc_top),
        jnp.transpose(total),
        jnp.transpose(acc, (1, 0, 2)),
    )

    query_local = query_rot.reshape(tok_count, local_kv, local_group, HD)
    new_allowed = (tok_sess[:, None] == tok_sess[None, :]) & (tok_ids[None, :] <= tok_ids[:, None])
    new_part = attend(query_local, key_new, value_new, new_allowed)
    new_flat = (
        new_part[0].reshape(tok_count, local_heads),
        new_part[1].reshape(tok_count, local_heads),
        new_part[2].reshape(tok_count, local_heads, HD),
    )
    combined = combine(hist_part, new_flat)
    attended = (
        (combined[2] / combined[1][..., None])
        .reshape(tok_count, local_heads * HD)
        .astype(jnp.bfloat16)
    )
    result = lax.psum_scatter(
        jnp.dot(attended, w_out, preferred_element_type=jnp.float32),
        "tensor",
        scatter_dimension=0,
        tiled=True,
    )
    return result.astype(jnp.bfloat16)


def solution(mesh):
    in_specs = (
        P("groups", "store"),
        P(("groups", "store"), "tensor", None, None),
        P("store", "tensor"),
        P("store", None),
        P("tensor", "store"),
        P("groups"),
        P("groups", None),
        P("groups"),
    )
    out_specs = P(("groups", "tensor"), "store")
    return jax.shard_map(body, mesh=mesh, in_specs=in_specs, out_specs=out_specs, check_vma=False)
```

```python
import math

import jax
import jax.numpy as jnp
import numpy as np
from jax import lax
from jax.sharding import PartitionSpec as P
from jax.experimental import pallas as pl
from jax.experimental.pallas import tpu as pltpu
import functools

HQ = 64
KVH = 8
HD = 128
TURN = 64
MAXPAGES = 256


THETA = 500000.0
NEG_FILL = -1e30
ROPE_FACTOR = 8.0
LOW_FACTOR = 1.0
HIGH_FACTOR = 4.0
INITIAL_CONTEXT = 8192.0


def joined(x, axis, combine):
    everything = jax.tree.map(lambda part: lax.all_gather(part, axis), x)
    first = jax.tree.map(lambda part: part[0], everything)

    def step(k, so_far):
        return combine(so_far, jax.tree.map(lambda part: part[k], everything))

    return lax.fori_loop(1, lax.axis_size(axis), step, first)


def inverse_freq(width):
    steps_half = jnp.arange(width // 2, dtype=jnp.float32)
    base_freq = jnp.exp(-(steps_half * (2.0 / width)) * jnp.log(jnp.float32(THETA)))
    wavelength = 2.0 * math.pi / base_freq
    low_wave = INITIAL_CONTEXT / LOW_FACTOR
    high_wave = INITIAL_CONTEXT / HIGH_FACTOR
    smooth = (INITIAL_CONTEXT / wavelength - LOW_FACTOR) / (HIGH_FACTOR - LOW_FACTOR)
    blended = (1.0 - smooth) * base_freq / ROPE_FACTOR + smooth * base_freq
    scaled = jnp.where(wavelength > low_wave, base_freq / ROPE_FACTOR, blended)
    return jnp.where(wavelength < high_wave, base_freq, scaled)


def rotate(values, rot_angle):
    half_width = values.shape[-1] // 2
    first_half = values[..., :half_width]
    second_half = values[..., half_width:]
    cosine = jnp.cos(rot_angle)
    sine_part = jnp.sin(rot_angle)
    return jnp.concatenate(
        [
            first_half * cosine - second_half * sine_part,
            second_half * cosine + first_half * sine_part,
        ],
        axis=-1,
    )


def to_half(values):
    return values.astype(jnp.bfloat16)


def table_lookup(table, index):
    hits = index[..., None] == jnp.arange(table.shape[0], dtype=jnp.int32)
    return jnp.sum(jnp.where(hits, table, 0), axis=-1)


def page_positions(page_store, shards, capacity):
    store_of = page_store[:, 0]
    onehot = (store_of[:, None] == jnp.arange(shards, dtype=jnp.int32)[None, :]).astype(jnp.int32)
    ranks = jnp.sum((jnp.cumsum(onehot, axis=0) - onehot) * onehot, axis=1)
    return store_of * capacity + ranks


def slot_meta(page_store, lengths, offsets, shards, capacity, first_slot, slot_count, page_len):
    positions = page_positions(page_store, shards, capacity)
    wanted = first_slot + jnp.arange(slot_count, dtype=jnp.int32)
    matches = (positions[:, None] == wanted[None, :]).astype(jnp.int32)
    page_ids = jnp.sum(matches * jnp.arange(positions.shape[0], dtype=jnp.int32)[:, None], axis=0)
    filled = jnp.sum(matches, axis=0) > 0
    slot_sess = page_ids // MAXPAGES
    slot_page = page_ids % MAXPAGES
    key_pos = slot_page[:, None] * page_len + jnp.arange(page_len, dtype=jnp.int32)[None, :]
    key_ok = filled[:, None] & (key_pos < table_lookup(lengths, slot_sess)[:, None])
    key_sess = jnp.broadcast_to(slot_sess[:, None], (slot_count, page_len))
    key_off = jnp.broadcast_to(table_lookup(offsets, slot_sess)[:, None], (slot_count, page_len))
    return (key_sess.reshape(-1), key_ok.reshape(-1), key_off.reshape(-1))


def attend(query, key_rows, value_rows, allowed):
    score_scale = 1.0 / query.shape[-1] ** 0.5
    scores = (
        jnp.einsum("tkgd,nkd->tkgn", query, key_rows, preferred_element_type=jnp.float32)
        * score_scale
    )
    wide_mask = allowed[:, None, None, :]
    scores = jnp.where(wide_mask, scores, NEG_FILL)
    row_top = jnp.max(scores, axis=-1)
    weights = jnp.where(wide_mask, jnp.exp(scores - row_top[..., None]), 0.0)
    weight_sum = jnp.sum(weights, axis=-1)
    head_mix = jnp.einsum(
        "tkgn,nkd->tkgd",
        weights.astype(jnp.bfloat16),
        value_rows,
        preferred_element_type=jnp.float32,
    )
    return (row_top, weight_sum, head_mix)


def combine(first_part, second_part):
    new_top = jnp.maximum(first_part[0], second_part[0])
    first_factor = jnp.exp(first_part[0] - new_top)
    second_factor = jnp.exp(second_part[0] - new_top)
    summed = first_part[1] * first_factor + second_part[1] * second_factor
    mixed_sum = first_part[2] * first_factor[..., None] + second_part[2] * second_factor[..., None]
    return (new_top, summed, mixed_sum)


MASK_FILL = -3e30


def hist_kernel(kv0_ref, q_ref, k_ref, v_ref, bias_ref, cos_ref, sin_ref, acc_out, m_out, l_out, m_sc, l_sc, acc_sc, *, scale, blocks):
    j = pl.program_id(1)

    @pl.when(j == 0)
    def _():
        m_sc[...] = jnp.full(m_sc.shape, NEG_FILL, jnp.float32)
        l_sc[...] = jnp.zeros(l_sc.shape, jnp.float32)
        acc_sc[...] = jnp.zeros(acc_sc.shape, jnp.float32)

    pages, page_len, hd = k_ref.shape
    n = pages * page_len
    keys = k_ref[...].reshape(n, hd).astype(jnp.float32)
    vals = v_ref[...].reshape(n, hd)
    keys = (keys * cos_ref[...] + pltpu.roll(keys, hd // 2, 1) * sin_ref[...]).astype(jnp.bfloat16)
    scores = lax.dot_general(
        q_ref[0], keys, (((1,), (1,)), ((), ())), preferred_element_type=jnp.float32
    )
    scores = scores * scale + bias_ref[0]
    m_old = m_sc[...]
    m_new = jnp.maximum(m_old, jnp.max(scores, axis=1, keepdims=True))
    alpha = jnp.exp(m_old - m_new)
    weights = jnp.exp(scores - m_new)
    l_sc[...] = alpha * l_sc[...] + jnp.sum(weights, axis=1, keepdims=True)
    acc_sc[...] = alpha * acc_sc[...] + jnp.dot(
        weights.astype(jnp.bfloat16), vals, preferred_element_type=jnp.float32
    )
    m_sc[...] = m_new

    @pl.when(j == blocks - 1)
    def _():
        acc_out[0] = acc_sc[...]
        m_out[0] = m_sc[...]
        l_out[0] = l_sc[...]


def hist_attend(kv0, q_k, kv_local, bias, cos2, sin2, pb):
    heads, rows, hd = q_k.shape
    slots, page_len, width = kv_local.shape
    kv_heads = width // (2 * hd)
    blocks = slots // pb
    kernel = functools.partial(hist_kernel, scale=1.0 / hd ** 0.5, blocks=blocks)

    def head_of(h, kv0_ref):
        return (kv0_ref[0] + h) % kv_heads

    grid_spec = pltpu.PrefetchScalarGridSpec(
        num_scalar_prefetch=1,
        grid=(heads, blocks),
        in_specs=[
            pl.BlockSpec((1, rows, hd), lambda h, j, r: (h, 0, 0)),
            pl.BlockSpec((pb, page_len, hd), lambda h, j, r: (j, 0, 2 * head_of(h, r))),
            pl.BlockSpec((pb, page_len, hd), lambda h, j, r: (j, 0, 2 * head_of(h, r) + 1)),
            pl.BlockSpec((1, 1, pb * page_len), lambda h, j, r: (j, 0, 0)),
            pl.BlockSpec((1, hd), lambda h, j, r: (0, 0)),
            pl.BlockSpec((1, hd), lambda h, j, r: (0, 0)),
        ],
        out_specs=[
            pl.BlockSpec((1, rows, hd), lambda h, j, r: (h, 0, 0)),
            pl.BlockSpec((1, rows, 1), lambda h, j, r: (h, 0, 0)),
            pl.BlockSpec((1, rows, 1), lambda h, j, r: (h, 0, 0)),
        ],
        scratch_shapes=[
            pltpu.VMEM((rows, 1), jnp.float32),
            pltpu.VMEM((rows, 1), jnp.float32),
            pltpu.VMEM((rows, hd), jnp.float32),
        ],
    )
    return pl.pallas_call(
        kernel,
        grid_spec=grid_spec,
        out_shape=[
            jax.ShapeDtypeStruct((heads, rows, hd), jnp.float32),
            jax.ShapeDtypeStruct((heads, rows, 1), jnp.float32),
            jax.ShapeDtypeStruct((heads, rows, 1), jnp.float32),
        ],
        compiler_params=pltpu.CompilerParams(dimension_semantics=("arbitrary", "arbitrary")),
    )(jnp.reshape(kv0, (1,)).astype(jnp.int32), q_k, kv_local, kv_local, bias, cos2, sin2)


def body(x_new, kv_pages, w_query, w_keyval, w_out, lengths, page_store, offsets):
    tensors = lax.axis_size("tensor")
    shards = lax.axis_size("store")
    tensor_idx = lax.axis_index("tensor")
    store_idx = lax.axis_index("store")
    tok_count = x_new.shape[0]
    assert tok_count == TURN and lengths.shape[0] == 1
    local_slots = kv_pages.shape[1]
    capacity = local_slots * tensors
    page_len = kv_pages.shape[2]
    kv_heads = kv_pages.shape[3] // (2 * HD)
    group_size = HQ // KVH
    local_heads = w_query.shape[1] // HD
    local_kv = max(1, local_heads // group_size)
    local_group = local_heads // local_kv
    freq_table = inverse_freq(HD)
    kv_first = tensor_idx * local_heads // group_size
    keyval_cols = lax.dynamic_slice_in_dim(w_keyval, kv_first * (2 * HD), local_kv * 2 * HD, 1)
    query_part = jnp.dot(x_new, w_query, preferred_element_type=jnp.float32)
    keyval_part = jnp.dot(x_new, keyval_cols, preferred_element_type=jnp.float32)
    query_sum, keyval_sum = lax.psum((query_part, keyval_part), "store")
    keyval_local = keyval_sum.reshape(tok_count, local_kv, 2, HD)
    tok_ids = jnp.arange(tok_count, dtype=jnp.int32)
    tok_sess = tok_ids // TURN
    tok_pos = table_lookup(lengths, tok_sess) + tok_ids % TURN
    tok_angle = tok_pos.astype(jnp.float32)[:, None, None] * freq_table
    query_rot = to_half(rotate(query_sum.reshape(tok_count, local_heads, HD), tok_angle))
    key_new = to_half(rotate(keyval_local[:, :, 0], tok_angle))
    value_new = to_half(keyval_local[:, :, 1])

    first_slot = store_idx * capacity + tensor_idx * local_slots
    key_sess, key_ok, key_off = slot_meta(
        page_store, lengths, offsets, shards, capacity, first_slot, local_slots, page_len
    )
    pb = local_slots
    bias = jnp.where(key_ok, 0.0, MASK_FILL).astype(jnp.float32)
    bias = bias.reshape(local_slots // pb, 1, pb * page_len)
    hist_angle = offsets[0].astype(jnp.float32) * freq_table
    kv_local = kv_pages.reshape(local_slots, page_len, kv_pages.shape[3])
    cosine = jnp.cos(hist_angle)
    sine = jnp.sin(hist_angle)
    cos2 = jnp.concatenate([cosine, cosine])[None, :]
    sin2 = jnp.concatenate([-sine, sine])[None, :]

    q_heads = jnp.transpose(query_rot, (1, 0, 2))
    q_all = lax.all_gather(q_heads, "tensor", axis=0, tiled=True)
    q_k = q_all.reshape(kv_heads, group_size * tok_count, HD)
    if local_heads % group_size == 0:
        own = hist_attend(
            kv_first, q_heads.reshape(local_kv, group_size * tok_count, HD), kv_local, bias, cos2, sin2, pb
        )
        rest_first = kv_first + local_kv
        q_rest = lax.dynamic_slice_in_dim(
            jnp.concatenate([q_k, q_k], axis=0), rest_first % kv_heads, kv_heads - local_kv, 0
        )
        rest = hist_attend(rest_first % kv_heads, q_rest, kv_local, bias, cos2, sin2, pb)
        parts = []
        for first, second in zip(own, rest):
            rolled = jnp.concatenate([first, second, first, second], axis=0)
            parts.append(lax.dynamic_slice_in_dim(rolled, kv_heads - kv_first, kv_heads, 0))
        acc, top, total = parts
    else:
        acc, top, total = hist_attend(jnp.int32(0), q_k, kv_local, bias, cos2, sin2, pb)
    acc = acc.reshape(HQ, tok_count, HD)
    top = top.reshape(HQ, tok_count)
    total = total.reshape(HQ, tok_count)

    glob_top = jnp.max(lax.all_gather(top, ("tensor", "store")), axis=0)
    factor = jnp.exp(top - glob_top)
    packed = jnp.concatenate(
        [(acc * factor[..., None]).reshape(HQ, tok_count * HD), total * factor], axis=1
    )
    packed = lax.psum_scatter(packed, "tensor", scatter_dimension=0, tiled=True)
    packed = lax.psum(packed, "store")
    acc = packed[:, : tok_count * HD].reshape(local_heads, tok_count, HD)
    total = packed[:, tok_count * HD :]
    loc_top = lax.dynamic_slice_in_dim(glob_top, tensor_idx * local_heads, local_heads, 0)
    hist_part = (
        jnp.transpose(loc_top),
        jnp.transpose(total),
        jnp.transpose(acc, (1, 0, 2)),
    )

    query_local = query_rot.reshape(tok_count, local_kv, local_group, HD)
    new_allowed = (tok_sess[:, None] == tok_sess[None, :]) & (tok_ids[None, :] <= tok_ids[:, None])
    new_part = attend(query_local, key_new, value_new, new_allowed)
    new_flat = (
        new_part[0].reshape(tok_count, local_heads),
        new_part[1].reshape(tok_count, local_heads),
        new_part[2].reshape(tok_count, local_heads, HD),
    )
    combined = combine(hist_part, new_flat)
    attended = (
        (combined[2] / combined[1][..., None])
        .reshape(tok_count, local_heads * HD)
        .astype(jnp.bfloat16)
    )
    result = lax.psum_scatter(
        jnp.dot(attended, w_out, preferred_element_type=jnp.float32),
        "tensor",
        scatter_dimension=0,
        tiled=True,
    )
    return result.astype(jnp.bfloat16)


def solution(mesh):
    in_specs = (
        P("groups", "store"),
        P(("groups", "store"), "tensor", None, None),
        P("store", "tensor"),
        P("store", None),
        P("tensor", "store"),
        P("groups"),
        P("groups", None),
        P("groups"),
    )
    out_specs = P(("groups", "tensor"), "store")
    return jax.shard_map(body, mesh=mesh, in_specs=in_specs, out_specs=out_specs, check_vma=False)
```

```python
import math

import jax
import jax.numpy as jnp
import numpy as np
from jax import lax
from jax.sharding import PartitionSpec as P
from jax.experimental import pallas as pl
from jax.experimental.pallas import tpu as pltpu
import functools

HQ = 64
KVH = 8
HD = 128
TURN = 64
MAXPAGES = 256


THETA = 500000.0
NEG_FILL = -1e30
ROPE_FACTOR = 8.0
LOW_FACTOR = 1.0
HIGH_FACTOR = 4.0
INITIAL_CONTEXT = 8192.0


def joined(x, axis, combine):
    everything = jax.tree.map(lambda part: lax.all_gather(part, axis), x)
    first = jax.tree.map(lambda part: part[0], everything)

    def step(k, so_far):
        return combine(so_far, jax.tree.map(lambda part: part[k], everything))

    return lax.fori_loop(1, lax.axis_size(axis), step, first)


def inverse_freq(width):
    steps_half = jnp.arange(width // 2, dtype=jnp.float32)
    base_freq = jnp.exp(-(steps_half * (2.0 / width)) * jnp.log(jnp.float32(THETA)))
    wavelength = 2.0 * math.pi / base_freq
    low_wave = INITIAL_CONTEXT / LOW_FACTOR
    high_wave = INITIAL_CONTEXT / HIGH_FACTOR
    smooth = (INITIAL_CONTEXT / wavelength - LOW_FACTOR) / (HIGH_FACTOR - LOW_FACTOR)
    blended = (1.0 - smooth) * base_freq / ROPE_FACTOR + smooth * base_freq
    scaled = jnp.where(wavelength > low_wave, base_freq / ROPE_FACTOR, blended)
    return jnp.where(wavelength < high_wave, base_freq, scaled)


def rotate(values, rot_angle):
    half_width = values.shape[-1] // 2
    first_half = values[..., :half_width]
    second_half = values[..., half_width:]
    cosine = jnp.cos(rot_angle)
    sine_part = jnp.sin(rot_angle)
    return jnp.concatenate(
        [
            first_half * cosine - second_half * sine_part,
            second_half * cosine + first_half * sine_part,
        ],
        axis=-1,
    )


def to_half(values):
    return values.astype(jnp.bfloat16)


def table_lookup(table, index):
    hits = index[..., None] == jnp.arange(table.shape[0], dtype=jnp.int32)
    return jnp.sum(jnp.where(hits, table, 0), axis=-1)


def page_positions(page_store, shards, capacity):
    store_of = page_store[:, 0]
    onehot = (store_of[:, None] == jnp.arange(shards, dtype=jnp.int32)[None, :]).astype(jnp.int32)
    ranks = jnp.sum((jnp.cumsum(onehot, axis=0) - onehot) * onehot, axis=1)
    return store_of * capacity + ranks


def slot_meta(page_store, lengths, offsets, shards, capacity, first_slot, slot_count, page_len):
    positions = page_positions(page_store, shards, capacity)
    wanted = first_slot + jnp.arange(slot_count, dtype=jnp.int32)
    matches = (positions[:, None] == wanted[None, :]).astype(jnp.int32)
    page_ids = jnp.sum(matches * jnp.arange(positions.shape[0], dtype=jnp.int32)[:, None], axis=0)
    filled = jnp.sum(matches, axis=0) > 0
    slot_sess = page_ids // MAXPAGES
    slot_page = page_ids % MAXPAGES
    key_pos = slot_page[:, None] * page_len + jnp.arange(page_len, dtype=jnp.int32)[None, :]
    key_ok = filled[:, None] & (key_pos < table_lookup(lengths, slot_sess)[:, None])
    key_sess = jnp.broadcast_to(slot_sess[:, None], (slot_count, page_len))
    key_off = jnp.broadcast_to(table_lookup(offsets, slot_sess)[:, None], (slot_count, page_len))
    return (key_sess.reshape(-1), key_ok.reshape(-1), key_off.reshape(-1))


def attend(query, key_rows, value_rows, allowed):
    score_scale = 1.0 / query.shape[-1] ** 0.5
    scores = (
        jnp.einsum("tkgd,nkd->tkgn", query, key_rows, preferred_element_type=jnp.float32)
        * score_scale
    )
    wide_mask = allowed[:, None, None, :]
    scores = jnp.where(wide_mask, scores, NEG_FILL)
    row_top = jnp.max(scores, axis=-1)
    weights = jnp.where(wide_mask, jnp.exp(scores - row_top[..., None]), 0.0)
    weight_sum = jnp.sum(weights, axis=-1)
    head_mix = jnp.einsum(
        "tkgn,nkd->tkgd",
        weights.astype(jnp.bfloat16),
        value_rows,
        preferred_element_type=jnp.float32,
    )
    return (row_top, weight_sum, head_mix)


def combine(first_part, second_part):
    new_top = jnp.maximum(first_part[0], second_part[0])
    first_factor = jnp.exp(first_part[0] - new_top)
    second_factor = jnp.exp(second_part[0] - new_top)
    summed = first_part[1] * first_factor + second_part[1] * second_factor
    mixed_sum = first_part[2] * first_factor[..., None] + second_part[2] * second_factor[..., None]
    return (new_top, summed, mixed_sum)


MASK_FILL = -3e30


def hist_kernel(kv0_ref, q_ref, k_ref, v_ref, bias_ref, cos_ref, sin_ref, acc_out, m_out, l_out, m_sc, l_sc, acc_sc, *, scale, blocks):
    j = pl.program_id(1)

    @pl.when(j == 0)
    def _():
        m_sc[...] = jnp.full(m_sc.shape, NEG_FILL, jnp.float32)
        l_sc[...] = jnp.zeros(l_sc.shape, jnp.float32)
        acc_sc[...] = jnp.zeros(acc_sc.shape, jnp.float32)

    pages, page_len, hd = k_ref.shape
    n = pages * page_len
    keys = k_ref[...].reshape(n, hd).astype(jnp.float32)
    vals = v_ref[...].reshape(n, hd)
    keys = (keys * cos_ref[...] + pltpu.roll(keys, hd // 2, 1) * sin_ref[...]).astype(jnp.bfloat16)
    scores = lax.dot_general(
        q_ref[0], keys, (((1,), (1,)), ((), ())), preferred_element_type=jnp.float32
    )
    scores = scores * scale + bias_ref[0]
    m_old = m_sc[...]
    m_new = jnp.maximum(m_old, jnp.max(scores, axis=1, keepdims=True))
    alpha = jnp.exp(m_old - m_new)
    weights = jnp.exp(scores - m_new)
    l_sc[...] = alpha * l_sc[...] + jnp.sum(weights, axis=1, keepdims=True)
    acc_sc[...] = alpha * acc_sc[...] + jnp.dot(
        weights.astype(jnp.bfloat16), vals, preferred_element_type=jnp.float32
    )
    m_sc[...] = m_new

    @pl.when(j == blocks - 1)
    def _():
        acc_out[0] = acc_sc[...]
        m_out[0] = m_sc[...]
        l_out[0] = l_sc[...]


def hist_attend(kv0, q_k, kv_local, bias, cos2, sin2, pb):
    heads, rows, hd = q_k.shape
    slots, page_len, width = kv_local.shape
    kv_heads = width // (2 * hd)
    blocks = slots // pb
    kernel = functools.partial(hist_kernel, scale=1.0 / hd ** 0.5, blocks=blocks)

    def head_of(h, kv0_ref):
        return (kv0_ref[0] + h) % kv_heads

    grid_spec = pltpu.PrefetchScalarGridSpec(
        num_scalar_prefetch=1,
        grid=(heads, blocks),
        in_specs=[
            pl.BlockSpec((1, rows, hd), lambda h, j, r: (h, 0, 0)),
            pl.BlockSpec((pb, page_len, hd), lambda h, j, r: (j, 0, 2 * head_of(h, r))),
            pl.BlockSpec((pb, page_len, hd), lambda h, j, r: (j, 0, 2 * head_of(h, r) + 1)),
            pl.BlockSpec((1, 1, pb * page_len), lambda h, j, r: (j, 0, 0)),
            pl.BlockSpec((1, hd), lambda h, j, r: (0, 0)),
            pl.BlockSpec((1, hd), lambda h, j, r: (0, 0)),
        ],
        out_specs=[
            pl.BlockSpec((1, rows, hd), lambda h, j, r: (h, 0, 0)),
            pl.BlockSpec((1, rows, 1), lambda h, j, r: (h, 0, 0)),
            pl.BlockSpec((1, rows, 1), lambda h, j, r: (h, 0, 0)),
        ],
        scratch_shapes=[
            pltpu.VMEM((rows, 1), jnp.float32),
            pltpu.VMEM((rows, 1), jnp.float32),
            pltpu.VMEM((rows, hd), jnp.float32),
        ],
    )
    return pl.pallas_call(
        kernel,
        grid_spec=grid_spec,
        out_shape=[
            jax.ShapeDtypeStruct((heads, rows, hd), jnp.float32),
            jax.ShapeDtypeStruct((heads, rows, 1), jnp.float32),
            jax.ShapeDtypeStruct((heads, rows, 1), jnp.float32),
        ],
        compiler_params=pltpu.CompilerParams(dimension_semantics=("arbitrary", "arbitrary")),
    )(jnp.reshape(kv0, (1,)).astype(jnp.int32), q_k, kv_local, kv_local, bias, cos2, sin2)


def body(x_new, kv_pages, w_query, w_keyval, w_out, lengths, page_store, offsets):
    tensors = lax.axis_size("tensor")
    shards = lax.axis_size("store")
    tensor_idx = lax.axis_index("tensor")
    store_idx = lax.axis_index("store")
    tok_count = x_new.shape[0]
    assert tok_count == TURN and lengths.shape[0] == 1
    local_slots = kv_pages.shape[1]
    capacity = local_slots * tensors
    page_len = kv_pages.shape[2]
    kv_heads = kv_pages.shape[3] // (2 * HD)
    group_size = HQ // KVH
    local_heads = w_query.shape[1] // HD
    local_kv = max(1, local_heads // group_size)
    local_group = local_heads // local_kv
    freq_table = inverse_freq(HD)
    kv_first = tensor_idx * local_heads // group_size
    keyval_cols = lax.dynamic_slice_in_dim(w_keyval, kv_first * (2 * HD), local_kv * 2 * HD, 1)
    query_part = jnp.dot(x_new, w_query, preferred_element_type=jnp.float32)
    keyval_part = jnp.dot(x_new, keyval_cols, preferred_element_type=jnp.float32)
    query_sum, keyval_sum = lax.psum((query_part, keyval_part), "store")
    keyval_local = keyval_sum.reshape(tok_count, local_kv, 2, HD)
    tok_ids = jnp.arange(tok_count, dtype=jnp.int32)
    tok_sess = tok_ids // TURN
    tok_pos = table_lookup(lengths, tok_sess) + tok_ids % TURN
    tok_angle = tok_pos.astype(jnp.float32)[:, None, None] * freq_table
    query_rot = to_half(rotate(query_sum.reshape(tok_count, local_heads, HD), tok_angle))
    key_new = to_half(rotate(keyval_local[:, :, 0], tok_angle))
    value_new = to_half(keyval_local[:, :, 1])

    first_slot = store_idx * capacity + tensor_idx * local_slots
    key_sess, key_ok, key_off = slot_meta(
        page_store, lengths, offsets, shards, capacity, first_slot, local_slots, page_len
    )
    pb = local_slots
    bias = jnp.where(key_ok, 0.0, MASK_FILL).astype(jnp.float32)
    bias = bias.reshape(local_slots // pb, 1, pb * page_len)
    hist_angle = offsets[0].astype(jnp.float32) * freq_table
    kv_local = kv_pages.reshape(local_slots, page_len, kv_pages.shape[3])
    cosine = jnp.cos(hist_angle)
    sine = jnp.sin(hist_angle)
    cos2 = jnp.concatenate([cosine, cosine])[None, :]
    sin2 = jnp.concatenate([-sine, sine])[None, :]

    q_heads = jnp.transpose(query_rot, (1, 0, 2))
    q_all = lax.all_gather(q_heads, "tensor", axis=0, tiled=True)
    q_k = q_all.reshape(kv_heads, group_size * tok_count, HD)
    if local_heads % group_size == 0:
        own = hist_attend(
            kv_first, q_heads.reshape(local_kv, group_size * tok_count, HD), kv_local, bias, cos2, sin2, pb
        )
        rest_first = kv_first + local_kv
        q_rest = lax.dynamic_slice_in_dim(
            jnp.concatenate([q_k, q_k], axis=0), rest_first % kv_heads, kv_heads - local_kv, 0
        )
        rest = hist_attend(rest_first % kv_heads, q_rest, kv_local, bias, cos2, sin2, pb)
        parts = []
        for first, second in zip(own, rest):
            rolled = jnp.concatenate([first, second, first, second], axis=0)
            parts.append(lax.dynamic_slice_in_dim(rolled, kv_heads - kv_first, kv_heads, 0))
        acc, top, total = parts
    else:
        acc, top, total = hist_attend(jnp.int32(0), q_k, kv_local, bias, cos2, sin2, pb)
    acc = acc.reshape(HQ, tok_count, HD)
    top = top.reshape(HQ, tok_count)
    total = total.reshape(HQ, tok_count)

    glob_top = jnp.max(lax.all_gather(top, ("tensor", "store")), axis=0)
    factor = jnp.exp(top - glob_top)
    packed = jnp.concatenate(
        [(acc * factor[..., None]).reshape(HQ, tok_count * HD), total * factor], axis=1
    )
    new_allowed = (tok_sess[:, None] == tok_sess[None, :]) & (tok_ids[None, :] <= tok_ids[:, None])
    chunk_heads = HQ // (tensors * shards)
    if HQ % (tensors * shards) == 0 and group_size % chunk_heads == 0:
        packed = lax.psum_scatter(packed, ("tensor", "store"), scatter_dimension=0, tiled=True)
        acc = packed[:, : tok_count * HD].reshape(chunk_heads, tok_count, HD)
        total = packed[:, tok_count * HD :]
        chunk_first = (tensor_idx * shards + store_idx) * chunk_heads
        loc_top = lax.dynamic_slice_in_dim(glob_top, chunk_first, chunk_heads, 0)
        hist_part = (jnp.transpose(loc_top), jnp.transpose(total), jnp.transpose(acc, (1, 0, 2)))
        in_group = store_idx * chunk_heads
        query_chunk = lax.dynamic_slice_in_dim(query_rot, in_group, chunk_heads, 1)
        kv_idx = in_group // group_size
        key_chunk = lax.dynamic_slice_in_dim(key_new, kv_idx, 1, 1)
        value_chunk = lax.dynamic_slice_in_dim(value_new, kv_idx, 1, 1)
        new_part = attend(query_chunk.reshape(tok_count, 1, chunk_heads, HD), key_chunk, value_chunk, new_allowed)
        new_flat = (
            new_part[0].reshape(tok_count, chunk_heads),
            new_part[1].reshape(tok_count, chunk_heads),
            new_part[2].reshape(tok_count, chunk_heads, HD),
        )
        combined = combine(hist_part, new_flat)
        attended = (
            (combined[2] / combined[1][..., None])
            .reshape(tok_count, chunk_heads * HD)
            .astype(jnp.bfloat16)
        )
        attended = lax.all_gather(attended, "store", axis=1, tiled=True)
    else:
        packed = lax.psum_scatter(packed, "tensor", scatter_dimension=0, tiled=True)
        packed = lax.psum(packed, "store")
        acc = packed[:, : tok_count * HD].reshape(local_heads, tok_count, HD)
        total = packed[:, tok_count * HD :]
        loc_top = lax.dynamic_slice_in_dim(glob_top, tensor_idx * local_heads, local_heads, 0)
        hist_part = (jnp.transpose(loc_top), jnp.transpose(total), jnp.transpose(acc, (1, 0, 2)))
        query_local = query_rot.reshape(tok_count, local_kv, local_group, HD)
        new_part = attend(query_local, key_new, value_new, new_allowed)
        new_flat = (
            new_part[0].reshape(tok_count, local_heads),
            new_part[1].reshape(tok_count, local_heads),
            new_part[2].reshape(tok_count, local_heads, HD),
        )
        combined = combine(hist_part, new_flat)
        attended = (
            (combined[2] / combined[1][..., None])
            .reshape(tok_count, local_heads * HD)
            .astype(jnp.bfloat16)
        )
    result = lax.psum_scatter(
        jnp.dot(attended, w_out, preferred_element_type=jnp.float32),
        "tensor",
        scatter_dimension=0,
        tiled=True,
    )
    return result.astype(jnp.bfloat16)


def solution(mesh):
    in_specs = (
        P("groups", "store"),
        P(("groups", "store"), "tensor", None, None),
        P("store", "tensor"),
        P("store", None),
        P("tensor", "store"),
        P("groups"),
        P("groups", None),
        P("groups"),
    )
    out_specs = P(("groups", "tensor"), "store")
    return jax.shard_map(body, mesh=mesh, in_specs=in_specs, out_specs=out_specs, check_vma=False)
```

```python
import math

import jax
import jax.numpy as jnp
import numpy as np
from jax import lax
from jax.sharding import PartitionSpec as P
from jax.experimental import pallas as pl
from jax.experimental.pallas import tpu as pltpu
import functools

HQ = 64
KVH = 8
HD = 128
TURN = 64
MAXPAGES = 256


THETA = 500000.0
NEG_FILL = -1e30
ROPE_FACTOR = 8.0
LOW_FACTOR = 1.0
HIGH_FACTOR = 4.0
INITIAL_CONTEXT = 8192.0


def joined(x, axis, combine):
    everything = jax.tree.map(lambda part: lax.all_gather(part, axis), x)
    first = jax.tree.map(lambda part: part[0], everything)

    def step(k, so_far):
        return combine(so_far, jax.tree.map(lambda part: part[k], everything))

    return lax.fori_loop(1, lax.axis_size(axis), step, first)


def inverse_freq(width):
    steps_half = jnp.arange(width // 2, dtype=jnp.float32)
    base_freq = jnp.exp(-(steps_half * (2.0 / width)) * jnp.log(jnp.float32(THETA)))
    wavelength = 2.0 * math.pi / base_freq
    low_wave = INITIAL_CONTEXT / LOW_FACTOR
    high_wave = INITIAL_CONTEXT / HIGH_FACTOR
    smooth = (INITIAL_CONTEXT / wavelength - LOW_FACTOR) / (HIGH_FACTOR - LOW_FACTOR)
    blended = (1.0 - smooth) * base_freq / ROPE_FACTOR + smooth * base_freq
    scaled = jnp.where(wavelength > low_wave, base_freq / ROPE_FACTOR, blended)
    return jnp.where(wavelength < high_wave, base_freq, scaled)


def rotate(values, rot_angle):
    half_width = values.shape[-1] // 2
    first_half = values[..., :half_width]
    second_half = values[..., half_width:]
    cosine = jnp.cos(rot_angle)
    sine_part = jnp.sin(rot_angle)
    return jnp.concatenate(
        [
            first_half * cosine - second_half * sine_part,
            second_half * cosine + first_half * sine_part,
        ],
        axis=-1,
    )


def to_half(values):
    return values.astype(jnp.bfloat16)


def table_lookup(table, index):
    hits = index[..., None] == jnp.arange(table.shape[0], dtype=jnp.int32)
    return jnp.sum(jnp.where(hits, table, 0), axis=-1)


def page_positions(page_store, shards, capacity):
    store_of = page_store[:, 0]
    onehot = (store_of[:, None] == jnp.arange(shards, dtype=jnp.int32)[None, :]).astype(jnp.int32)
    ranks = jnp.sum((jnp.cumsum(onehot, axis=0) - onehot) * onehot, axis=1)
    return store_of * capacity + ranks


def slot_meta(page_store, lengths, offsets, shards, capacity, first_slot, slot_count, page_len):
    positions = page_positions(page_store, shards, capacity)
    wanted = first_slot + jnp.arange(slot_count, dtype=jnp.int32)
    matches = (positions[:, None] == wanted[None, :]).astype(jnp.int32)
    page_ids = jnp.sum(matches * jnp.arange(positions.shape[0], dtype=jnp.int32)[:, None], axis=0)
    filled = jnp.sum(matches, axis=0) > 0
    slot_sess = page_ids // MAXPAGES
    slot_page = page_ids % MAXPAGES
    key_pos = slot_page[:, None] * page_len + jnp.arange(page_len, dtype=jnp.int32)[None, :]
    key_ok = filled[:, None] & (key_pos < table_lookup(lengths, slot_sess)[:, None])
    key_sess = jnp.broadcast_to(slot_sess[:, None], (slot_count, page_len))
    key_off = jnp.broadcast_to(table_lookup(offsets, slot_sess)[:, None], (slot_count, page_len))
    return (key_sess.reshape(-1), key_ok.reshape(-1), key_off.reshape(-1))


def attend(query, key_rows, value_rows, allowed):
    score_scale = 1.0 / query.shape[-1] ** 0.5
    scores = (
        jnp.einsum("tkgd,nkd->tkgn", query, key_rows, preferred_element_type=jnp.float32)
        * score_scale
    )
    wide_mask = allowed[:, None, None, :]
    scores = jnp.where(wide_mask, scores, NEG_FILL)
    row_top = jnp.max(scores, axis=-1)
    weights = jnp.where(wide_mask, jnp.exp(scores - row_top[..., None]), 0.0)
    weight_sum = jnp.sum(weights, axis=-1)
    head_mix = jnp.einsum(
        "tkgn,nkd->tkgd",
        weights.astype(jnp.bfloat16),
        value_rows,
        preferred_element_type=jnp.float32,
    )
    return (row_top, weight_sum, head_mix)


def combine(first_part, second_part):
    new_top = jnp.maximum(first_part[0], second_part[0])
    first_factor = jnp.exp(first_part[0] - new_top)
    second_factor = jnp.exp(second_part[0] - new_top)
    summed = first_part[1] * first_factor + second_part[1] * second_factor
    mixed_sum = first_part[2] * first_factor[..., None] + second_part[2] * second_factor[..., None]
    return (new_top, summed, mixed_sum)


MASK_FILL = -3e30


def hist_kernel(kv0_ref, q_ref, k_ref, v_ref, bias_ref, cos_ref, sin_ref, acc_out, m_out, l_out, m_sc, l_sc, acc_sc, *, scale, blocks):
    j = pl.program_id(1)

    @pl.when(j == 0)
    def _():
        m_sc[...] = jnp.full(m_sc.shape, NEG_FILL, jnp.float32)
        l_sc[...] = jnp.zeros(l_sc.shape, jnp.float32)
        acc_sc[...] = jnp.zeros(acc_sc.shape, jnp.float32)

    pages, page_len, hd = k_ref.shape
    n = pages * page_len
    keys = k_ref[...].reshape(n, hd).astype(jnp.float32)
    vals = v_ref[...].reshape(n, hd)
    keys = (keys * cos_ref[...] + pltpu.roll(keys, hd // 2, 1) * sin_ref[...]).astype(jnp.bfloat16)
    scores = lax.dot_general(
        q_ref[0], keys, (((1,), (1,)), ((), ())), preferred_element_type=jnp.float32
    )
    scores = scores * scale + bias_ref[0]
    m_old = m_sc[...]
    m_new = jnp.maximum(m_old, jnp.max(scores, axis=1, keepdims=True))
    alpha = jnp.exp(m_old - m_new)
    weights = jnp.exp(scores - m_new)
    l_sc[...] = alpha * l_sc[...] + jnp.sum(weights, axis=1, keepdims=True)
    acc_sc[...] = alpha * acc_sc[...] + jnp.dot(
        weights.astype(jnp.bfloat16), vals, preferred_element_type=jnp.float32
    )
    m_sc[...] = m_new

    @pl.when(j == blocks - 1)
    def _():
        acc_out[0] = acc_sc[...]
        m_out[0] = m_sc[...]
        l_out[0] = l_sc[...]


def hist_attend(kv0, q_k, kv_local, bias, cos2, sin2, pb):
    heads, rows, hd = q_k.shape
    slots, page_len, width = kv_local.shape
    kv_heads = width // (2 * hd)
    blocks = slots // pb
    kernel = functools.partial(hist_kernel, scale=1.0 / hd ** 0.5, blocks=blocks)

    def head_of(h, kv0_ref):
        return (kv0_ref[0] + h) % kv_heads

    grid_spec = pltpu.PrefetchScalarGridSpec(
        num_scalar_prefetch=1,
        grid=(heads, blocks),
        in_specs=[
            pl.BlockSpec((1, rows, hd), lambda h, j, r: (h, 0, 0)),
            pl.BlockSpec((pb, page_len, hd), lambda h, j, r: (j, 0, 2 * head_of(h, r))),
            pl.BlockSpec((pb, page_len, hd), lambda h, j, r: (j, 0, 2 * head_of(h, r) + 1)),
            pl.BlockSpec((1, 1, pb * page_len), lambda h, j, r: (j, 0, 0)),
            pl.BlockSpec((1, hd), lambda h, j, r: (0, 0)),
            pl.BlockSpec((1, hd), lambda h, j, r: (0, 0)),
        ],
        out_specs=[
            pl.BlockSpec((1, rows, hd), lambda h, j, r: (h, 0, 0)),
            pl.BlockSpec((1, rows, 1), lambda h, j, r: (h, 0, 0)),
            pl.BlockSpec((1, rows, 1), lambda h, j, r: (h, 0, 0)),
        ],
        scratch_shapes=[
            pltpu.VMEM((rows, 1), jnp.float32),
            pltpu.VMEM((rows, 1), jnp.float32),
            pltpu.VMEM((rows, hd), jnp.float32),
        ],
    )
    return pl.pallas_call(
        kernel,
        grid_spec=grid_spec,
        out_shape=[
            jax.ShapeDtypeStruct((heads, rows, hd), jnp.float32),
            jax.ShapeDtypeStruct((heads, rows, 1), jnp.float32),
            jax.ShapeDtypeStruct((heads, rows, 1), jnp.float32),
        ],
        compiler_params=pltpu.CompilerParams(dimension_semantics=("arbitrary", "arbitrary")),
    )(jnp.reshape(kv0, (1,)).astype(jnp.int32), q_k, kv_local, kv_local, bias, cos2, sin2)


def axis_sum(x, axis):
    n = lax.axis_size(axis)
    if n & (n - 1):
        return lax.psum(x, axis)
    d = 1
    while d < n:
        x = x + lax.ppermute(x, axis, perm=[(i, i ^ d) for i in range(n)])
        d *= 2
    return x


def body(x_new, kv_pages, w_query, w_keyval, w_out, lengths, page_store, offsets):
    tensors = lax.axis_size("tensor")
    shards = lax.axis_size("store")
    tensor_idx = lax.axis_index("tensor")
    store_idx = lax.axis_index("store")
    tok_count = x_new.shape[0]
    assert tok_count == TURN and lengths.shape[0] == 1
    local_slots = kv_pages.shape[1]
    capacity = local_slots * tensors
    page_len = kv_pages.shape[2]
    kv_heads = kv_pages.shape[3] // (2 * HD)
    group_size = HQ // KVH
    local_heads = w_query.shape[1] // HD
    local_kv = max(1, local_heads // group_size)
    local_group = local_heads // local_kv
    freq_table = inverse_freq(HD)
    kv_first = tensor_idx * local_heads // group_size
    keyval_cols = lax.dynamic_slice_in_dim(w_keyval, kv_first * (2 * HD), local_kv * 2 * HD, 1)
    query_part = jnp.dot(x_new, w_query, preferred_element_type=jnp.float32)
    keyval_part = jnp.dot(x_new, keyval_cols, preferred_element_type=jnp.float32)
    width_q = query_part.shape[1]
    both = axis_sum(jnp.concatenate([query_part, keyval_part], axis=1), "store")
    query_sum, keyval_sum = both[:, :width_q], both[:, width_q:]
    keyval_local = keyval_sum.reshape(tok_count, local_kv, 2, HD)
    tok_ids = jnp.arange(tok_count, dtype=jnp.int32)
    tok_sess = tok_ids // TURN
    tok_pos = table_lookup(lengths, tok_sess) + tok_ids % TURN
    tok_angle = tok_pos.astype(jnp.float32)[:, None, None] * freq_table
    query_rot = to_half(rotate(query_sum.reshape(tok_count, local_heads, HD), tok_angle))
    key_new = to_half(rotate(keyval_local[:, :, 0], tok_angle))
    value_new = to_half(keyval_local[:, :, 1])

    first_slot = store_idx * capacity + tensor_idx * local_slots
    key_sess, key_ok, key_off = slot_meta(
        page_store, lengths, offsets, shards, capacity, first_slot, local_slots, page_len
    )
    pb = local_slots
    bias = jnp.where(key_ok, 0.0, MASK_FILL).astype(jnp.float32)
    bias = bias.reshape(local_slots // pb, 1, pb * page_len)
    hist_angle = offsets[0].astype(jnp.float32) * freq_table
    kv_local = kv_pages.reshape(local_slots, page_len, kv_pages.shape[3])
    cosine = jnp.cos(hist_angle)
    sine = jnp.sin(hist_angle)
    cos2 = jnp.concatenate([cosine, cosine])[None, :]
    sin2 = jnp.concatenate([-sine, sine])[None, :]

    q_heads = jnp.transpose(query_rot, (1, 0, 2))
    q_all = lax.all_gather(q_heads, "tensor", axis=0, tiled=True)
    q_k = q_all.reshape(kv_heads, group_size * tok_count, HD)
    if local_heads % group_size == 0:
        own = hist_attend(
            kv_first, q_heads.reshape(local_kv, group_size * tok_count, HD), kv_local, bias, cos2, sin2, pb
        )
        rest_first = kv_first + local_kv
        q_rest = lax.dynamic_slice_in_dim(
            jnp.concatenate([q_k, q_k], axis=0), rest_first % kv_heads, kv_heads - local_kv, 0
        )
        rest = hist_attend(rest_first % kv_heads, q_rest, kv_local, bias, cos2, sin2, pb)
        parts = []
        for first, second in zip(own, rest):
            rolled = jnp.concatenate([first, second, first, second], axis=0)
            parts.append(lax.dynamic_slice_in_dim(rolled, kv_heads - kv_first, kv_heads, 0))
        acc, top, total = parts
    else:
        acc, top, total = hist_attend(jnp.int32(0), q_k, kv_local, bias, cos2, sin2, pb)
    acc = acc.reshape(HQ, tok_count, HD)
    top = top.reshape(HQ, tok_count)
    total = total.reshape(HQ, tok_count)

    glob_top = jnp.max(lax.all_gather(top, ("tensor", "store")), axis=0)
    factor = jnp.exp(top - glob_top)
    packed = jnp.concatenate(
        [(acc * factor[..., None]).reshape(HQ, tok_count * HD), total * factor], axis=1
    )
    packed = lax.psum_scatter(packed, "tensor", scatter_dimension=0, tiled=True)
    packed = axis_sum(packed, "store")
    acc = packed[:, : tok_count * HD].reshape(local_heads, tok_count, HD)
    total = packed[:, tok_count * HD :]
    loc_top = lax.dynamic_slice_in_dim(glob_top, tensor_idx * local_heads, local_heads, 0)
    hist_part = (
        jnp.transpose(loc_top),
        jnp.transpose(total),
        jnp.transpose(acc, (1, 0, 2)),
    )

    query_local = query_rot.reshape(tok_count, local_kv, local_group, HD)
    new_allowed = (tok_sess[:, None] == tok_sess[None, :]) & (tok_ids[None, :] <= tok_ids[:, None])
    new_part = attend(query_local, key_new, value_new, new_allowed)
    new_flat = (
        new_part[0].reshape(tok_count, local_heads),
        new_part[1].reshape(tok_count, local_heads),
        new_part[2].reshape(tok_count, local_heads, HD),
    )
    combined = combine(hist_part, new_flat)
    attended = (
        (combined[2] / combined[1][..., None])
        .reshape(tok_count, local_heads * HD)
        .astype(jnp.bfloat16)
    )
    result = lax.psum_scatter(
        jnp.dot(attended, w_out, preferred_element_type=jnp.float32),
        "tensor",
        scatter_dimension=0,
        tiled=True,
    )
    return result.astype(jnp.bfloat16)


def solution(mesh):
    in_specs = (
        P("groups", "store"),
        P(("groups", "store"), "tensor", None, None),
        P("store", "tensor"),
        P("store", None),
        P("tensor", "store"),
        P("groups"),
        P("groups", None),
        P("groups"),
    )
    out_specs = P(("groups", "tensor"), "store")
    return jax.shard_map(body, mesh=mesh, in_specs=in_specs, out_specs=out_specs, check_vma=False)
```

```python
import math

import jax
import jax.numpy as jnp
import numpy as np
from jax import lax
from jax.sharding import PartitionSpec as P
from jax.experimental import pallas as pl
from jax.experimental.pallas import tpu as pltpu
import functools

HQ = 64
KVH = 8
HD = 128
TURN = 64
MAXPAGES = 256


THETA = 500000.0
NEG_FILL = -1e30
ROPE_FACTOR = 8.0
LOW_FACTOR = 1.0
HIGH_FACTOR = 4.0
INITIAL_CONTEXT = 8192.0


def joined(x, axis, combine):
    everything = jax.tree.map(lambda part: lax.all_gather(part, axis), x)
    first = jax.tree.map(lambda part: part[0], everything)

    def step(k, so_far):
        return combine(so_far, jax.tree.map(lambda part: part[k], everything))

    return lax.fori_loop(1, lax.axis_size(axis), step, first)


def inverse_freq(width):
    steps_half = jnp.arange(width // 2, dtype=jnp.float32)
    base_freq = jnp.exp(-(steps_half * (2.0 / width)) * jnp.log(jnp.float32(THETA)))
    wavelength = 2.0 * math.pi / base_freq
    low_wave = INITIAL_CONTEXT / LOW_FACTOR
    high_wave = INITIAL_CONTEXT / HIGH_FACTOR
    smooth = (INITIAL_CONTEXT / wavelength - LOW_FACTOR) / (HIGH_FACTOR - LOW_FACTOR)
    blended = (1.0 - smooth) * base_freq / ROPE_FACTOR + smooth * base_freq
    scaled = jnp.where(wavelength > low_wave, base_freq / ROPE_FACTOR, blended)
    return jnp.where(wavelength < high_wave, base_freq, scaled)


def rotate(values, rot_angle):
    half_width = values.shape[-1] // 2
    first_half = values[..., :half_width]
    second_half = values[..., half_width:]
    cosine = jnp.cos(rot_angle)
    sine_part = jnp.sin(rot_angle)
    return jnp.concatenate(
        [
            first_half * cosine - second_half * sine_part,
            second_half * cosine + first_half * sine_part,
        ],
        axis=-1,
    )


def to_half(values):
    return values.astype(jnp.bfloat16)


def table_lookup(table, index):
    hits = index[..., None] == jnp.arange(table.shape[0], dtype=jnp.int32)
    return jnp.sum(jnp.where(hits, table, 0), axis=-1)


def page_positions(page_store, shards, capacity):
    store_of = page_store[:, 0]
    onehot = (store_of[:, None] == jnp.arange(shards, dtype=jnp.int32)[None, :]).astype(jnp.int32)
    ranks = jnp.sum((jnp.cumsum(onehot, axis=0) - onehot) * onehot, axis=1)
    return store_of * capacity + ranks


def slot_meta(page_store, lengths, offsets, shards, capacity, first_slot, slot_count, page_len):
    positions = page_positions(page_store, shards, capacity)
    wanted = first_slot + jnp.arange(slot_count, dtype=jnp.int32)
    matches = (positions[:, None] == wanted[None, :]).astype(jnp.int32)
    page_ids = jnp.sum(matches * jnp.arange(positions.shape[0], dtype=jnp.int32)[:, None], axis=0)
    filled = jnp.sum(matches, axis=0) > 0
    slot_sess = page_ids // MAXPAGES
    slot_page = page_ids % MAXPAGES
    key_pos = slot_page[:, None] * page_len + jnp.arange(page_len, dtype=jnp.int32)[None, :]
    key_ok = filled[:, None] & (key_pos < table_lookup(lengths, slot_sess)[:, None])
    key_sess = jnp.broadcast_to(slot_sess[:, None], (slot_count, page_len))
    key_off = jnp.broadcast_to(table_lookup(offsets, slot_sess)[:, None], (slot_count, page_len))
    return (key_sess.reshape(-1), key_ok.reshape(-1), key_off.reshape(-1))


def attend(query, key_rows, value_rows, allowed):
    score_scale = 1.0 / query.shape[-1] ** 0.5
    scores = (
        jnp.einsum("tkgd,nkd->tkgn", query, key_rows, preferred_element_type=jnp.float32)
        * score_scale
    )
    wide_mask = allowed[:, None, None, :]
    scores = jnp.where(wide_mask, scores, NEG_FILL)
    row_top = jnp.max(scores, axis=-1)
    weights = jnp.where(wide_mask, jnp.exp(scores - row_top[..., None]), 0.0)
    weight_sum = jnp.sum(weights, axis=-1)
    head_mix = jnp.einsum(
        "tkgn,nkd->tkgd",
        weights.astype(jnp.bfloat16),
        value_rows,
        preferred_element_type=jnp.float32,
    )
    return (row_top, weight_sum, head_mix)


def combine(first_part, second_part):
    new_top = jnp.maximum(first_part[0], second_part[0])
    first_factor = jnp.exp(first_part[0] - new_top)
    second_factor = jnp.exp(second_part[0] - new_top)
    summed = first_part[1] * first_factor + second_part[1] * second_factor
    mixed_sum = first_part[2] * first_factor[..., None] + second_part[2] * second_factor[..., None]
    return (new_top, summed, mixed_sum)


MASK_FILL = -3e30


def hist_kernel(kv0_ref, q_ref, k_ref, v_ref, bias_ref, cos_ref, sin_ref, acc_out, m_out, l_out, m_sc, l_sc, acc_sc, *, scale, blocks):
    j = pl.program_id(1)

    @pl.when(j == 0)
    def _():
        m_sc[...] = jnp.full(m_sc.shape, NEG_FILL, jnp.float32)
        l_sc[...] = jnp.zeros(l_sc.shape, jnp.float32)
        acc_sc[...] = jnp.zeros(acc_sc.shape, jnp.float32)

    pages, page_len, hd = k_ref.shape
    n = pages * page_len
    keys = k_ref[...].reshape(n, hd).astype(jnp.float32)
    vals = v_ref[...].reshape(n, hd)
    keys = (keys * cos_ref[...] + pltpu.roll(keys, hd // 2, 1) * sin_ref[...]).astype(jnp.bfloat16)
    scores = lax.dot_general(
        q_ref[0], keys, (((1,), (1,)), ((), ())), preferred_element_type=jnp.float32
    )
    scores = scores * scale + bias_ref[0]
    m_old = m_sc[...]
    m_new = jnp.maximum(m_old, jnp.max(scores, axis=1, keepdims=True))
    alpha = jnp.exp(m_old - m_new)
    weights = jnp.exp(scores - m_new)
    l_sc[...] = alpha * l_sc[...] + jnp.sum(weights, axis=1, keepdims=True)
    acc_sc[...] = alpha * acc_sc[...] + jnp.dot(
        weights.astype(jnp.bfloat16), vals, preferred_element_type=jnp.float32
    )
    m_sc[...] = m_new

    @pl.when(j == blocks - 1)
    def _():
        acc_out[0] = acc_sc[...]
        m_out[0] = m_sc[...]
        l_out[0] = l_sc[...]


def hist_attend(kv0, q_k, kv_local, bias, cos2, sin2, pb):
    heads, rows, hd = q_k.shape
    slots, page_len, width = kv_local.shape
    kv_heads = width // (2 * hd)
    blocks = slots // pb
    kernel = functools.partial(hist_kernel, scale=1.0 / hd ** 0.5, blocks=blocks)

    def head_of(h, kv0_ref):
        return (kv0_ref[0] + h) % kv_heads

    grid_spec = pltpu.PrefetchScalarGridSpec(
        num_scalar_prefetch=1,
        grid=(heads, blocks),
        in_specs=[
            pl.BlockSpec((1, rows, hd), lambda h, j, r: (h, 0, 0)),
            pl.BlockSpec((pb, page_len, hd), lambda h, j, r: (j, 0, 2 * head_of(h, r))),
            pl.BlockSpec((pb, page_len, hd), lambda h, j, r: (j, 0, 2 * head_of(h, r) + 1)),
            pl.BlockSpec((1, 1, pb * page_len), lambda h, j, r: (j, 0, 0)),
            pl.BlockSpec((1, hd), lambda h, j, r: (0, 0)),
            pl.BlockSpec((1, hd), lambda h, j, r: (0, 0)),
        ],
        out_specs=[
            pl.BlockSpec((1, rows, hd), lambda h, j, r: (h, 0, 0)),
            pl.BlockSpec((1, rows, 1), lambda h, j, r: (h, 0, 0)),
            pl.BlockSpec((1, rows, 1), lambda h, j, r: (h, 0, 0)),
        ],
        scratch_shapes=[
            pltpu.VMEM((rows, 1), jnp.float32),
            pltpu.VMEM((rows, 1), jnp.float32),
            pltpu.VMEM((rows, hd), jnp.float32),
        ],
    )
    return pl.pallas_call(
        kernel,
        grid_spec=grid_spec,
        out_shape=[
            jax.ShapeDtypeStruct((heads, rows, hd), jnp.float32),
            jax.ShapeDtypeStruct((heads, rows, 1), jnp.float32),
            jax.ShapeDtypeStruct((heads, rows, 1), jnp.float32),
        ],
        compiler_params=pltpu.CompilerParams(dimension_semantics=("arbitrary", "arbitrary")),
    )(jnp.reshape(kv0, (1,)).astype(jnp.int32), q_k, kv_local, kv_local, bias, cos2, sin2)


def axis_reduce(x, axis, op):
    n = lax.axis_size(axis)
    d = 1
    while d < n:
        x = op(x, lax.ppermute(x, axis, perm=[(i, i ^ d) for i in range(n)]))
        d *= 2
    return x


def axis_sum(x, axis):
    n = lax.axis_size(axis)
    if n & (n - 1):
        return lax.psum(x, axis)
    return axis_reduce(x, axis, jnp.add)


def axis_max(x, axes):
    if any(lax.axis_size(a) & (lax.axis_size(a) - 1) for a in axes):
        return jnp.max(lax.all_gather(x, axes), axis=0)
    for a in axes:
        x = axis_reduce(x, a, jnp.maximum)
    return x


def body(x_new, kv_pages, w_query, w_keyval, w_out, lengths, page_store, offsets):
    tensors = lax.axis_size("tensor")
    shards = lax.axis_size("store")
    tensor_idx = lax.axis_index("tensor")
    store_idx = lax.axis_index("store")
    tok_count = x_new.shape[0]
    assert tok_count == TURN and lengths.shape[0] == 1
    local_slots = kv_pages.shape[1]
    capacity = local_slots * tensors
    page_len = kv_pages.shape[2]
    kv_heads = kv_pages.shape[3] // (2 * HD)
    group_size = HQ // KVH
    local_heads = w_query.shape[1] // HD
    local_kv = max(1, local_heads // group_size)
    local_group = local_heads // local_kv
    freq_table = inverse_freq(HD)
    kv_first = tensor_idx * local_heads // group_size
    keyval_cols = lax.dynamic_slice_in_dim(w_keyval, kv_first * (2 * HD), local_kv * 2 * HD, 1)
    query_part = jnp.dot(x_new, w_query, preferred_element_type=jnp.float32)
    keyval_part = jnp.dot(x_new, keyval_cols, preferred_element_type=jnp.float32)
    width_q = query_part.shape[1]
    both = axis_sum(jnp.concatenate([query_part, keyval_part], axis=1), "store")
    query_sum, keyval_sum = both[:, :width_q], both[:, width_q:]
    keyval_local = keyval_sum.reshape(tok_count, local_kv, 2, HD)
    tok_ids = jnp.arange(tok_count, dtype=jnp.int32)
    tok_sess = tok_ids // TURN
    tok_pos = table_lookup(lengths, tok_sess) + tok_ids % TURN
    tok_angle = tok_pos.astype(jnp.float32)[:, None, None] * freq_table
    query_rot = to_half(rotate(query_sum.reshape(tok_count, local_heads, HD), tok_angle))
    key_new = to_half(rotate(keyval_local[:, :, 0], tok_angle))
    value_new = to_half(keyval_local[:, :, 1])

    first_slot = store_idx * capacity + tensor_idx * local_slots
    key_sess, key_ok, key_off = slot_meta(
        page_store, lengths, offsets, shards, capacity, first_slot, local_slots, page_len
    )
    pb = local_slots
    bias = jnp.where(key_ok, 0.0, MASK_FILL).astype(jnp.float32)
    bias = bias.reshape(local_slots // pb, 1, pb * page_len)
    hist_angle = offsets[0].astype(jnp.float32) * freq_table
    kv_local = kv_pages.reshape(local_slots, page_len, kv_pages.shape[3])
    cosine = jnp.cos(hist_angle)
    sine = jnp.sin(hist_angle)
    cos2 = jnp.concatenate([cosine, cosine])[None, :]
    sin2 = jnp.concatenate([-sine, sine])[None, :]

    q_heads = jnp.transpose(query_rot, (1, 0, 2))
    q_all = lax.all_gather(q_heads, "tensor", axis=0, tiled=True)
    q_k = q_all.reshape(kv_heads, group_size * tok_count, HD)
    if local_heads % group_size == 0:
        own = hist_attend(
            kv_first, q_heads.reshape(local_kv, group_size * tok_count, HD), kv_local, bias, cos2, sin2, pb
        )
        rest_first = kv_first + local_kv
        q_rest = lax.dynamic_slice_in_dim(
            jnp.concatenate([q_k, q_k], axis=0), rest_first % kv_heads, kv_heads - local_kv, 0
        )
        rest = hist_attend(rest_first % kv_heads, q_rest, kv_local, bias, cos2, sin2, pb)
        parts = []
        for first, second in zip(own, rest):
            rolled = jnp.concatenate([first, second, first, second], axis=0)
            parts.append(lax.dynamic_slice_in_dim(rolled, kv_heads - kv_first, kv_heads, 0))
        acc, top, total = parts
    else:
        acc, top, total = hist_attend(jnp.int32(0), q_k, kv_local, bias, cos2, sin2, pb)
    acc = acc.reshape(HQ, tok_count, HD)
    top = top.reshape(HQ, tok_count)
    total = total.reshape(HQ, tok_count)

    glob_top = axis_max(top, ("store", "tensor"))
    factor = jnp.exp(top - glob_top)
    packed = jnp.concatenate(
        [(acc * factor[..., None]).reshape(HQ, tok_count * HD), total * factor], axis=1
    )
    packed = lax.psum_scatter(packed, "tensor", scatter_dimension=0, tiled=True)
    packed = axis_sum(packed, "store")
    acc = packed[:, : tok_count * HD].reshape(local_heads, tok_count, HD)
    total = packed[:, tok_count * HD :]
    loc_top = lax.dynamic_slice_in_dim(glob_top, tensor_idx * local_heads, local_heads, 0)
    hist_part = (
        jnp.transpose(loc_top),
        jnp.transpose(total),
        jnp.transpose(acc, (1, 0, 2)),
    )

    query_local = query_rot.reshape(tok_count, local_kv, local_group, HD)
    new_allowed = (tok_sess[:, None] == tok_sess[None, :]) & (tok_ids[None, :] <= tok_ids[:, None])
    new_part = attend(query_local, key_new, value_new, new_allowed)
    new_flat = (
        new_part[0].reshape(tok_count, local_heads),
        new_part[1].reshape(tok_count, local_heads),
        new_part[2].reshape(tok_count, local_heads, HD),
    )
    combined = combine(hist_part, new_flat)
    attended = (
        (combined[2] / combined[1][..., None])
        .reshape(tok_count, local_heads * HD)
        .astype(jnp.bfloat16)
    )
    result = lax.psum_scatter(
        jnp.dot(attended, w_out, preferred_element_type=jnp.float32),
        "tensor",
        scatter_dimension=0,
        tiled=True,
    )
    return result.astype(jnp.bfloat16)


def solution(mesh):
    in_specs = (
        P("groups", "store"),
        P(("groups", "store"), "tensor", None, None),
        P("store", "tensor"),
        P("store", None),
        P("tensor", "store"),
        P("groups"),
        P("groups", None),
        P("groups"),
    )
    out_specs = P(("groups", "tensor"), "store")
    return jax.shard_map(body, mesh=mesh, in_specs=in_specs, out_specs=out_specs, check_vma=False)
```

```python
import math

import jax
import jax.numpy as jnp
import numpy as np
from jax import lax
from jax.sharding import PartitionSpec as P
from jax.experimental import pallas as pl
from jax.experimental.pallas import tpu as pltpu
import functools

HQ = 64
KVH = 8
HD = 128
TURN = 64
MAXPAGES = 256


THETA = 500000.0
NEG_FILL = -1e30
ROPE_FACTOR = 8.0
LOW_FACTOR = 1.0
HIGH_FACTOR = 4.0
INITIAL_CONTEXT = 8192.0


def joined(x, axis, combine):
    everything = jax.tree.map(lambda part: lax.all_gather(part, axis), x)
    first = jax.tree.map(lambda part: part[0], everything)

    def step(k, so_far):
        return combine(so_far, jax.tree.map(lambda part: part[k], everything))

    return lax.fori_loop(1, lax.axis_size(axis), step, first)


def inverse_freq(width):
    steps_half = jnp.arange(width // 2, dtype=jnp.float32)
    base_freq = jnp.exp(-(steps_half * (2.0 / width)) * jnp.log(jnp.float32(THETA)))
    wavelength = 2.0 * math.pi / base_freq
    low_wave = INITIAL_CONTEXT / LOW_FACTOR
    high_wave = INITIAL_CONTEXT / HIGH_FACTOR
    smooth = (INITIAL_CONTEXT / wavelength - LOW_FACTOR) / (HIGH_FACTOR - LOW_FACTOR)
    blended = (1.0 - smooth) * base_freq / ROPE_FACTOR + smooth * base_freq
    scaled = jnp.where(wavelength > low_wave, base_freq / ROPE_FACTOR, blended)
    return jnp.where(wavelength < high_wave, base_freq, scaled)


def rotate(values, rot_angle):
    half_width = values.shape[-1] // 2
    first_half = values[..., :half_width]
    second_half = values[..., half_width:]
    cosine = jnp.cos(rot_angle)
    sine_part = jnp.sin(rot_angle)
    return jnp.concatenate(
        [
            first_half * cosine - second_half * sine_part,
            second_half * cosine + first_half * sine_part,
        ],
        axis=-1,
    )


def to_half(values):
    return values.astype(jnp.bfloat16)


def table_lookup(table, index):
    hits = index[..., None] == jnp.arange(table.shape[0], dtype=jnp.int32)
    return jnp.sum(jnp.where(hits, table, 0), axis=-1)


def page_positions(page_store, shards, capacity):
    store_of = page_store[:, 0]
    onehot = (store_of[:, None] == jnp.arange(shards, dtype=jnp.int32)[None, :]).astype(jnp.int32)
    ranks = jnp.sum((jnp.cumsum(onehot, axis=0) - onehot) * onehot, axis=1)
    return store_of * capacity + ranks


def slot_meta(page_store, lengths, offsets, shards, capacity, first_slot, slot_count, page_len):
    positions = page_positions(page_store, shards, capacity)
    wanted = first_slot + jnp.arange(slot_count, dtype=jnp.int32)
    matches = (positions[:, None] == wanted[None, :]).astype(jnp.int32)
    page_ids = jnp.sum(matches * jnp.arange(positions.shape[0], dtype=jnp.int32)[:, None], axis=0)
    filled = jnp.sum(matches, axis=0) > 0
    slot_sess = page_ids // MAXPAGES
    slot_page = page_ids % MAXPAGES
    key_pos = slot_page[:, None] * page_len + jnp.arange(page_len, dtype=jnp.int32)[None, :]
    key_ok = filled[:, None] & (key_pos < table_lookup(lengths, slot_sess)[:, None])
    key_sess = jnp.broadcast_to(slot_sess[:, None], (slot_count, page_len))
    key_off = jnp.broadcast_to(table_lookup(offsets, slot_sess)[:, None], (slot_count, page_len))
    return (key_sess.reshape(-1), key_ok.reshape(-1), key_off.reshape(-1))


def attend(query, key_rows, value_rows, allowed):
    score_scale = 1.0 / query.shape[-1] ** 0.5
    scores = (
        jnp.einsum("tkgd,nkd->tkgn", query, key_rows, preferred_element_type=jnp.float32)
        * score_scale
    )
    wide_mask = allowed[:, None, None, :]
    scores = jnp.where(wide_mask, scores, NEG_FILL)
    row_top = jnp.max(scores, axis=-1)
    weights = jnp.where(wide_mask, jnp.exp(scores - row_top[..., None]), 0.0)
    weight_sum = jnp.sum(weights, axis=-1)
    head_mix = jnp.einsum(
        "tkgn,nkd->tkgd",
        weights.astype(jnp.bfloat16),
        value_rows,
        preferred_element_type=jnp.float32,
    )
    return (row_top, weight_sum, head_mix)


def combine(first_part, second_part):
    new_top = jnp.maximum(first_part[0], second_part[0])
    first_factor = jnp.exp(first_part[0] - new_top)
    second_factor = jnp.exp(second_part[0] - new_top)
    summed = first_part[1] * first_factor + second_part[1] * second_factor
    mixed_sum = first_part[2] * first_factor[..., None] + second_part[2] * second_factor[..., None]
    return (new_top, summed, mixed_sum)


MASK_FILL = -3e30


def hist_kernel(kv0_ref, q_ref, k_ref, v_ref, bias_ref, cos_ref, sin_ref, acc_out, m_out, l_out, m_sc, l_sc, acc_sc, *, scale, blocks):
    j = pl.program_id(1)

    @pl.when(j == 0)
    def _():
        m_sc[...] = jnp.full(m_sc.shape, NEG_FILL, jnp.float32)
        l_sc[...] = jnp.zeros(l_sc.shape, jnp.float32)
        acc_sc[...] = jnp.zeros(acc_sc.shape, jnp.float32)

    pages, page_len, hd = k_ref.shape
    n = pages * page_len
    keys = k_ref[...].reshape(n, hd).astype(jnp.float32)
    vals = v_ref[...].reshape(n, hd)
    keys = (keys * cos_ref[...] + pltpu.roll(keys, hd // 2, 1) * sin_ref[...]).astype(jnp.bfloat16)
    scores = lax.dot_general(
        q_ref[0], keys, (((1,), (1,)), ((), ())), preferred_element_type=jnp.float32
    )
    scores = scores * scale + bias_ref[0]
    m_old = m_sc[...]
    m_new = jnp.maximum(m_old, jnp.max(scores, axis=1, keepdims=True))
    alpha = jnp.exp(m_old - m_new)
    weights = jnp.exp(scores - m_new)
    l_sc[...] = alpha * l_sc[...] + jnp.sum(weights, axis=1, keepdims=True)
    acc_sc[...] = alpha * acc_sc[...] + jnp.dot(
        weights.astype(jnp.bfloat16), vals, preferred_element_type=jnp.float32
    )
    m_sc[...] = m_new

    @pl.when(j == blocks - 1)
    def _():
        acc_out[0] = acc_sc[...]
        m_out[0] = m_sc[...]
        l_out[0] = l_sc[...]


def hist_attend(kv0, q_k, kv_local, bias, cos2, sin2, pb):
    heads, rows, hd = q_k.shape
    slots, page_len, width = kv_local.shape
    kv_heads = width // (2 * hd)
    blocks = slots // pb
    kernel = functools.partial(hist_kernel, scale=1.0 / hd ** 0.5, blocks=blocks)

    def head_of(h, kv0_ref):
        return (kv0_ref[0] + h) % kv_heads

    grid_spec = pltpu.PrefetchScalarGridSpec(
        num_scalar_prefetch=1,
        grid=(heads, blocks),
        in_specs=[
            pl.BlockSpec((1, rows, hd), lambda h, j, r: (h, 0, 0)),
            pl.BlockSpec((pb, page_len, hd), lambda h, j, r: (j, 0, 2 * head_of(h, r))),
            pl.BlockSpec((pb, page_len, hd), lambda h, j, r: (j, 0, 2 * head_of(h, r) + 1)),
            pl.BlockSpec((1, 1, pb * page_len), lambda h, j, r: (j, 0, 0)),
            pl.BlockSpec((1, hd), lambda h, j, r: (0, 0)),
            pl.BlockSpec((1, hd), lambda h, j, r: (0, 0)),
        ],
        out_specs=[
            pl.BlockSpec((1, rows, hd), lambda h, j, r: (h, 0, 0)),
            pl.BlockSpec((1, rows, 1), lambda h, j, r: (h, 0, 0)),
            pl.BlockSpec((1, rows, 1), lambda h, j, r: (h, 0, 0)),
        ],
        scratch_shapes=[
            pltpu.VMEM((rows, 1), jnp.float32),
            pltpu.VMEM((rows, 1), jnp.float32),
            pltpu.VMEM((rows, hd), jnp.float32),
        ],
    )
    return pl.pallas_call(
        kernel,
        grid_spec=grid_spec,
        out_shape=[
            jax.ShapeDtypeStruct((heads, rows, hd), jnp.float32),
            jax.ShapeDtypeStruct((heads, rows, 1), jnp.float32),
            jax.ShapeDtypeStruct((heads, rows, 1), jnp.float32),
        ],
        compiler_params=pltpu.CompilerParams(dimension_semantics=("arbitrary", "arbitrary")),
    )(jnp.reshape(kv0, (1,)).astype(jnp.int32), q_k, kv_local, kv_local, bias, cos2, sin2)


def axis_reduce(x, axis, op):
    n = lax.axis_size(axis)
    d = 1
    while d < n:
        x = op(x, lax.ppermute(x, axis, perm=[(i, i ^ d) for i in range(n)]))
        d *= 2
    return x


def bit_scatter(block, axis):
    n = lax.axis_size(axis)
    idx = lax.axis_index(axis)
    d = 1
    while d < n:
        bit = (idx // d) % 2
        keep = lax.dynamic_index_in_dim(block, bit, 0, keepdims=False)
        send = lax.dynamic_index_in_dim(block, 1 - bit, 0, keepdims=False)
        block = keep + lax.ppermute(send, axis, perm=[(i, i ^ d) for i in range(n)])
        d *= 2
    return block


def axis_sum(x, axis):
    n = lax.axis_size(axis)
    if n & (n - 1):
        return lax.psum(x, axis)
    return axis_reduce(x, axis, jnp.add)


def axis_max(x, axes):
    if any(lax.axis_size(a) & (lax.axis_size(a) - 1) for a in axes):
        return jnp.max(lax.all_gather(x, axes), axis=0)
    for a in axes:
        x = axis_reduce(x, a, jnp.maximum)
    return x


def body(x_new, kv_pages, w_query, w_keyval, w_out, lengths, page_store, offsets):
    tensors = lax.axis_size("tensor")
    shards = lax.axis_size("store")
    tensor_idx = lax.axis_index("tensor")
    store_idx = lax.axis_index("store")
    tok_count = x_new.shape[0]
    assert tok_count == TURN and lengths.shape[0] == 1
    local_slots = kv_pages.shape[1]
    capacity = local_slots * tensors
    page_len = kv_pages.shape[2]
    kv_heads = kv_pages.shape[3] // (2 * HD)
    group_size = HQ // KVH
    local_heads = w_query.shape[1] // HD
    local_kv = max(1, local_heads // group_size)
    local_group = local_heads // local_kv
    freq_table = inverse_freq(HD)
    kv_first = tensor_idx * local_heads // group_size
    keyval_cols = lax.dynamic_slice_in_dim(w_keyval, kv_first * (2 * HD), local_kv * 2 * HD, 1)
    query_part = jnp.dot(x_new, w_query, preferred_element_type=jnp.float32)
    keyval_part = jnp.dot(x_new, keyval_cols, preferred_element_type=jnp.float32)
    width_q = query_part.shape[1]
    both = axis_sum(jnp.concatenate([query_part, keyval_part], axis=1), "store")
    query_sum, keyval_sum = both[:, :width_q], both[:, width_q:]
    keyval_local = keyval_sum.reshape(tok_count, local_kv, 2, HD)
    tok_ids = jnp.arange(tok_count, dtype=jnp.int32)
    tok_sess = tok_ids // TURN
    tok_pos = table_lookup(lengths, tok_sess) + tok_ids % TURN
    tok_angle = tok_pos.astype(jnp.float32)[:, None, None] * freq_table
    query_rot = to_half(rotate(query_sum.reshape(tok_count, local_heads, HD), tok_angle))
    key_new = to_half(rotate(keyval_local[:, :, 0], tok_angle))
    value_new = to_half(keyval_local[:, :, 1])

    first_slot = store_idx * capacity + tensor_idx * local_slots
    key_sess, key_ok, key_off = slot_meta(
        page_store, lengths, offsets, shards, capacity, first_slot, local_slots, page_len
    )
    pb = local_slots
    bias = jnp.where(key_ok, 0.0, MASK_FILL).astype(jnp.float32)
    bias = bias.reshape(local_slots // pb, 1, pb * page_len)
    hist_angle = offsets[0].astype(jnp.float32) * freq_table
    kv_local = kv_pages.reshape(local_slots, page_len, kv_pages.shape[3])
    cosine = jnp.cos(hist_angle)
    sine = jnp.sin(hist_angle)
    cos2 = jnp.concatenate([cosine, cosine])[None, :]
    sin2 = jnp.concatenate([-sine, sine])[None, :]

    q_heads = jnp.transpose(query_rot, (1, 0, 2))
    q_all = lax.all_gather(q_heads, "tensor", axis=0, tiled=True)
    q_k = q_all.reshape(kv_heads, group_size * tok_count, HD)
    if local_heads % group_size == 0:
        own = hist_attend(
            kv_first, q_heads.reshape(local_kv, group_size * tok_count, HD), kv_local, bias, cos2, sin2, pb
        )
        rest_first = kv_first + local_kv
        q_rest = lax.dynamic_slice_in_dim(
            jnp.concatenate([q_k, q_k], axis=0), rest_first % kv_heads, kv_heads - local_kv, 0
        )
        rest = hist_attend(rest_first % kv_heads, q_rest, kv_local, bias, cos2, sin2, pb)
        parts = []
        for first, second in zip(own, rest):
            rolled = jnp.concatenate([first, second, first, second], axis=0)
            parts.append(lax.dynamic_slice_in_dim(rolled, kv_heads - kv_first, kv_heads, 0))
        acc, top, total = parts
    else:
        acc, top, total = hist_attend(jnp.int32(0), q_k, kv_local, bias, cos2, sin2, pb)
    acc = acc.reshape(HQ, tok_count, HD)
    top = top.reshape(HQ, tok_count)
    total = total.reshape(HQ, tok_count)

    glob_top = axis_max(top, ("store", "tensor"))
    factor = jnp.exp(top - glob_top)
    packed = jnp.concatenate(
        [(acc * factor[..., None]).reshape(HQ, tok_count * HD), total * factor], axis=1
    )
    new_allowed = (tok_sess[:, None] == tok_sess[None, :]) & (tok_ids[None, :] <= tok_ids[:, None])
    chunk_heads = HQ // (tensors * shards)
    if (
        HQ % (tensors * shards) == 0
        and group_size % chunk_heads == 0
        and not shards & (shards - 1)
        and not tensors & (tensors - 1)
    ):
        width = packed.shape[1]
        s_bits = shards.bit_length() - 1
        t_bits = tensors.bit_length() - 1
        block = packed.reshape((2,) * t_bits + (2,) * s_bits + (chunk_heads, width))
        order = tuple(range(t_bits + s_bits - 1, t_bits - 1, -1)) + tuple(range(t_bits - 1, -1, -1))
        block = jnp.transpose(block, order + (t_bits + s_bits, t_bits + s_bits + 1))
        block = bit_scatter(block, "store")
        block = bit_scatter(block, "tensor")
        acc = block[:, : tok_count * HD].reshape(chunk_heads, tok_count, HD)
        total = block[:, tok_count * HD :]
        chunk_first = (tensor_idx * shards + store_idx) * chunk_heads
        loc_top = lax.dynamic_slice_in_dim(glob_top, chunk_first, chunk_heads, 0)
        hist_part = (jnp.transpose(loc_top), jnp.transpose(total), jnp.transpose(acc, (1, 0, 2)))
        in_group = store_idx * chunk_heads
        query_chunk = lax.dynamic_slice_in_dim(query_rot, in_group, chunk_heads, 1)
        kv_idx = in_group // group_size
        key_chunk = lax.dynamic_slice_in_dim(key_new, kv_idx, 1, 1)
        value_chunk = lax.dynamic_slice_in_dim(value_new, kv_idx, 1, 1)
        new_part = attend(
            query_chunk.reshape(tok_count, 1, chunk_heads, HD), key_chunk, value_chunk, new_allowed
        )
        new_flat = (
            new_part[0].reshape(tok_count, chunk_heads),
            new_part[1].reshape(tok_count, chunk_heads),
            new_part[2].reshape(tok_count, chunk_heads, HD),
        )
        combined = combine(hist_part, new_flat)
        attended = (
            (combined[2] / combined[1][..., None])
            .reshape(tok_count, chunk_heads * HD)
            .astype(jnp.bfloat16)
        )
        attended = lax.all_gather(attended, "store", axis=1, tiled=True)
    else:
        packed = lax.psum_scatter(packed, "tensor", scatter_dimension=0, tiled=True)
        packed = axis_sum(packed, "store")
        acc = packed[:, : tok_count * HD].reshape(local_heads, tok_count, HD)
        total = packed[:, tok_count * HD :]
        loc_top = lax.dynamic_slice_in_dim(glob_top, tensor_idx * local_heads, local_heads, 0)
        hist_part = (
            jnp.transpose(loc_top),
            jnp.transpose(total),
            jnp.transpose(acc, (1, 0, 2)),
        )

        query_local = query_rot.reshape(tok_count, local_kv, local_group, HD)
        new_part = attend(query_local, key_new, value_new, new_allowed)
        new_flat = (
            new_part[0].reshape(tok_count, local_heads),
            new_part[1].reshape(tok_count, local_heads),
            new_part[2].reshape(tok_count, local_heads, HD),
        )
        combined = combine(hist_part, new_flat)
        attended = (
            (combined[2] / combined[1][..., None])
            .reshape(tok_count, local_heads * HD)
            .astype(jnp.bfloat16)
        )
    result = lax.psum_scatter(
        jnp.dot(attended, w_out, preferred_element_type=jnp.float32),
        "tensor",
        scatter_dimension=0,
        tiled=True,
    )
    return result.astype(jnp.bfloat16)


def solution(mesh):
    in_specs = (
        P("groups", "store"),
        P(("groups", "store"), "tensor", None, None),
        P("store", "tensor"),
        P("store", None),
        P("tensor", "store"),
        P("groups"),
        P("groups", None),
        P("groups"),
    )
    out_specs = P(("groups", "tensor"), "store")
    return jax.shard_map(body, mesh=mesh, in_specs=in_specs, out_specs=out_specs, check_vma=False)
```

```python
import math

import jax
import jax.numpy as jnp
import numpy as np
from jax import lax
from jax.sharding import PartitionSpec as P
from jax.experimental import pallas as pl
from jax.experimental.pallas import tpu as pltpu
import functools

HQ = 64
KVH = 8
HD = 128
TURN = 64
MAXPAGES = 256


THETA = 500000.0
NEG_FILL = -1e30
ROPE_FACTOR = 8.0
LOW_FACTOR = 1.0
HIGH_FACTOR = 4.0
INITIAL_CONTEXT = 8192.0


def joined(x, axis, combine):
    everything = jax.tree.map(lambda part: lax.all_gather(part, axis), x)
    first = jax.tree.map(lambda part: part[0], everything)

    def step(k, so_far):
        return combine(so_far, jax.tree.map(lambda part: part[k], everything))

    return lax.fori_loop(1, lax.axis_size(axis), step, first)


def inverse_freq(width):
    steps_half = jnp.arange(width // 2, dtype=jnp.float32)
    base_freq = jnp.exp(-(steps_half * (2.0 / width)) * jnp.log(jnp.float32(THETA)))
    wavelength = 2.0 * math.pi / base_freq
    low_wave = INITIAL_CONTEXT / LOW_FACTOR
    high_wave = INITIAL_CONTEXT / HIGH_FACTOR
    smooth = (INITIAL_CONTEXT / wavelength - LOW_FACTOR) / (HIGH_FACTOR - LOW_FACTOR)
    blended = (1.0 - smooth) * base_freq / ROPE_FACTOR + smooth * base_freq
    scaled = jnp.where(wavelength > low_wave, base_freq / ROPE_FACTOR, blended)
    return jnp.where(wavelength < high_wave, base_freq, scaled)


def rotate(values, rot_angle):
    half_width = values.shape[-1] // 2
    first_half = values[..., :half_width]
    second_half = values[..., half_width:]
    cosine = jnp.cos(rot_angle)
    sine_part = jnp.sin(rot_angle)
    return jnp.concatenate(
        [
            first_half * cosine - second_half * sine_part,
            second_half * cosine + first_half * sine_part,
        ],
        axis=-1,
    )


def to_half(values):
    return values.astype(jnp.bfloat16)


def table_lookup(table, index):
    hits = index[..., None] == jnp.arange(table.shape[0], dtype=jnp.int32)
    return jnp.sum(jnp.where(hits, table, 0), axis=-1)


def page_positions(page_store, shards, capacity):
    store_of = page_store[:, 0]
    onehot = (store_of[:, None] == jnp.arange(shards, dtype=jnp.int32)[None, :]).astype(jnp.int32)
    ranks = jnp.sum((jnp.cumsum(onehot, axis=0) - onehot) * onehot, axis=1)
    return store_of * capacity + ranks


def slot_meta(page_store, lengths, offsets, shards, capacity, first_slot, slot_count, page_len):
    positions = page_positions(page_store, shards, capacity)
    wanted = first_slot + jnp.arange(slot_count, dtype=jnp.int32)
    matches = (positions[:, None] == wanted[None, :]).astype(jnp.int32)
    page_ids = jnp.sum(matches * jnp.arange(positions.shape[0], dtype=jnp.int32)[:, None], axis=0)
    filled = jnp.sum(matches, axis=0) > 0
    slot_sess = page_ids // MAXPAGES
    slot_page = page_ids % MAXPAGES
    key_pos = slot_page[:, None] * page_len + jnp.arange(page_len, dtype=jnp.int32)[None, :]
    key_ok = filled[:, None] & (key_pos < table_lookup(lengths, slot_sess)[:, None])
    key_sess = jnp.broadcast_to(slot_sess[:, None], (slot_count, page_len))
    key_off = jnp.broadcast_to(table_lookup(offsets, slot_sess)[:, None], (slot_count, page_len))
    return (key_sess.reshape(-1), key_ok.reshape(-1), key_off.reshape(-1))


def attend(query, key_rows, value_rows, allowed):
    score_scale = 1.0 / query.shape[-1] ** 0.5
    scores = (
        jnp.einsum("tkgd,nkd->tkgn", query, key_rows, preferred_element_type=jnp.float32)
        * score_scale
    )
    wide_mask = allowed[:, None, None, :]
    scores = jnp.where(wide_mask, scores, NEG_FILL)
    row_top = jnp.max(scores, axis=-1)
    weights = jnp.where(wide_mask, jnp.exp(scores - row_top[..., None]), 0.0)
    weight_sum = jnp.sum(weights, axis=-1)
    head_mix = jnp.einsum(
        "tkgn,nkd->tkgd",
        weights.astype(jnp.bfloat16),
        value_rows,
        preferred_element_type=jnp.float32,
    )
    return (row_top, weight_sum, head_mix)


def combine(first_part, second_part):
    new_top = jnp.maximum(first_part[0], second_part[0])
    first_factor = jnp.exp(first_part[0] - new_top)
    second_factor = jnp.exp(second_part[0] - new_top)
    summed = first_part[1] * first_factor + second_part[1] * second_factor
    mixed_sum = first_part[2] * first_factor[..., None] + second_part[2] * second_factor[..., None]
    return (new_top, summed, mixed_sum)


MASK_FILL = -3e30


def hist_kernel(kv0_ref, q_ref, k_ref, v_ref, bias_ref, cos_ref, sin_ref, acc_out, m_out, l_out, m_sc, l_sc, acc_sc, *, scale, blocks):
    j = pl.program_id(1)

    @pl.when(j == 0)
    def _():
        m_sc[...] = jnp.full(m_sc.shape, NEG_FILL, jnp.float32)
        l_sc[...] = jnp.zeros(l_sc.shape, jnp.float32)
        acc_sc[...] = jnp.zeros(acc_sc.shape, jnp.float32)

    pages, page_len, hd = k_ref.shape
    n = pages * page_len
    keys = k_ref[...].reshape(n, hd).astype(jnp.float32)
    vals = v_ref[...].reshape(n, hd)
    keys = (keys * cos_ref[...] + pltpu.roll(keys, hd // 2, 1) * sin_ref[...]).astype(jnp.bfloat16)
    scores = lax.dot_general(
        q_ref[0], keys, (((1,), (1,)), ((), ())), preferred_element_type=jnp.float32
    )
    scores = scores * scale + bias_ref[0]
    m_old = m_sc[...]
    m_new = jnp.maximum(m_old, jnp.max(scores, axis=1, keepdims=True))
    alpha = jnp.exp(m_old - m_new)
    weights = jnp.exp(scores - m_new)
    l_sc[...] = alpha * l_sc[...] + jnp.sum(weights, axis=1, keepdims=True)
    acc_sc[...] = alpha * acc_sc[...] + jnp.dot(
        weights.astype(jnp.bfloat16), vals, preferred_element_type=jnp.float32
    )
    m_sc[...] = m_new

    @pl.when(j == blocks - 1)
    def _():
        acc_out[0] = acc_sc[...]
        m_out[0] = m_sc[...]
        l_out[0] = l_sc[...]


def hist_attend(kv0, q_k, kv_local, bias, cos2, sin2, pb):
    heads, rows, hd = q_k.shape
    slots, page_len, width = kv_local.shape
    kv_heads = width // (2 * hd)
    blocks = slots // pb
    kernel = functools.partial(hist_kernel, scale=1.0 / hd ** 0.5, blocks=blocks)

    def head_of(h, kv0_ref):
        return (kv0_ref[0] + h) % kv_heads

    grid_spec = pltpu.PrefetchScalarGridSpec(
        num_scalar_prefetch=1,
        grid=(heads, blocks),
        in_specs=[
            pl.BlockSpec((1, rows, hd), lambda h, j, r: (h, 0, 0)),
            pl.BlockSpec((pb, page_len, hd), lambda h, j, r: (j, 0, 2 * head_of(h, r))),
            pl.BlockSpec((pb, page_len, hd), lambda h, j, r: (j, 0, 2 * head_of(h, r) + 1)),
            pl.BlockSpec((1, 1, pb * page_len), lambda h, j, r: (j, 0, 0)),
            pl.BlockSpec((1, hd), lambda h, j, r: (0, 0)),
            pl.BlockSpec((1, hd), lambda h, j, r: (0, 0)),
        ],
        out_specs=[
            pl.BlockSpec((1, rows, hd), lambda h, j, r: (h, 0, 0)),
            pl.BlockSpec((1, rows, 1), lambda h, j, r: (h, 0, 0)),
            pl.BlockSpec((1, rows, 1), lambda h, j, r: (h, 0, 0)),
        ],
        scratch_shapes=[
            pltpu.VMEM((rows, 1), jnp.float32),
            pltpu.VMEM((rows, 1), jnp.float32),
            pltpu.VMEM((rows, hd), jnp.float32),
        ],
    )
    return pl.pallas_call(
        kernel,
        grid_spec=grid_spec,
        out_shape=[
            jax.ShapeDtypeStruct((heads, rows, hd), jnp.float32),
            jax.ShapeDtypeStruct((heads, rows, 1), jnp.float32),
            jax.ShapeDtypeStruct((heads, rows, 1), jnp.float32),
        ],
        compiler_params=pltpu.CompilerParams(dimension_semantics=("arbitrary", "arbitrary")),
    )(jnp.reshape(kv0, (1,)).astype(jnp.int32), q_k, kv_local, kv_local, bias, cos2, sin2)


def axis_reduce(x, axis, op):
    n = lax.axis_size(axis)
    d = 1
    while d < n:
        x = op(x, lax.ppermute(x, axis, perm=[(i, i ^ d) for i in range(n)]))
        d *= 2
    return x


def bit_scatter(block, axis):
    n = lax.axis_size(axis)
    idx = lax.axis_index(axis)
    d = 1
    while d < n:
        bit = (idx // d) % 2
        keep = lax.dynamic_index_in_dim(block, bit, 0, keepdims=False)
        send = lax.dynamic_index_in_dim(block, 1 - bit, 0, keepdims=False)
        block = keep + lax.ppermute(send, axis, perm=[(i, i ^ d) for i in range(n)])
        d *= 2
    return block


def bit_gather(x, axis):
    n = lax.axis_size(axis)
    idx = lax.axis_index(axis)
    dists = []
    d = n // 2
    while d >= 1:
        other = lax.ppermute(x, axis, perm=[(i, i ^ d) for i in range(n)])
        low = (idx // d) % 2 == 0
        x = jnp.stack([jnp.where(low, x, other), jnp.where(low, other, x)])
        dists.insert(0, d)
        d //= 2
    k = len(dists)
    order = sorted(range(k), key=lambda j: -dists[j])
    x = jnp.transpose(x, tuple(order) + tuple(range(k, x.ndim)))
    return x.reshape((n * x.shape[k],) + x.shape[k + 1 :])


def scatter_rows(x, axis):
    n = lax.axis_size(axis)
    if n & (n - 1):
        return lax.psum_scatter(x, axis, scatter_dimension=0, tiled=True)
    bits = n.bit_length() - 1
    x = x.reshape((2,) * bits + (x.shape[0] // n,) + x.shape[1:])
    x = jnp.transpose(x, tuple(range(bits - 1, -1, -1)) + tuple(range(bits, x.ndim)))
    return bit_scatter(x, axis)


def axis_sum(x, axis):
    n = lax.axis_size(axis)
    if n & (n - 1):
        return lax.psum(x, axis)
    return axis_reduce(x, axis, jnp.add)


def axis_max(x, axes):
    if any(lax.axis_size(a) & (lax.axis_size(a) - 1) for a in axes):
        return jnp.max(lax.all_gather(x, axes), axis=0)
    for a in axes:
        x = axis_reduce(x, a, jnp.maximum)
    return x


def body(x_new, kv_pages, w_query, w_keyval, w_out, lengths, page_store, offsets):
    tensors = lax.axis_size("tensor")
    shards = lax.axis_size("store")
    tensor_idx = lax.axis_index("tensor")
    store_idx = lax.axis_index("store")
    tok_count = x_new.shape[0]
    assert tok_count == TURN and lengths.shape[0] == 1
    local_slots = kv_pages.shape[1]
    capacity = local_slots * tensors
    page_len = kv_pages.shape[2]
    kv_heads = kv_pages.shape[3] // (2 * HD)
    group_size = HQ // KVH
    local_heads = w_query.shape[1] // HD
    local_kv = max(1, local_heads // group_size)
    local_group = local_heads // local_kv
    freq_table = inverse_freq(HD)
    kv_first = tensor_idx * local_heads // group_size
    keyval_cols = lax.dynamic_slice_in_dim(w_keyval, kv_first * (2 * HD), local_kv * 2 * HD, 1)
    query_part = jnp.dot(x_new, w_query, preferred_element_type=jnp.float32)
    keyval_part = jnp.dot(x_new, keyval_cols, preferred_element_type=jnp.float32)
    width_q = query_part.shape[1]
    both = axis_sum(jnp.concatenate([query_part, keyval_part], axis=1), "store")
    query_sum, keyval_sum = both[:, :width_q], both[:, width_q:]
    keyval_local = keyval_sum.reshape(tok_count, local_kv, 2, HD)
    tok_ids = jnp.arange(tok_count, dtype=jnp.int32)
    tok_sess = tok_ids // TURN
    tok_pos = table_lookup(lengths, tok_sess) + tok_ids % TURN
    tok_angle = tok_pos.astype(jnp.float32)[:, None, None] * freq_table
    query_rot = to_half(rotate(query_sum.reshape(tok_count, local_heads, HD), tok_angle))
    key_new = to_half(rotate(keyval_local[:, :, 0], tok_angle))
    value_new = to_half(keyval_local[:, :, 1])

    first_slot = store_idx * capacity + tensor_idx * local_slots
    key_sess, key_ok, key_off = slot_meta(
        page_store, lengths, offsets, shards, capacity, first_slot, local_slots, page_len
    )
    pb = local_slots
    bias = jnp.where(key_ok, 0.0, MASK_FILL).astype(jnp.float32)
    bias = bias.reshape(local_slots // pb, 1, pb * page_len)
    hist_angle = offsets[0].astype(jnp.float32) * freq_table
    kv_local = kv_pages.reshape(local_slots, page_len, kv_pages.shape[3])
    cosine = jnp.cos(hist_angle)
    sine = jnp.sin(hist_angle)
    cos2 = jnp.concatenate([cosine, cosine])[None, :]
    sin2 = jnp.concatenate([-sine, sine])[None, :]

    q_heads = jnp.transpose(query_rot, (1, 0, 2))
    if tensors & (tensors - 1):
        q_all = lax.all_gather(q_heads, "tensor", axis=0, tiled=True)
    else:
        q_all = bit_gather(q_heads, "tensor")
    q_k = q_all.reshape(kv_heads, group_size * tok_count, HD)
    if local_heads % group_size == 0:
        own = hist_attend(
            kv_first, q_heads.reshape(local_kv, group_size * tok_count, HD), kv_local, bias, cos2, sin2, pb
        )
        rest_first = kv_first + local_kv
        q_rest = lax.dynamic_slice_in_dim(
            jnp.concatenate([q_k, q_k], axis=0), rest_first % kv_heads, kv_heads - local_kv, 0
        )
        rest = hist_attend(rest_first % kv_heads, q_rest, kv_local, bias, cos2, sin2, pb)
        parts = []
        for first, second in zip(own, rest):
            rolled = jnp.concatenate([first, second, first, second], axis=0)
            parts.append(lax.dynamic_slice_in_dim(rolled, kv_heads - kv_first, kv_heads, 0))
        acc, top, total = parts
    else:
        acc, top, total = hist_attend(jnp.int32(0), q_k, kv_local, bias, cos2, sin2, pb)
    acc = acc.reshape(HQ, tok_count, HD)
    top = top.reshape(HQ, tok_count)
    total = total.reshape(HQ, tok_count)

    glob_top = axis_max(top, ("store", "tensor"))
    factor = jnp.exp(top - glob_top)
    packed = jnp.concatenate(
        [(acc * factor[..., None]).reshape(HQ, tok_count * HD), total * factor], axis=1
    )
    new_allowed = (tok_sess[:, None] == tok_sess[None, :]) & (tok_ids[None, :] <= tok_ids[:, None])
    chunk_heads = HQ // (tensors * shards)
    if (
        HQ % (tensors * shards) == 0
        and group_size % chunk_heads == 0
        and not shards & (shards - 1)
        and not tensors & (tensors - 1)
    ):
        width = packed.shape[1]
        s_bits = shards.bit_length() - 1
        t_bits = tensors.bit_length() - 1
        block = packed.reshape((2,) * t_bits + (2,) * s_bits + (chunk_heads, width))
        order = tuple(range(t_bits + s_bits - 1, t_bits - 1, -1)) + tuple(range(t_bits - 1, -1, -1))
        block = jnp.transpose(block, order + (t_bits + s_bits, t_bits + s_bits + 1))
        block = bit_scatter(block, "store")
        block = bit_scatter(block, "tensor")
        acc = block[:, : tok_count * HD].reshape(chunk_heads, tok_count, HD)
        total = block[:, tok_count * HD :]
        chunk_first = (tensor_idx * shards + store_idx) * chunk_heads
        loc_top = lax.dynamic_slice_in_dim(glob_top, chunk_first, chunk_heads, 0)
        hist_part = (jnp.transpose(loc_top), jnp.transpose(total), jnp.transpose(acc, (1, 0, 2)))
        in_group = store_idx * chunk_heads
        query_chunk = lax.dynamic_slice_in_dim(query_rot, in_group, chunk_heads, 1)
        kv_idx = in_group // group_size
        key_chunk = lax.dynamic_slice_in_dim(key_new, kv_idx, 1, 1)
        value_chunk = lax.dynamic_slice_in_dim(value_new, kv_idx, 1, 1)
        new_part = attend(
            query_chunk.reshape(tok_count, 1, chunk_heads, HD), key_chunk, value_chunk, new_allowed
        )
        new_flat = (
            new_part[0].reshape(tok_count, chunk_heads),
            new_part[1].reshape(tok_count, chunk_heads),
            new_part[2].reshape(tok_count, chunk_heads, HD),
        )
        combined = combine(hist_part, new_flat)
        attended = (
            (combined[2] / combined[1][..., None])
            .reshape(tok_count, chunk_heads * HD)
            .astype(jnp.bfloat16)
        )
        attended = lax.all_gather(attended, "store", axis=1, tiled=True)
    else:
        packed = lax.psum_scatter(packed, "tensor", scatter_dimension=0, tiled=True)
        packed = axis_sum(packed, "store")
        acc = packed[:, : tok_count * HD].reshape(local_heads, tok_count, HD)
        total = packed[:, tok_count * HD :]
        loc_top = lax.dynamic_slice_in_dim(glob_top, tensor_idx * local_heads, local_heads, 0)
        hist_part = (
            jnp.transpose(loc_top),
            jnp.transpose(total),
            jnp.transpose(acc, (1, 0, 2)),
        )

        query_local = query_rot.reshape(tok_count, local_kv, local_group, HD)
        new_part = attend(query_local, key_new, value_new, new_allowed)
        new_flat = (
            new_part[0].reshape(tok_count, local_heads),
            new_part[1].reshape(tok_count, local_heads),
            new_part[2].reshape(tok_count, local_heads, HD),
        )
        combined = combine(hist_part, new_flat)
        attended = (
            (combined[2] / combined[1][..., None])
            .reshape(tok_count, local_heads * HD)
            .astype(jnp.bfloat16)
        )
    result = scatter_rows(jnp.dot(attended, w_out, preferred_element_type=jnp.float32), "tensor")
    return result.astype(jnp.bfloat16)


def solution(mesh):
    in_specs = (
        P("groups", "store"),
        P(("groups", "store"), "tensor", None, None),
        P("store", "tensor"),
        P("store", None),
        P("tensor", "store"),
        P("groups"),
        P("groups", None),
        P("groups"),
    )
    out_specs = P(("groups", "tensor"), "store")
    return jax.shard_map(body, mesh=mesh, in_specs=in_specs, out_specs=out_specs, check_vma=False)
```

```python
import math

import jax
import jax.numpy as jnp
import numpy as np
from jax import lax
from jax.sharding import PartitionSpec as P
from jax.experimental import pallas as pl
from jax.experimental.pallas import tpu as pltpu
import functools

HQ = 64
KVH = 8
HD = 128
TURN = 64
MAXPAGES = 256


THETA = 500000.0
NEG_FILL = -1e30
ROPE_FACTOR = 8.0
LOW_FACTOR = 1.0
HIGH_FACTOR = 4.0
INITIAL_CONTEXT = 8192.0


def joined(x, axis, combine):
    everything = jax.tree.map(lambda part: lax.all_gather(part, axis), x)
    first = jax.tree.map(lambda part: part[0], everything)

    def step(k, so_far):
        return combine(so_far, jax.tree.map(lambda part: part[k], everything))

    return lax.fori_loop(1, lax.axis_size(axis), step, first)


def inverse_freq(width):
    steps_half = jnp.arange(width // 2, dtype=jnp.float32)
    base_freq = jnp.exp(-(steps_half * (2.0 / width)) * jnp.log(jnp.float32(THETA)))
    wavelength = 2.0 * math.pi / base_freq
    low_wave = INITIAL_CONTEXT / LOW_FACTOR
    high_wave = INITIAL_CONTEXT / HIGH_FACTOR
    smooth = (INITIAL_CONTEXT / wavelength - LOW_FACTOR) / (HIGH_FACTOR - LOW_FACTOR)
    blended = (1.0 - smooth) * base_freq / ROPE_FACTOR + smooth * base_freq
    scaled = jnp.where(wavelength > low_wave, base_freq / ROPE_FACTOR, blended)
    return jnp.where(wavelength < high_wave, base_freq, scaled)


def rotate(values, rot_angle):
    half_width = values.shape[-1] // 2
    first_half = values[..., :half_width]
    second_half = values[..., half_width:]
    cosine = jnp.cos(rot_angle)
    sine_part = jnp.sin(rot_angle)
    return jnp.concatenate(
        [
            first_half * cosine - second_half * sine_part,
            second_half * cosine + first_half * sine_part,
        ],
        axis=-1,
    )


def to_half(values):
    return values.astype(jnp.bfloat16)


def table_lookup(table, index):
    hits = index[..., None] == jnp.arange(table.shape[0], dtype=jnp.int32)
    return jnp.sum(jnp.where(hits, table, 0), axis=-1)


def page_positions(page_store, shards, capacity):
    store_of = page_store[:, 0]
    onehot = (store_of[:, None] == jnp.arange(shards, dtype=jnp.int32)[None, :]).astype(jnp.int32)
    ranks = jnp.sum((jnp.cumsum(onehot, axis=0) - onehot) * onehot, axis=1)
    return store_of * capacity + ranks


def slot_meta(page_store, lengths, offsets, shards, capacity, first_slot, slot_count, page_len):
    positions = page_positions(page_store, shards, capacity)
    wanted = first_slot + jnp.arange(slot_count, dtype=jnp.int32)
    matches = (positions[:, None] == wanted[None, :]).astype(jnp.int32)
    page_ids = jnp.sum(matches * jnp.arange(positions.shape[0], dtype=jnp.int32)[:, None], axis=0)
    filled = jnp.sum(matches, axis=0) > 0
    slot_sess = page_ids // MAXPAGES
    slot_page = page_ids % MAXPAGES
    key_pos = slot_page[:, None] * page_len + jnp.arange(page_len, dtype=jnp.int32)[None, :]
    key_ok = filled[:, None] & (key_pos < table_lookup(lengths, slot_sess)[:, None])
    key_sess = jnp.broadcast_to(slot_sess[:, None], (slot_count, page_len))
    key_off = jnp.broadcast_to(table_lookup(offsets, slot_sess)[:, None], (slot_count, page_len))
    return (key_sess.reshape(-1), key_ok.reshape(-1), key_off.reshape(-1))


def attend(query, key_rows, value_rows, allowed):
    score_scale = 1.0 / query.shape[-1] ** 0.5
    scores = (
        jnp.einsum("tkgd,nkd->tkgn", query, key_rows, preferred_element_type=jnp.float32)
        * score_scale
    )
    wide_mask = allowed[:, None, None, :]
    scores = jnp.where(wide_mask, scores, NEG_FILL)
    row_top = jnp.max(scores, axis=-1)
    weights = jnp.where(wide_mask, jnp.exp(scores - row_top[..., None]), 0.0)
    weight_sum = jnp.sum(weights, axis=-1)
    head_mix = jnp.einsum(
        "tkgn,nkd->tkgd",
        weights.astype(jnp.bfloat16),
        value_rows,
        preferred_element_type=jnp.float32,
    )
    return (row_top, weight_sum, head_mix)


def combine(first_part, second_part):
    new_top = jnp.maximum(first_part[0], second_part[0])
    first_factor = jnp.exp(first_part[0] - new_top)
    second_factor = jnp.exp(second_part[0] - new_top)
    summed = first_part[1] * first_factor + second_part[1] * second_factor
    mixed_sum = first_part[2] * first_factor[..., None] + second_part[2] * second_factor[..., None]
    return (new_top, summed, mixed_sum)


MASK_FILL = -3e30


def hist_kernel(kv0_ref, q_ref, k_ref, v_ref, bias_ref, cos_ref, sin_ref, acc_out, m_out, l_out, m_sc, l_sc, acc_sc, *, scale, blocks):
    j = pl.program_id(1)

    @pl.when(j == 0)
    def _():
        m_sc[...] = jnp.full(m_sc.shape, NEG_FILL, jnp.float32)
        l_sc[...] = jnp.zeros(l_sc.shape, jnp.float32)
        acc_sc[...] = jnp.zeros(acc_sc.shape, jnp.float32)

    pages, page_len, hd = k_ref.shape
    n = pages * page_len
    keys = k_ref[...].reshape(n, hd).astype(jnp.float32)
    vals = v_ref[...].reshape(n, hd)
    keys = (keys * cos_ref[...] + pltpu.roll(keys, hd // 2, 1) * sin_ref[...]).astype(jnp.bfloat16)
    scores = lax.dot_general(
        q_ref[0], keys, (((1,), (1,)), ((), ())), preferred_element_type=jnp.float32
    )
    scores = scores * scale + bias_ref[0]
    m_old = m_sc[...]
    m_new = jnp.maximum(m_old, jnp.max(scores, axis=1, keepdims=True))
    alpha = jnp.exp(m_old - m_new)
    weights = jnp.exp(scores - m_new)
    l_sc[...] = alpha * l_sc[...] + jnp.sum(weights, axis=1, keepdims=True)
    acc_sc[...] = alpha * acc_sc[...] + jnp.dot(
        weights.astype(jnp.bfloat16), vals, preferred_element_type=jnp.float32
    )
    m_sc[...] = m_new

    @pl.when(j == blocks - 1)
    def _():
        acc_out[0] = acc_sc[...]
        m_out[0] = m_sc[...]
        l_out[0] = l_sc[...]


def hist_attend(kv0, q_k, kv_local, bias, cos2, sin2, pb):
    heads, rows, hd = q_k.shape
    slots, page_len, width = kv_local.shape
    kv_heads = width // (2 * hd)
    blocks = slots // pb
    kernel = functools.partial(hist_kernel, scale=1.0 / hd ** 0.5, blocks=blocks)

    def head_of(h, kv0_ref):
        return (kv0_ref[0] + h) % kv_heads

    grid_spec = pltpu.PrefetchScalarGridSpec(
        num_scalar_prefetch=1,
        grid=(heads, blocks),
        in_specs=[
            pl.BlockSpec((1, rows, hd), lambda h, j, r: (h, 0, 0)),
            pl.BlockSpec((pb, page_len, hd), lambda h, j, r: (j, 0, 2 * head_of(h, r))),
            pl.BlockSpec((pb, page_len, hd), lambda h, j, r: (j, 0, 2 * head_of(h, r) + 1)),
            pl.BlockSpec((1, 1, pb * page_len), lambda h, j, r: (j, 0, 0)),
            pl.BlockSpec((1, hd), lambda h, j, r: (0, 0)),
            pl.BlockSpec((1, hd), lambda h, j, r: (0, 0)),
        ],
        out_specs=[
            pl.BlockSpec((1, rows, hd), lambda h, j, r: (h, 0, 0)),
            pl.BlockSpec((1, rows, 1), lambda h, j, r: (h, 0, 0)),
            pl.BlockSpec((1, rows, 1), lambda h, j, r: (h, 0, 0)),
        ],
        scratch_shapes=[
            pltpu.VMEM((rows, 1), jnp.float32),
            pltpu.VMEM((rows, 1), jnp.float32),
            pltpu.VMEM((rows, hd), jnp.float32),
        ],
    )
    return pl.pallas_call(
        kernel,
        grid_spec=grid_spec,
        out_shape=[
            jax.ShapeDtypeStruct((heads, rows, hd), jnp.float32),
            jax.ShapeDtypeStruct((heads, rows, 1), jnp.float32),
            jax.ShapeDtypeStruct((heads, rows, 1), jnp.float32),
        ],
        compiler_params=pltpu.CompilerParams(dimension_semantics=("arbitrary", "arbitrary")),
        cost_estimate=pl.CostEstimate(
            flops=4 * heads * rows * slots * page_len * hd,
            transcendentals=heads * rows * slots * page_len,
            bytes_accessed=heads * (slots * page_len * 2 * hd * 2 + rows * hd * 6),
        ),
    )(jnp.reshape(kv0, (1,)).astype(jnp.int32), q_k, kv_local, kv_local, bias, cos2, sin2)


def axis_reduce(x, axis, op):
    n = lax.axis_size(axis)
    d = 1
    while d < n:
        x = op(x, lax.ppermute(x, axis, perm=[(i, i ^ d) for i in range(n)]))
        d *= 2
    return x


def bit_scatter(block, axis):
    n = lax.axis_size(axis)
    idx = lax.axis_index(axis)
    d = 1
    while d < n:
        bit = (idx // d) % 2
        keep = lax.dynamic_index_in_dim(block, bit, 0, keepdims=False)
        send = lax.dynamic_index_in_dim(block, 1 - bit, 0, keepdims=False)
        block = keep + lax.ppermute(send, axis, perm=[(i, i ^ d) for i in range(n)])
        d *= 2
    return block


def bit_gather(x, axis):
    n = lax.axis_size(axis)
    idx = lax.axis_index(axis)
    dists = []
    d = n // 2
    while d >= 1:
        other = lax.ppermute(x, axis, perm=[(i, i ^ d) for i in range(n)])
        low = (idx // d) % 2 == 0
        x = jnp.stack([jnp.where(low, x, other), jnp.where(low, other, x)])
        dists.insert(0, d)
        d //= 2
    k = len(dists)
    order = sorted(range(k), key=lambda j: -dists[j])
    x = jnp.transpose(x, tuple(order) + tuple(range(k, x.ndim)))
    return x.reshape((n * x.shape[k],) + x.shape[k + 1 :])


def scatter_rows(x, axis):
    n = lax.axis_size(axis)
    if n & (n - 1):
        return lax.psum_scatter(x, axis, scatter_dimension=0, tiled=True)
    bits = n.bit_length() - 1
    x = x.reshape((2,) * bits + (x.shape[0] // n,) + x.shape[1:])
    x = jnp.transpose(x, tuple(range(bits - 1, -1, -1)) + tuple(range(bits, x.ndim)))
    return bit_scatter(x, axis)


def axis_sum(x, axis):
    n = lax.axis_size(axis)
    if n & (n - 1):
        return lax.psum(x, axis)
    return axis_reduce(x, axis, jnp.add)


def axis_max(x, axes):
    if any(lax.axis_size(a) & (lax.axis_size(a) - 1) for a in axes):
        return jnp.max(lax.all_gather(x, axes), axis=0)
    for a in axes:
        x = axis_reduce(x, a, jnp.maximum)
    return x


def body(x_new, kv_pages, w_query, w_keyval, w_out, lengths, page_store, offsets):
    tensors = lax.axis_size("tensor")
    shards = lax.axis_size("store")
    tensor_idx = lax.axis_index("tensor")
    store_idx = lax.axis_index("store")
    tok_count = x_new.shape[0]
    assert tok_count == TURN and lengths.shape[0] == 1
    local_slots = kv_pages.shape[1]
    capacity = local_slots * tensors
    page_len = kv_pages.shape[2]
    kv_heads = kv_pages.shape[3] // (2 * HD)
    group_size = HQ // KVH
    local_heads = w_query.shape[1] // HD
    local_kv = max(1, local_heads // group_size)
    local_group = local_heads // local_kv
    freq_table = inverse_freq(HD)
    kv_first = tensor_idx * local_heads // group_size
    keyval_cols = lax.dynamic_slice_in_dim(w_keyval, kv_first * (2 * HD), local_kv * 2 * HD, 1)
    query_part = jnp.dot(x_new, w_query, preferred_element_type=jnp.float32)
    keyval_part = jnp.dot(x_new, keyval_cols, preferred_element_type=jnp.float32)
    width_q = query_part.shape[1]
    both = axis_sum(jnp.concatenate([query_part, keyval_part], axis=1), "store")
    query_sum, keyval_sum = both[:, :width_q], both[:, width_q:]
    keyval_local = keyval_sum.reshape(tok_count, local_kv, 2, HD)
    tok_ids = jnp.arange(tok_count, dtype=jnp.int32)
    tok_sess = tok_ids // TURN
    tok_pos = table_lookup(lengths, tok_sess) + tok_ids % TURN
    tok_angle = tok_pos.astype(jnp.float32)[:, None, None] * freq_table
    query_rot = to_half(rotate(query_sum.reshape(tok_count, local_heads, HD), tok_angle))
    key_new = to_half(rotate(keyval_local[:, :, 0], tok_angle))
    value_new = to_half(keyval_local[:, :, 1])

    first_slot = store_idx * capacity + tensor_idx * local_slots
    key_sess, key_ok, key_off = slot_meta(
        page_store, lengths, offsets, shards, capacity, first_slot, local_slots, page_len
    )
    pb = local_slots
    bias = jnp.where(key_ok, 0.0, MASK_FILL).astype(jnp.float32)
    bias = bias.reshape(local_slots // pb, 1, pb * page_len)
    hist_angle = offsets[0].astype(jnp.float32) * freq_table
    kv_local = kv_pages.reshape(local_slots, page_len, kv_pages.shape[3])
    cosine = jnp.cos(hist_angle)
    sine = jnp.sin(hist_angle)
    cos2 = jnp.concatenate([cosine, cosine])[None, :]
    sin2 = jnp.concatenate([-sine, sine])[None, :]

    q_heads = jnp.transpose(query_rot, (1, 0, 2))
    if tensors & (tensors - 1):
        q_all = lax.all_gather(q_heads, "tensor", axis=0, tiled=True)
    else:
        q_all = bit_gather(q_heads, "tensor")
    q_k = q_all.reshape(kv_heads, group_size * tok_count, HD)
    if local_heads % group_size == 0:
        own = hist_attend(
            kv_first, q_heads.reshape(local_kv, group_size * tok_count, HD), kv_local, bias, cos2, sin2, pb
        )
        rest_first = kv_first + local_kv
        q_rest = lax.dynamic_slice_in_dim(
            jnp.concatenate([q_k, q_k], axis=0), rest_first % kv_heads, kv_heads - local_kv, 0
        )
        rest = hist_attend(rest_first % kv_heads, q_rest, kv_local, bias, cos2, sin2, pb)
        parts = []
        for first, second in zip(own, rest):
            rolled = jnp.concatenate([first, second, first, second], axis=0)
            parts.append(lax.dynamic_slice_in_dim(rolled, kv_heads - kv_first, kv_heads, 0))
        acc, top, total = parts
    else:
        acc, top, total = hist_attend(jnp.int32(0), q_k, kv_local, bias, cos2, sin2, pb)
    acc = acc.reshape(HQ, tok_count, HD)
    top = top.reshape(HQ, tok_count)
    total = total.reshape(HQ, tok_count)

    glob_top = axis_max(top, ("store", "tensor"))
    factor = jnp.exp(top - glob_top)
    packed = jnp.concatenate(
        [(acc * factor[..., None]).reshape(HQ, tok_count * HD), total * factor], axis=1
    )
    new_allowed = (tok_sess[:, None] == tok_sess[None, :]) & (tok_ids[None, :] <= tok_ids[:, None])
    chunk_heads = HQ // (tensors * shards)
    if (
        HQ % (tensors * shards) == 0
        and group_size % chunk_heads == 0
        and not shards & (shards - 1)
        and not tensors & (tensors - 1)
    ):
        width = packed.shape[1]
        s_bits = shards.bit_length() - 1
        t_bits = tensors.bit_length() - 1
        block = packed.reshape((2,) * t_bits + (2,) * s_bits + (chunk_heads, width))
        order = tuple(range(t_bits + s_bits - 1, t_bits - 1, -1)) + tuple(range(t_bits - 1, -1, -1))
        block = jnp.transpose(block, order + (t_bits + s_bits, t_bits + s_bits + 1))
        block = bit_scatter(block, "store")
        block = bit_scatter(block, "tensor")
        acc = block[:, : tok_count * HD].reshape(chunk_heads, tok_count, HD)
        total = block[:, tok_count * HD :]
        chunk_first = (tensor_idx * shards + store_idx) * chunk_heads
        loc_top = lax.dynamic_slice_in_dim(glob_top, chunk_first, chunk_heads, 0)
        hist_part = (jnp.transpose(loc_top), jnp.transpose(total), jnp.transpose(acc, (1, 0, 2)))
        in_group = store_idx * chunk_heads
        query_chunk = lax.dynamic_slice_in_dim(query_rot, in_group, chunk_heads, 1)
        kv_idx = in_group // group_size
        key_chunk = lax.dynamic_slice_in_dim(key_new, kv_idx, 1, 1)
        value_chunk = lax.dynamic_slice_in_dim(value_new, kv_idx, 1, 1)
        new_part = attend(
            query_chunk.reshape(tok_count, 1, chunk_heads, HD), key_chunk, value_chunk, new_allowed
        )
        new_flat = (
            new_part[0].reshape(tok_count, chunk_heads),
            new_part[1].reshape(tok_count, chunk_heads),
            new_part[2].reshape(tok_count, chunk_heads, HD),
        )
        combined = combine(hist_part, new_flat)
        attended = (
            (combined[2] / combined[1][..., None])
            .reshape(tok_count, chunk_heads * HD)
            .astype(jnp.bfloat16)
        )
        attended = lax.all_gather(attended, "store", axis=1, tiled=True)
    else:
        packed = lax.psum_scatter(packed, "tensor", scatter_dimension=0, tiled=True)
        packed = axis_sum(packed, "store")
        acc = packed[:, : tok_count * HD].reshape(local_heads, tok_count, HD)
        total = packed[:, tok_count * HD :]
        loc_top = lax.dynamic_slice_in_dim(glob_top, tensor_idx * local_heads, local_heads, 0)
        hist_part = (
            jnp.transpose(loc_top),
            jnp.transpose(total),
            jnp.transpose(acc, (1, 0, 2)),
        )

        query_local = query_rot.reshape(tok_count, local_kv, local_group, HD)
        new_part = attend(query_local, key_new, value_new, new_allowed)
        new_flat = (
            new_part[0].reshape(tok_count, local_heads),
            new_part[1].reshape(tok_count, local_heads),
            new_part[2].reshape(tok_count, local_heads, HD),
        )
        combined = combine(hist_part, new_flat)
        attended = (
            (combined[2] / combined[1][..., None])
            .reshape(tok_count, local_heads * HD)
            .astype(jnp.bfloat16)
        )
    result = scatter_rows(jnp.dot(attended, w_out, preferred_element_type=jnp.float32), "tensor")
    return result.astype(jnp.bfloat16)


def solution(mesh):
    in_specs = (
        P("groups", "store"),
        P(("groups", "store"), "tensor", None, None),
        P("store", "tensor"),
        P("store", None),
        P("tensor", "store"),
        P("groups"),
        P("groups", None),
        P("groups"),
    )
    out_specs = P(("groups", "tensor"), "store")
    return jax.shard_map(body, mesh=mesh, in_specs=in_specs, out_specs=out_specs, check_vma=False)
```

```python
import math

import jax
import jax.numpy as jnp
import numpy as np
from jax import lax
from jax.sharding import PartitionSpec as P
from jax.experimental import pallas as pl
from jax.experimental.pallas import tpu as pltpu
import functools

HQ = 64
KVH = 8
HD = 128
TURN = 64
MAXPAGES = 256


THETA = 500000.0
NEG_FILL = -1e30
ROPE_FACTOR = 8.0
LOW_FACTOR = 1.0
HIGH_FACTOR = 4.0
INITIAL_CONTEXT = 8192.0


def joined(x, axis, combine):
    everything = jax.tree.map(lambda part: lax.all_gather(part, axis), x)
    first = jax.tree.map(lambda part: part[0], everything)

    def step(k, so_far):
        return combine(so_far, jax.tree.map(lambda part: part[k], everything))

    return lax.fori_loop(1, lax.axis_size(axis), step, first)


def inverse_freq(width):
    steps_half = jnp.arange(width // 2, dtype=jnp.float32)
    base_freq = jnp.exp(-(steps_half * (2.0 / width)) * jnp.log(jnp.float32(THETA)))
    wavelength = 2.0 * math.pi / base_freq
    low_wave = INITIAL_CONTEXT / LOW_FACTOR
    high_wave = INITIAL_CONTEXT / HIGH_FACTOR
    smooth = (INITIAL_CONTEXT / wavelength - LOW_FACTOR) / (HIGH_FACTOR - LOW_FACTOR)
    blended = (1.0 - smooth) * base_freq / ROPE_FACTOR + smooth * base_freq
    scaled = jnp.where(wavelength > low_wave, base_freq / ROPE_FACTOR, blended)
    return jnp.where(wavelength < high_wave, base_freq, scaled)


def rotate(values, rot_angle):
    half_width = values.shape[-1] // 2
    first_half = values[..., :half_width]
    second_half = values[..., half_width:]
    cosine = jnp.cos(rot_angle)
    sine_part = jnp.sin(rot_angle)
    return jnp.concatenate(
        [
            first_half * cosine - second_half * sine_part,
            second_half * cosine + first_half * sine_part,
        ],
        axis=-1,
    )


def to_half(values):
    return values.astype(jnp.bfloat16)


def table_lookup(table, index):
    hits = index[..., None] == jnp.arange(table.shape[0], dtype=jnp.int32)
    return jnp.sum(jnp.where(hits, table, 0), axis=-1)


def page_positions(page_store, shards, capacity):
    store_of = page_store[:, 0]
    onehot = (store_of[:, None] == jnp.arange(shards, dtype=jnp.int32)[None, :]).astype(jnp.int32)
    ranks = jnp.sum((jnp.cumsum(onehot, axis=0) - onehot) * onehot, axis=1)
    return store_of * capacity + ranks


def slot_meta(page_store, lengths, offsets, shards, capacity, first_slot, slot_count, page_len):
    positions = page_positions(page_store, shards, capacity)
    wanted = first_slot + jnp.arange(slot_count, dtype=jnp.int32)
    matches = (positions[:, None] == wanted[None, :]).astype(jnp.int32)
    page_ids = jnp.sum(matches * jnp.arange(positions.shape[0], dtype=jnp.int32)[:, None], axis=0)
    filled = jnp.sum(matches, axis=0) > 0
    slot_sess = page_ids // MAXPAGES
    slot_page = page_ids % MAXPAGES
    key_pos = slot_page[:, None] * page_len + jnp.arange(page_len, dtype=jnp.int32)[None, :]
    key_ok = filled[:, None] & (key_pos < table_lookup(lengths, slot_sess)[:, None])
    key_sess = jnp.broadcast_to(slot_sess[:, None], (slot_count, page_len))
    key_off = jnp.broadcast_to(table_lookup(offsets, slot_sess)[:, None], (slot_count, page_len))
    return (key_sess.reshape(-1), key_ok.reshape(-1), key_off.reshape(-1))


def attend(query, key_rows, value_rows, allowed):
    score_scale = 1.0 / query.shape[-1] ** 0.5
    scores = (
        jnp.einsum("tkgd,nkd->tkgn", query, key_rows, preferred_element_type=jnp.float32)
        * score_scale
    )
    wide_mask = allowed[:, None, None, :]
    scores = jnp.where(wide_mask, scores, NEG_FILL)
    row_top = jnp.max(scores, axis=-1)
    weights = jnp.where(wide_mask, jnp.exp(scores - row_top[..., None]), 0.0)
    weight_sum = jnp.sum(weights, axis=-1)
    head_mix = jnp.einsum(
        "tkgn,nkd->tkgd",
        weights.astype(jnp.bfloat16),
        value_rows,
        preferred_element_type=jnp.float32,
    )
    return (row_top, weight_sum, head_mix)


def combine(first_part, second_part):
    new_top = jnp.maximum(first_part[0], second_part[0])
    first_factor = jnp.exp(first_part[0] - new_top)
    second_factor = jnp.exp(second_part[0] - new_top)
    summed = first_part[1] * first_factor + second_part[1] * second_factor
    mixed_sum = first_part[2] * first_factor[..., None] + second_part[2] * second_factor[..., None]
    return (new_top, summed, mixed_sum)


MASK_FILL = -3e30


def hist_kernel(kv0_ref, q_ref, k_ref, v_ref, bias_ref, cos_ref, sin_ref, *refs, scale, blocks):
    acc_out, m_out, l_out, m_sc, l_sc, acc_sc = refs[-6:]
    j = pl.program_id(1)

    @pl.when(j == 0)
    def _():
        m_sc[...] = jnp.full(m_sc.shape, NEG_FILL, jnp.float32)
        l_sc[...] = jnp.zeros(l_sc.shape, jnp.float32)
        acc_sc[...] = jnp.zeros(acc_sc.shape, jnp.float32)

    pages, page_len, hd = k_ref.shape
    n = pages * page_len
    keys = k_ref[...].reshape(n, hd).astype(jnp.float32)
    vals = v_ref[...].reshape(n, hd)
    keys = (keys * cos_ref[...] + pltpu.roll(keys, hd // 2, 1) * sin_ref[...]).astype(jnp.bfloat16)
    scores = lax.dot_general(
        q_ref[0], keys, (((1,), (1,)), ((), ())), preferred_element_type=jnp.float32
    )
    scores = scores * scale + bias_ref[0]
    m_old = m_sc[...]
    m_new = jnp.maximum(m_old, jnp.max(scores, axis=1, keepdims=True))
    alpha = jnp.exp(m_old - m_new)
    weights = jnp.exp(scores - m_new)
    l_sc[...] = alpha * l_sc[...] + jnp.sum(weights, axis=1, keepdims=True)
    acc_sc[...] = alpha * acc_sc[...] + jnp.dot(
        weights.astype(jnp.bfloat16), vals, preferred_element_type=jnp.float32
    )
    m_sc[...] = m_new

    @pl.when(j == blocks - 1)
    def _():
        acc_out[0] = acc_sc[...]
        m_out[0] = m_sc[...]
        l_out[0] = l_sc[...]


def hist_attend(kv0, q_k, kv_local, bias, cos2, sin2, pb, prev=None):
    heads, rows, hd = q_k.shape
    slots, page_len, width = kv_local.shape
    kv_heads = width // (2 * hd)
    blocks = slots // pb
    kernel = functools.partial(hist_kernel, scale=1.0 / hd ** 0.5, blocks=blocks)

    def head_of(h, kv0_ref):
        return (kv0_ref[0] + h) % kv_heads

    grid_spec = pltpu.PrefetchScalarGridSpec(
        num_scalar_prefetch=1,
        grid=(heads, blocks),
        in_specs=[
            pl.BlockSpec((1, rows, hd), lambda h, j, r: (h, 0, 0)),
            pl.BlockSpec((pb, page_len, hd), lambda h, j, r: (j, 0, 2 * head_of(h, r))),
            pl.BlockSpec((pb, page_len, hd), lambda h, j, r: (j, 0, 2 * head_of(h, r) + 1)),
            pl.BlockSpec((1, 1, pb * page_len), lambda h, j, r: (j, 0, 0)),
            pl.BlockSpec((1, hd), lambda h, j, r: (0, 0)),
            pl.BlockSpec((1, hd), lambda h, j, r: (0, 0)),
        ]
        + ([pl.BlockSpec(memory_space=pl.ANY)] * 3 if prev is not None else []),
        out_specs=[
            pl.BlockSpec((1, rows, hd), lambda h, j, r: (head_of(h, r), 0, 0)),
            pl.BlockSpec((1, rows, 1), lambda h, j, r: (head_of(h, r), 0, 0)),
            pl.BlockSpec((1, rows, 1), lambda h, j, r: (head_of(h, r), 0, 0)),
        ],
        scratch_shapes=[
            pltpu.VMEM((rows, 1), jnp.float32),
            pltpu.VMEM((rows, 1), jnp.float32),
            pltpu.VMEM((rows, hd), jnp.float32),
        ],
    )
    return pl.pallas_call(
        kernel,
        grid_spec=grid_spec,
        out_shape=[
            jax.ShapeDtypeStruct((kv_heads, rows, hd), jnp.float32),
            jax.ShapeDtypeStruct((kv_heads, rows, 1), jnp.float32),
            jax.ShapeDtypeStruct((kv_heads, rows, 1), jnp.float32),
        ],
        input_output_aliases={7: 0, 8: 1, 9: 2} if prev is not None else {},
        compiler_params=pltpu.CompilerParams(dimension_semantics=("arbitrary", "arbitrary")),
        cost_estimate=pl.CostEstimate(
            flops=4 * heads * rows * slots * page_len * hd,
            transcendentals=heads * rows * slots * page_len,
            bytes_accessed=heads * (slots * page_len * 2 * hd * 2 + rows * hd * 6),
        ),
    )(jnp.reshape(kv0, (1,)).astype(jnp.int32), q_k, kv_local, kv_local, bias, cos2, sin2, *(prev or ()))


def axis_reduce(x, axis, op):
    n = lax.axis_size(axis)
    d = 1
    while d < n:
        x = op(x, lax.ppermute(x, axis, perm=[(i, i ^ d) for i in range(n)]))
        d *= 2
    return x


def bit_scatter(block, axis):
    n = lax.axis_size(axis)
    idx = lax.axis_index(axis)
    d = 1
    while d < n:
        bit = (idx // d) % 2
        keep = lax.dynamic_index_in_dim(block, bit, 0, keepdims=False)
        send = lax.dynamic_index_in_dim(block, 1 - bit, 0, keepdims=False)
        block = keep + lax.ppermute(send, axis, perm=[(i, i ^ d) for i in range(n)])
        d *= 2
    return block


def bit_gather(x, axis):
    n = lax.axis_size(axis)
    idx = lax.axis_index(axis)
    dists = []
    d = n // 2
    while d >= 1:
        other = lax.ppermute(x, axis, perm=[(i, i ^ d) for i in range(n)])
        low = (idx // d) % 2 == 0
        x = jnp.stack([jnp.where(low, x, other), jnp.where(low, other, x)])
        dists.insert(0, d)
        d //= 2
    k = len(dists)
    order = sorted(range(k), key=lambda j: -dists[j])
    x = jnp.transpose(x, tuple(order) + tuple(range(k, x.ndim)))
    return x.reshape((n * x.shape[k],) + x.shape[k + 1 :])


def scatter_rows(x, axis):
    n = lax.axis_size(axis)
    if n & (n - 1):
        return lax.psum_scatter(x, axis, scatter_dimension=0, tiled=True)
    bits = n.bit_length() - 1
    x = x.reshape((2,) * bits + (x.shape[0] // n,) + x.shape[1:])
    x = jnp.transpose(x, tuple(range(bits - 1, -1, -1)) + tuple(range(bits, x.ndim)))
    return bit_scatter(x, axis)


def axis_sum(x, axis):
    n = lax.axis_size(axis)
    if n & (n - 1):
        return lax.psum(x, axis)
    return axis_reduce(x, axis, jnp.add)


def axis_max(x, axes):
    if any(lax.axis_size(a) & (lax.axis_size(a) - 1) for a in axes):
        return jnp.max(lax.all_gather(x, axes), axis=0)
    for a in axes:
        x = axis_reduce(x, a, jnp.maximum)
    return x


def body(x_new, kv_pages, w_query, w_keyval, w_out, lengths, page_store, offsets):
    tensors = lax.axis_size("tensor")
    shards = lax.axis_size("store")
    tensor_idx = lax.axis_index("tensor")
    store_idx = lax.axis_index("store")
    tok_count = x_new.shape[0]
    assert tok_count == TURN and lengths.shape[0] == 1
    local_slots = kv_pages.shape[1]
    capacity = local_slots * tensors
    page_len = kv_pages.shape[2]
    kv_heads = kv_pages.shape[3] // (2 * HD)
    group_size = HQ // KVH
    local_heads = w_query.shape[1] // HD
    local_kv = max(1, local_heads // group_size)
    local_group = local_heads // local_kv
    freq_table = inverse_freq(HD)
    kv_first = tensor_idx * local_heads // group_size
    keyval_cols = lax.dynamic_slice_in_dim(w_keyval, kv_first * (2 * HD), local_kv * 2 * HD, 1)
    query_part = jnp.dot(x_new, w_query, preferred_element_type=jnp.float32)
    keyval_part = jnp.dot(x_new, keyval_cols, preferred_element_type=jnp.float32)
    width_q = query_part.shape[1]
    both = axis_sum(jnp.concatenate([query_part, keyval_part], axis=1), "store")
    query_sum, keyval_sum = both[:, :width_q], both[:, width_q:]
    keyval_local = keyval_sum.reshape(tok_count, local_kv, 2, HD)
    tok_ids = jnp.arange(tok_count, dtype=jnp.int32)
    tok_sess = tok_ids // TURN
    tok_pos = table_lookup(lengths, tok_sess) + tok_ids % TURN
    tok_angle = tok_pos.astype(jnp.float32)[:, None, None] * freq_table
    query_rot = to_half(rotate(query_sum.reshape(tok_count, local_heads, HD), tok_angle))
    key_new = to_half(rotate(keyval_local[:, :, 0], tok_angle))
    value_new = to_half(keyval_local[:, :, 1])

    first_slot = store_idx * capacity + tensor_idx * local_slots
    key_sess, key_ok, key_off = slot_meta(
        page_store, lengths, offsets, shards, capacity, first_slot, local_slots, page_len
    )
    pb = local_slots
    bias = jnp.where(key_ok, 0.0, MASK_FILL).astype(jnp.float32)
    bias = bias.reshape(local_slots // pb, 1, pb * page_len)
    hist_angle = offsets[0].astype(jnp.float32) * freq_table
    kv_local = kv_pages.reshape(local_slots, page_len, kv_pages.shape[3])
    cosine = jnp.cos(hist_angle)
    sine = jnp.sin(hist_angle)
    cos2 = jnp.concatenate([cosine, cosine])[None, :]
    sin2 = jnp.concatenate([-sine, sine])[None, :]

    q_heads = jnp.transpose(query_rot, (1, 0, 2))
    if tensors & (tensors - 1):
        q_all = lax.all_gather(q_heads, "tensor", axis=0, tiled=True)
    else:
        q_all = bit_gather(q_heads, "tensor")
    q_k = q_all.reshape(kv_heads, group_size * tok_count, HD)
    if local_heads % group_size == 0:
        own = hist_attend(
            kv_first, q_heads.reshape(local_kv, group_size * tok_count, HD), kv_local, bias, cos2, sin2, pb
        )
        rest_first = kv_first + local_kv
        q_rest = lax.dynamic_slice_in_dim(
            jnp.concatenate([q_k, q_k], axis=0), rest_first % kv_heads, kv_heads - local_kv, 0
        )
        acc, top, total = hist_attend(
            rest_first % kv_heads, q_rest, kv_local, bias, cos2, sin2, pb, prev=tuple(own)
        )
    else:
        acc, top, total = hist_attend(jnp.int32(0), q_k, kv_local, bias, cos2, sin2, pb)
    acc = acc.reshape(HQ, tok_count, HD)
    top = top.reshape(HQ, tok_count)
    total = total.reshape(HQ, tok_count)

    glob_top = axis_max(top, ("store", "tensor"))
    factor = jnp.exp(top - glob_top)
    packed = jnp.concatenate(
        [(acc * factor[..., None]).reshape(HQ, tok_count * HD), total * factor], axis=1
    )
    new_allowed = (tok_sess[:, None] == tok_sess[None, :]) & (tok_ids[None, :] <= tok_ids[:, None])
    chunk_heads = HQ // (tensors * shards)
    if (
        HQ % (tensors * shards) == 0
        and group_size % chunk_heads == 0
        and not shards & (shards - 1)
        and not tensors & (tensors - 1)
    ):
        width = packed.shape[1]
        s_bits = shards.bit_length() - 1
        t_bits = tensors.bit_length() - 1
        block = packed.reshape((2,) * t_bits + (2,) * s_bits + (chunk_heads, width))
        order = tuple(range(t_bits + s_bits - 1, t_bits - 1, -1)) + tuple(range(t_bits - 1, -1, -1))
        block = jnp.transpose(block, order + (t_bits + s_bits, t_bits + s_bits + 1))
        block = bit_scatter(block, "store")
        block = bit_scatter(block, "tensor")
        acc = block[:, : tok_count * HD].reshape(chunk_heads, tok_count, HD)
        total = block[:, tok_count * HD :]
        chunk_first = (tensor_idx * shards + store_idx) * chunk_heads
        loc_top = lax.dynamic_slice_in_dim(glob_top, chunk_first, chunk_heads, 0)
        hist_part = (jnp.transpose(loc_top), jnp.transpose(total), jnp.transpose(acc, (1, 0, 2)))
        in_group = store_idx * chunk_heads
        query_chunk = lax.dynamic_slice_in_dim(query_rot, in_group, chunk_heads, 1)
        kv_idx = in_group // group_size
        key_chunk = lax.dynamic_slice_in_dim(key_new, kv_idx, 1, 1)
        value_chunk = lax.dynamic_slice_in_dim(value_new, kv_idx, 1, 1)
        new_part = attend(
            query_chunk.reshape(tok_count, 1, chunk_heads, HD), key_chunk, value_chunk, new_allowed
        )
        new_flat = (
            new_part[0].reshape(tok_count, chunk_heads),
            new_part[1].reshape(tok_count, chunk_heads),
            new_part[2].reshape(tok_count, chunk_heads, HD),
        )
        combined = combine(hist_part, new_flat)
        attended = (
            (combined[2] / combined[1][..., None])
            .reshape(tok_count, chunk_heads * HD)
            .astype(jnp.bfloat16)
        )
        attended = lax.all_gather(attended, "store", axis=1, tiled=True)
    else:
        packed = lax.psum_scatter(packed, "tensor", scatter_dimension=0, tiled=True)
        packed = axis_sum(packed, "store")
        acc = packed[:, : tok_count * HD].reshape(local_heads, tok_count, HD)
        total = packed[:, tok_count * HD :]
        loc_top = lax.dynamic_slice_in_dim(glob_top, tensor_idx * local_heads, local_heads, 0)
        hist_part = (
            jnp.transpose(loc_top),
            jnp.transpose(total),
            jnp.transpose(acc, (1, 0, 2)),
        )

        query_local = query_rot.reshape(tok_count, local_kv, local_group, HD)
        new_part = attend(query_local, key_new, value_new, new_allowed)
        new_flat = (
            new_part[0].reshape(tok_count, local_heads),
            new_part[1].reshape(tok_count, local_heads),
            new_part[2].reshape(tok_count, local_heads, HD),
        )
        combined = combine(hist_part, new_flat)
        attended = (
            (combined[2] / combined[1][..., None])
            .reshape(tok_count, local_heads * HD)
            .astype(jnp.bfloat16)
        )
    result = scatter_rows(jnp.dot(attended, w_out, preferred_element_type=jnp.float32), "tensor")
    return result.astype(jnp.bfloat16)


def solution(mesh):
    in_specs = (
        P("groups", "store"),
        P(("groups", "store"), "tensor", None, None),
        P("store", "tensor"),
        P("store", None),
        P("tensor", "store"),
        P("groups"),
        P("groups", None),
        P("groups"),
    )
    out_specs = P(("groups", "tensor"), "store")
    return jax.shard_map(body, mesh=mesh, in_specs=in_specs, out_specs=out_specs, check_vma=False)
```

```python
import math

import jax
import jax.numpy as jnp
import numpy as np
from jax import lax
from jax.sharding import PartitionSpec as P
from jax.experimental import pallas as pl
from jax.experimental.pallas import tpu as pltpu
import functools

HQ = 64
KVH = 8
HD = 128
TURN = 64
MAXPAGES = 256


THETA = 500000.0
NEG_FILL = -1e30
ROPE_FACTOR = 8.0
LOW_FACTOR = 1.0
HIGH_FACTOR = 4.0
INITIAL_CONTEXT = 8192.0


def joined(x, axis, combine):
    everything = jax.tree.map(lambda part: lax.all_gather(part, axis), x)
    first = jax.tree.map(lambda part: part[0], everything)

    def step(k, so_far):
        return combine(so_far, jax.tree.map(lambda part: part[k], everything))

    return lax.fori_loop(1, lax.axis_size(axis), step, first)


def inverse_freq(width):
    steps_half = jnp.arange(width // 2, dtype=jnp.float32)
    base_freq = jnp.exp(-(steps_half * (2.0 / width)) * jnp.log(jnp.float32(THETA)))
    wavelength = 2.0 * math.pi / base_freq
    low_wave = INITIAL_CONTEXT / LOW_FACTOR
    high_wave = INITIAL_CONTEXT / HIGH_FACTOR
    smooth = (INITIAL_CONTEXT / wavelength - LOW_FACTOR) / (HIGH_FACTOR - LOW_FACTOR)
    blended = (1.0 - smooth) * base_freq / ROPE_FACTOR + smooth * base_freq
    scaled = jnp.where(wavelength > low_wave, base_freq / ROPE_FACTOR, blended)
    return jnp.where(wavelength < high_wave, base_freq, scaled)


def rotate(values, rot_angle):
    half_width = values.shape[-1] // 2
    first_half = values[..., :half_width]
    second_half = values[..., half_width:]
    cosine = jnp.cos(rot_angle)
    sine_part = jnp.sin(rot_angle)
    return jnp.concatenate(
        [
            first_half * cosine - second_half * sine_part,
            second_half * cosine + first_half * sine_part,
        ],
        axis=-1,
    )


def to_half(values):
    return values.astype(jnp.bfloat16)


def table_lookup(table, index):
    hits = index[..., None] == jnp.arange(table.shape[0], dtype=jnp.int32)
    return jnp.sum(jnp.where(hits, table, 0), axis=-1)


def page_positions(page_store, shards, capacity):
    store_of = page_store[:, 0]
    onehot = (store_of[:, None] == jnp.arange(shards, dtype=jnp.int32)[None, :]).astype(jnp.int32)
    ranks = jnp.sum((jnp.cumsum(onehot, axis=0) - onehot) * onehot, axis=1)
    return store_of * capacity + ranks


def slot_meta(page_store, lengths, offsets, shards, capacity, first_slot, slot_count, page_len):
    positions = page_positions(page_store, shards, capacity)
    wanted = first_slot + jnp.arange(slot_count, dtype=jnp.int32)
    matches = (positions[:, None] == wanted[None, :]).astype(jnp.int32)
    page_ids = jnp.sum(matches * jnp.arange(positions.shape[0], dtype=jnp.int32)[:, None], axis=0)
    filled = jnp.sum(matches, axis=0) > 0
    slot_sess = page_ids // MAXPAGES
    slot_page = page_ids % MAXPAGES
    key_pos = slot_page[:, None] * page_len + jnp.arange(page_len, dtype=jnp.int32)[None, :]
    key_ok = filled[:, None] & (key_pos < table_lookup(lengths, slot_sess)[:, None])
    key_sess = jnp.broadcast_to(slot_sess[:, None], (slot_count, page_len))
    key_off = jnp.broadcast_to(table_lookup(offsets, slot_sess)[:, None], (slot_count, page_len))
    return (key_sess.reshape(-1), key_ok.reshape(-1), key_off.reshape(-1))


def attend(query, key_rows, value_rows, allowed):
    score_scale = 1.0 / query.shape[-1] ** 0.5
    scores = (
        jnp.einsum("tkgd,nkd->tkgn", query, key_rows, preferred_element_type=jnp.float32)
        * score_scale
    )
    wide_mask = allowed[:, None, None, :]
    scores = jnp.where(wide_mask, scores, NEG_FILL)
    row_top = jnp.max(scores, axis=-1)
    weights = jnp.where(wide_mask, jnp.exp(scores - row_top[..., None]), 0.0)
    weight_sum = jnp.sum(weights, axis=-1)
    head_mix = jnp.einsum(
        "tkgn,nkd->tkgd",
        weights.astype(jnp.bfloat16),
        value_rows,
        preferred_element_type=jnp.float32,
    )
    return (row_top, weight_sum, head_mix)


def combine(first_part, second_part):
    new_top = jnp.maximum(first_part[0], second_part[0])
    first_factor = jnp.exp(first_part[0] - new_top)
    second_factor = jnp.exp(second_part[0] - new_top)
    summed = first_part[1] * first_factor + second_part[1] * second_factor
    mixed_sum = first_part[2] * first_factor[..., None] + second_part[2] * second_factor[..., None]
    return (new_top, summed, mixed_sum)


MASK_FILL = -3e30


def hist_kernel(kv0_ref, q_ref, k_ref, v_ref, bias_ref, cos_ref, sin_ref, acc_out, m_out, l_out, m_sc, l_sc, acc_sc, *, scale, blocks):
    j = pl.program_id(1)

    @pl.when(j == 0)
    def _():
        m_sc[...] = jnp.full(m_sc.shape, NEG_FILL, jnp.float32)
        l_sc[...] = jnp.zeros(l_sc.shape, jnp.float32)
        acc_sc[...] = jnp.zeros(acc_sc.shape, jnp.float32)

    pages, page_len, hd = k_ref.shape
    n = pages * page_len
    keys = k_ref[...].reshape(n, hd).astype(jnp.float32)
    vals = v_ref[...].reshape(n, hd)
    keys = (keys * cos_ref[...] + pltpu.roll(keys, hd // 2, 1) * sin_ref[...]).astype(jnp.bfloat16)
    scores = lax.dot_general(
        q_ref[0], keys, (((1,), (1,)), ((), ())), preferred_element_type=jnp.float32
    )
    scores = scores * scale + bias_ref[0]
    m_old = m_sc[...]
    m_new = jnp.maximum(m_old, jnp.max(scores, axis=1, keepdims=True))
    alpha = jnp.exp(m_old - m_new)
    weights = jnp.exp(scores - m_new)
    l_sc[...] = alpha * l_sc[...] + jnp.sum(weights, axis=1, keepdims=True)
    acc_sc[...] = alpha * acc_sc[...] + jnp.dot(
        weights.astype(jnp.bfloat16), vals, preferred_element_type=jnp.float32
    )
    m_sc[...] = m_new

    @pl.when(j == blocks - 1)
    def _():
        acc_out[0] = acc_sc[...]
        m_out[0] = m_sc[...]
        l_out[0] = l_sc[...]


def hist_attend(kv0, q_k, kv_local, bias, cos2, sin2, pb):
    heads, rows, hd = q_k.shape
    slots, page_len, width = kv_local.shape
    kv_heads = width // (2 * hd)
    blocks = slots // pb
    kernel = functools.partial(hist_kernel, scale=1.0 / hd ** 0.5, blocks=blocks)

    def head_of(h, kv0_ref):
        return (kv0_ref[0] + h) % kv_heads

    grid_spec = pltpu.PrefetchScalarGridSpec(
        num_scalar_prefetch=1,
        grid=(heads, blocks),
        in_specs=[
            pl.BlockSpec((1, rows, hd), lambda h, j, r: (h, 0, 0)),
            pl.BlockSpec((pb, page_len, hd), lambda h, j, r: (j, 0, 2 * head_of(h, r))),
            pl.BlockSpec((pb, page_len, hd), lambda h, j, r: (j, 0, 2 * head_of(h, r) + 1)),
            pl.BlockSpec((1, 1, pb * page_len), lambda h, j, r: (j, 0, 0)),
            pl.BlockSpec((1, hd), lambda h, j, r: (0, 0)),
            pl.BlockSpec((1, hd), lambda h, j, r: (0, 0)),
        ],
        out_specs=[
            pl.BlockSpec((1, rows, hd), lambda h, j, r: (h, 0, 0)),
            pl.BlockSpec((1, rows, 1), lambda h, j, r: (h, 0, 0)),
            pl.BlockSpec((1, rows, 1), lambda h, j, r: (h, 0, 0)),
        ],
        scratch_shapes=[
            pltpu.VMEM((rows, 1), jnp.float32),
            pltpu.VMEM((rows, 1), jnp.float32),
            pltpu.VMEM((rows, hd), jnp.float32),
        ],
    )
    return pl.pallas_call(
        kernel,
        grid_spec=grid_spec,
        out_shape=[
            jax.ShapeDtypeStruct((heads, rows, hd), jnp.float32),
            jax.ShapeDtypeStruct((heads, rows, 1), jnp.float32),
            jax.ShapeDtypeStruct((heads, rows, 1), jnp.float32),
        ],
        compiler_params=pltpu.CompilerParams(dimension_semantics=("arbitrary", "arbitrary")),
        cost_estimate=pl.CostEstimate(
            flops=4 * heads * rows * slots * page_len * hd,
            transcendentals=heads * rows * slots * page_len,
            bytes_accessed=heads * (slots * page_len * 2 * hd * 2 + rows * hd * 6),
        ),
    )(jnp.reshape(kv0, (1,)).astype(jnp.int32), q_k, kv_local, kv_local, bias, cos2, sin2)


def axis_reduce(x, axis, op):
    n = lax.axis_size(axis)
    d = 1
    while d < n:
        x = op(x, lax.ppermute(x, axis, perm=[(i, i ^ d) for i in range(n)]))
        d *= 2
    return x


def bit_scatter(block, axis):
    n = lax.axis_size(axis)
    idx = lax.axis_index(axis)
    d = 1
    while d < n:
        bit = (idx // d) % 2
        keep = lax.dynamic_index_in_dim(block, bit, 0, keepdims=False)
        send = lax.dynamic_index_in_dim(block, 1 - bit, 0, keepdims=False)
        block = keep + lax.ppermute(send, axis, perm=[(i, i ^ d) for i in range(n)])
        d *= 2
    return block


def bit_gather(x, axis):
    n = lax.axis_size(axis)
    idx = lax.axis_index(axis)
    dists = []
    d = n // 2
    while d >= 1:
        other = lax.ppermute(x, axis, perm=[(i, i ^ d) for i in range(n)])
        low = (idx // d) % 2 == 0
        x = jnp.stack([jnp.where(low, x, other), jnp.where(low, other, x)])
        dists.insert(0, d)
        d //= 2
    k = len(dists)
    order = sorted(range(k), key=lambda j: -dists[j])
    x = jnp.transpose(x, tuple(order) + tuple(range(k, x.ndim)))
    return x.reshape((n * x.shape[k],) + x.shape[k + 1 :])


def scatter_rows(x, axis):
    n = lax.axis_size(axis)
    if n & (n - 1):
        return lax.psum_scatter(x, axis, scatter_dimension=0, tiled=True)
    bits = n.bit_length() - 1
    x = x.reshape((2,) * bits + (x.shape[0] // n,) + x.shape[1:])
    x = jnp.transpose(x, tuple(range(bits - 1, -1, -1)) + tuple(range(bits, x.ndim)))
    return bit_scatter(x, axis)


def axis_sum(x, axis):
    n = lax.axis_size(axis)
    if n & (n - 1):
        return lax.psum(x, axis)
    return axis_reduce(x, axis, jnp.add)


def axis_max(x, axes):
    if any(lax.axis_size(a) & (lax.axis_size(a) - 1) for a in axes):
        return jnp.max(lax.all_gather(x, axes), axis=0)
    for a in axes:
        x = axis_reduce(x, a, jnp.maximum)
    return x


def body(x_new, kv_pages, w_query, w_keyval, w_out, lengths, page_store, offsets):
    tensors = lax.axis_size("tensor")
    shards = lax.axis_size("store")
    tensor_idx = lax.axis_index("tensor")
    store_idx = lax.axis_index("store")
    tok_count = x_new.shape[0]
    assert tok_count == TURN and lengths.shape[0] == 1
    local_slots = kv_pages.shape[1]
    capacity = local_slots * tensors
    page_len = kv_pages.shape[2]
    kv_heads = kv_pages.shape[3] // (2 * HD)
    group_size = HQ // KVH
    local_heads = w_query.shape[1] // HD
    local_kv = max(1, local_heads // group_size)
    local_group = local_heads // local_kv
    freq_table = inverse_freq(HD)
    kv_first = tensor_idx * local_heads // group_size
    keyval_cols = lax.dynamic_slice_in_dim(w_keyval, kv_first * (2 * HD), local_kv * 2 * HD, 1)
    query_part = jnp.dot(x_new, w_query, preferred_element_type=jnp.float32)
    keyval_part = jnp.dot(x_new, keyval_cols, preferred_element_type=jnp.float32)
    keyval_sum = axis_sum(keyval_part, "store")
    keyval_local = keyval_sum.reshape(tok_count, local_kv, 2, HD)
    tok_ids = jnp.arange(tok_count, dtype=jnp.int32)
    tok_sess = tok_ids // TURN
    tok_pos = table_lookup(lengths, tok_sess) + tok_ids % TURN
    tok_angle = tok_pos.astype(jnp.float32)[:, None, None] * freq_table
    if local_heads % shards == 0 and not shards & (shards - 1):
        s_bits = shards.bit_length() - 1
        heads_major = jnp.transpose(query_part.reshape(tok_count, local_heads, HD), (1, 0, 2))
        block = heads_major.reshape((2,) * s_bits + (local_heads // shards, tok_count, HD))
        block = jnp.transpose(block, tuple(range(s_bits - 1, -1, -1)) + tuple(range(s_bits, s_bits + 3)))
        block = bit_scatter(block, "store")
        block = to_half(rotate(block, jnp.transpose(tok_angle, (1, 0, 2))))
        q_heads = bit_gather(block, "store")
        query_rot = jnp.transpose(q_heads, (1, 0, 2))
    else:
        query_sum = axis_sum(query_part, "store")
        query_rot = to_half(rotate(query_sum.reshape(tok_count, local_heads, HD), tok_angle))
        q_heads = jnp.transpose(query_rot, (1, 0, 2))
    key_new = to_half(rotate(keyval_local[:, :, 0], tok_angle))
    value_new = to_half(keyval_local[:, :, 1])

    first_slot = store_idx * capacity + tensor_idx * local_slots
    key_sess, key_ok, key_off = slot_meta(
        page_store, lengths, offsets, shards, capacity, first_slot, local_slots, page_len
    )
    pb = local_slots
    bias = jnp.where(key_ok, 0.0, MASK_FILL).astype(jnp.float32)
    bias = bias.reshape(local_slots // pb, 1, pb * page_len)
    hist_angle = offsets[0].astype(jnp.float32) * freq_table
    kv_local = kv_pages.reshape(local_slots, page_len, kv_pages.shape[3])
    cosine = jnp.cos(hist_angle)
    sine = jnp.sin(hist_angle)
    cos2 = jnp.concatenate([cosine, cosine])[None, :]
    sin2 = jnp.concatenate([-sine, sine])[None, :]

    if tensors & (tensors - 1):
        q_all = lax.all_gather(q_heads, "tensor", axis=0, tiled=True)
    else:
        q_all = bit_gather(q_heads, "tensor")
    q_k = q_all.reshape(kv_heads, group_size * tok_count, HD)
    if local_heads % group_size == 0:
        own = hist_attend(
            kv_first, q_heads.reshape(local_kv, group_size * tok_count, HD), kv_local, bias, cos2, sin2, pb
        )
        rest_first = kv_first + local_kv
        q_rest = lax.dynamic_slice_in_dim(
            jnp.concatenate([q_k, q_k], axis=0), rest_first % kv_heads, kv_heads - local_kv, 0
        )
        rest = hist_attend(rest_first % kv_heads, q_rest, kv_local, bias, cos2, sin2, pb)
        parts = []
        for first, second in zip(own, rest):
            rolled = jnp.concatenate([first, second, first, second], axis=0)
            parts.append(lax.dynamic_slice_in_dim(rolled, kv_heads - kv_first, kv_heads, 0))
        acc, top, total = parts
    else:
        acc, top, total = hist_attend(jnp.int32(0), q_k, kv_local, bias, cos2, sin2, pb)
    acc = acc.reshape(HQ, tok_count, HD)
    top = top.reshape(HQ, tok_count)
    total = total.reshape(HQ, tok_count)

    glob_top = axis_max(top, ("store", "tensor"))
    factor = jnp.exp(top - glob_top)
    packed = jnp.concatenate(
        [(acc * factor[..., None]).reshape(HQ, tok_count * HD), total * factor], axis=1
    )
    new_allowed = (tok_sess[:, None] == tok_sess[None, :]) & (tok_ids[None, :] <= tok_ids[:, None])
    chunk_heads = HQ // (tensors * shards)
    if (
        HQ % (tensors * shards) == 0
        and group_size % chunk_heads == 0
        and not shards & (shards - 1)
        and not tensors & (tensors - 1)
    ):
        width = packed.shape[1]
        s_bits = shards.bit_length() - 1
        t_bits = tensors.bit_length() - 1
        block = packed.reshape((2,) * t_bits + (2,) * s_bits + (chunk_heads, width))
        order = tuple(range(t_bits + s_bits - 1, t_bits - 1, -1)) + tuple(range(t_bits - 1, -1, -1))
        block = jnp.transpose(block, order + (t_bits + s_bits, t_bits + s_bits + 1))
        block = bit_scatter(block, "store")
        block = bit_scatter(block, "tensor")
        acc = block[:, : tok_count * HD].reshape(chunk_heads, tok_count, HD)
        total = block[:, tok_count * HD :]
        chunk_first = (tensor_idx * shards + store_idx) * chunk_heads
        loc_top = lax.dynamic_slice_in_dim(glob_top, chunk_first, chunk_heads, 0)
        hist_part = (jnp.transpose(loc_top), jnp.transpose(total), jnp.transpose(acc, (1, 0, 2)))
        in_group = store_idx * chunk_heads
        query_chunk = lax.dynamic_slice_in_dim(query_rot, in_group, chunk_heads, 1)
        kv_idx = in_group // group_size
        key_chunk = lax.dynamic_slice_in_dim(key_new, kv_idx, 1, 1)
        value_chunk = lax.dynamic_slice_in_dim(value_new, kv_idx, 1, 1)
        new_part = attend(
            query_chunk.reshape(tok_count, 1, chunk_heads, HD), key_chunk, value_chunk, new_allowed
        )
        new_flat = (
            new_part[0].reshape(tok_count, chunk_heads),
            new_part[1].reshape(tok_count, chunk_heads),
            new_part[2].reshape(tok_count, chunk_heads, HD),
        )
        combined = combine(hist_part, new_flat)
        attended = (
            (combined[2] / combined[1][..., None])
            .reshape(tok_count, chunk_heads * HD)
            .astype(jnp.bfloat16)
        )
        attended = lax.all_gather(attended, "store", axis=1, tiled=True)
    else:
        packed = lax.psum_scatter(packed, "tensor", scatter_dimension=0, tiled=True)
        packed = axis_sum(packed, "store")
        acc = packed[:, : tok_count * HD].reshape(local_heads, tok_count, HD)
        total = packed[:, tok_count * HD :]
        loc_top = lax.dynamic_slice_in_dim(glob_top, tensor_idx * local_heads, local_heads, 0)
        hist_part = (
            jnp.transpose(loc_top),
            jnp.transpose(total),
            jnp.transpose(acc, (1, 0, 2)),
        )

        query_local = query_rot.reshape(tok_count, local_kv, local_group, HD)
        new_part = attend(query_local, key_new, value_new, new_allowed)
        new_flat = (
            new_part[0].reshape(tok_count, local_heads),
            new_part[1].reshape(tok_count, local_heads),
            new_part[2].reshape(tok_count, local_heads, HD),
        )
        combined = combine(hist_part, new_flat)
        attended = (
            (combined[2] / combined[1][..., None])
            .reshape(tok_count, local_heads * HD)
            .astype(jnp.bfloat16)
        )
    result = scatter_rows(jnp.dot(attended, w_out, preferred_element_type=jnp.float32), "tensor")
    return result.astype(jnp.bfloat16)


def solution(mesh):
    in_specs = (
        P("groups", "store"),
        P(("groups", "store"), "tensor", None, None),
        P("store", "tensor"),
        P("store", None),
        P("tensor", "store"),
        P("groups"),
        P("groups", None),
        P("groups"),
    )
    out_specs = P(("groups", "tensor"), "store")
    return jax.shard_map(body, mesh=mesh, in_specs=in_specs, out_specs=out_specs, check_vma=False)
```

```python
import math

import jax
import jax.numpy as jnp
import numpy as np
from jax import lax
from jax.sharding import PartitionSpec as P
from jax.experimental import pallas as pl
from jax.experimental.pallas import tpu as pltpu
import functools

HQ = 64
KVH = 8
HD = 128
TURN = 64
MAXPAGES = 256


THETA = 500000.0
NEG_FILL = -1e30
ROPE_FACTOR = 8.0
LOW_FACTOR = 1.0
HIGH_FACTOR = 4.0
INITIAL_CONTEXT = 8192.0


def joined(x, axis, combine):
    everything = jax.tree.map(lambda part: lax.all_gather(part, axis), x)
    first = jax.tree.map(lambda part: part[0], everything)

    def step(k, so_far):
        return combine(so_far, jax.tree.map(lambda part: part[k], everything))

    return lax.fori_loop(1, lax.axis_size(axis), step, first)


def inverse_freq(width):
    steps_half = jnp.arange(width // 2, dtype=jnp.float32)
    base_freq = jnp.exp(-(steps_half * (2.0 / width)) * jnp.log(jnp.float32(THETA)))
    wavelength = 2.0 * math.pi / base_freq
    low_wave = INITIAL_CONTEXT / LOW_FACTOR
    high_wave = INITIAL_CONTEXT / HIGH_FACTOR
    smooth = (INITIAL_CONTEXT / wavelength - LOW_FACTOR) / (HIGH_FACTOR - LOW_FACTOR)
    blended = (1.0 - smooth) * base_freq / ROPE_FACTOR + smooth * base_freq
    scaled = jnp.where(wavelength > low_wave, base_freq / ROPE_FACTOR, blended)
    return jnp.where(wavelength < high_wave, base_freq, scaled)


def rotate(values, rot_angle):
    half_width = values.shape[-1] // 2
    first_half = values[..., :half_width]
    second_half = values[..., half_width:]
    cosine = jnp.cos(rot_angle)
    sine_part = jnp.sin(rot_angle)
    return jnp.concatenate(
        [
            first_half * cosine - second_half * sine_part,
            second_half * cosine + first_half * sine_part,
        ],
        axis=-1,
    )


def to_half(values):
    return values.astype(jnp.bfloat16)


def table_lookup(table, index):
    hits = index[..., None] == jnp.arange(table.shape[0], dtype=jnp.int32)
    return jnp.sum(jnp.where(hits, table, 0), axis=-1)


def page_positions(page_store, shards, capacity):
    store_of = page_store[:, 0]
    onehot = (store_of[:, None] == jnp.arange(shards, dtype=jnp.int32)[None, :]).astype(jnp.int32)
    ranks = jnp.sum((jnp.cumsum(onehot, axis=0) - onehot) * onehot, axis=1)
    return store_of * capacity + ranks


def slot_meta(page_store, lengths, offsets, shards, capacity, first_slot, slot_count, page_len):
    positions = page_positions(page_store, shards, capacity)
    wanted = first_slot + jnp.arange(slot_count, dtype=jnp.int32)
    matches = (positions[:, None] == wanted[None, :]).astype(jnp.int32)
    page_ids = jnp.sum(matches * jnp.arange(positions.shape[0], dtype=jnp.int32)[:, None], axis=0)
    filled = jnp.sum(matches, axis=0) > 0
    slot_sess = page_ids // MAXPAGES
    slot_page = page_ids % MAXPAGES
    key_pos = slot_page[:, None] * page_len + jnp.arange(page_len, dtype=jnp.int32)[None, :]
    key_ok = filled[:, None] & (key_pos < table_lookup(lengths, slot_sess)[:, None])
    key_sess = jnp.broadcast_to(slot_sess[:, None], (slot_count, page_len))
    key_off = jnp.broadcast_to(table_lookup(offsets, slot_sess)[:, None], (slot_count, page_len))
    return (key_sess.reshape(-1), key_ok.reshape(-1), key_off.reshape(-1))


def attend(query, key_rows, value_rows, allowed):
    score_scale = 1.0 / query.shape[-1] ** 0.5
    scores = (
        jnp.einsum("tkgd,nkd->tkgn", query, key_rows, preferred_element_type=jnp.float32)
        * score_scale
    )
    wide_mask = allowed[:, None, None, :]
    scores = jnp.where(wide_mask, scores, NEG_FILL)
    row_top = jnp.max(scores, axis=-1)
    weights = jnp.where(wide_mask, jnp.exp(scores - row_top[..., None]), 0.0)
    weight_sum = jnp.sum(weights, axis=-1)
    head_mix = jnp.einsum(
        "tkgn,nkd->tkgd",
        weights.astype(jnp.bfloat16),
        value_rows,
        preferred_element_type=jnp.float32,
    )
    return (row_top, weight_sum, head_mix)


def combine(first_part, second_part):
    new_top = jnp.maximum(first_part[0], second_part[0])
    first_factor = jnp.exp(first_part[0] - new_top)
    second_factor = jnp.exp(second_part[0] - new_top)
    summed = first_part[1] * first_factor + second_part[1] * second_factor
    mixed_sum = first_part[2] * first_factor[..., None] + second_part[2] * second_factor[..., None]
    return (new_top, summed, mixed_sum)


MASK_FILL = -3e30


def hist_kernel(kv0_ref, q_ref, k_ref, v_ref, bias_ref, cos_ref, sin_ref, acc_out, m_out, l_out, m_sc, l_sc, acc_sc, *, scale, blocks):
    j = pl.program_id(1)

    @pl.when(j == 0)
    def _():
        m_sc[...] = jnp.full(m_sc.shape, NEG_FILL, jnp.float32)
        l_sc[...] = jnp.zeros(l_sc.shape, jnp.float32)
        acc_sc[...] = jnp.zeros(acc_sc.shape, jnp.float32)

    pages, page_len, hd = k_ref.shape
    n = pages * page_len
    keys = k_ref[...].reshape(n, hd).astype(jnp.float32)
    vals = v_ref[...].reshape(n, hd)
    keys = (keys * cos_ref[...] + pltpu.roll(keys, hd // 2, 1) * sin_ref[...]).astype(jnp.bfloat16)
    scores = lax.dot_general(
        q_ref[0], keys, (((1,), (1,)), ((), ())), preferred_element_type=jnp.float32
    )
    scores = scores * scale + bias_ref[0]
    m_old = m_sc[...]
    m_new = jnp.maximum(m_old, jnp.max(scores, axis=1, keepdims=True))
    alpha = jnp.exp(m_old - m_new)
    weights = jnp.exp(scores - m_new)
    l_sc[...] = alpha * l_sc[...] + jnp.sum(weights, axis=1, keepdims=True)
    acc_sc[...] = alpha * acc_sc[...] + jnp.dot(
        weights.astype(jnp.bfloat16), vals, preferred_element_type=jnp.float32
    )
    m_sc[...] = m_new

    @pl.when(j == blocks - 1)
    def _():
        acc_out[0] = acc_sc[...]
        m_out[0] = m_sc[...]
        l_out[0] = l_sc[...]


def hist_attend(kv0, q_k, kv_local, bias, cos2, sin2, pb):
    heads, rows, hd = q_k.shape
    slots, page_len, width = kv_local.shape
    kv_heads = width // (2 * hd)
    blocks = slots // pb
    kernel = functools.partial(hist_kernel, scale=1.0 / hd ** 0.5, blocks=blocks)

    def head_of(h, kv0_ref):
        return (kv0_ref[0] + h) % kv_heads

    grid_spec = pltpu.PrefetchScalarGridSpec(
        num_scalar_prefetch=1,
        grid=(heads, blocks),
        in_specs=[
            pl.BlockSpec((1, rows, hd), lambda h, j, r: (h, 0, 0)),
            pl.BlockSpec((pb, page_len, hd), lambda h, j, r: (j, 0, 2 * head_of(h, r))),
            pl.BlockSpec((pb, page_len, hd), lambda h, j, r: (j, 0, 2 * head_of(h, r) + 1)),
            pl.BlockSpec((1, 1, pb * page_len), lambda h, j, r: (j, 0, 0)),
            pl.BlockSpec((1, hd), lambda h, j, r: (0, 0)),
            pl.BlockSpec((1, hd), lambda h, j, r: (0, 0)),
        ],
        out_specs=[
            pl.BlockSpec((1, rows, hd), lambda h, j, r: (h, 0, 0)),
            pl.BlockSpec((1, rows, 1), lambda h, j, r: (h, 0, 0)),
            pl.BlockSpec((1, rows, 1), lambda h, j, r: (h, 0, 0)),
        ],
        scratch_shapes=[
            pltpu.VMEM((rows, 1), jnp.float32),
            pltpu.VMEM((rows, 1), jnp.float32),
            pltpu.VMEM((rows, hd), jnp.float32),
        ],
    )
    return pl.pallas_call(
        kernel,
        grid_spec=grid_spec,
        out_shape=[
            jax.ShapeDtypeStruct((heads, rows, hd), jnp.float32),
            jax.ShapeDtypeStruct((heads, rows, 1), jnp.float32),
            jax.ShapeDtypeStruct((heads, rows, 1), jnp.float32),
        ],
        compiler_params=pltpu.CompilerParams(dimension_semantics=("arbitrary", "arbitrary")),
        cost_estimate=pl.CostEstimate(
            flops=4 * heads * rows * slots * page_len * hd,
            transcendentals=heads * rows * slots * page_len,
            bytes_accessed=heads * (slots * page_len * 2 * hd * 2 + rows * hd * 6),
        ),
    )(jnp.reshape(kv0, (1,)).astype(jnp.int32), q_k, kv_local, kv_local, bias, cos2, sin2)


def axis_reduce(x, axis, op):
    n = lax.axis_size(axis)
    d = 1
    while d < n:
        x = op(x, lax.ppermute(x, axis, perm=[(i, i ^ d) for i in range(n)]))
        d *= 2
    return x


def bit_scatter(block, axis):
    n = lax.axis_size(axis)
    idx = lax.axis_index(axis)
    d = 1
    while d < n:
        bit = (idx // d) % 2
        keep = lax.dynamic_index_in_dim(block, bit, 0, keepdims=False)
        send = lax.dynamic_index_in_dim(block, 1 - bit, 0, keepdims=False)
        block = keep + lax.ppermute(send, axis, perm=[(i, i ^ d) for i in range(n)])
        d *= 2
    return block


def bit_gather(x, axis):
    n = lax.axis_size(axis)
    idx = lax.axis_index(axis)
    dists = []
    d = n // 2
    while d >= 1:
        other = lax.ppermute(x, axis, perm=[(i, i ^ d) for i in range(n)])
        low = (idx // d) % 2 == 0
        x = jnp.stack([jnp.where(low, x, other), jnp.where(low, other, x)])
        dists.insert(0, d)
        d //= 2
    k = len(dists)
    order = sorted(range(k), key=lambda j: -dists[j])
    x = jnp.transpose(x, tuple(order) + tuple(range(k, x.ndim)))
    return x.reshape((n * x.shape[k],) + x.shape[k + 1 :])


def scatter_rows(x, axis):
    n = lax.axis_size(axis)
    if n & (n - 1):
        return lax.psum_scatter(x, axis, scatter_dimension=0, tiled=True)
    bits = n.bit_length() - 1
    x = x.reshape((2,) * bits + (x.shape[0] // n,) + x.shape[1:])
    x = jnp.transpose(x, tuple(range(bits - 1, -1, -1)) + tuple(range(bits, x.ndim)))
    return bit_scatter(x, axis)


def axis_sum(x, axis):
    n = lax.axis_size(axis)
    if n & (n - 1):
        return lax.psum(x, axis)
    return axis_reduce(x, axis, jnp.add)


def axis_max(x, axes):
    if any(lax.axis_size(a) & (lax.axis_size(a) - 1) for a in axes):
        return jnp.max(lax.all_gather(x, axes), axis=0)
    for a in axes:
        x = axis_reduce(x, a, jnp.maximum)
    return x


def body(x_new, kv_pages, w_query, w_keyval, w_out, lengths, page_store, offsets):
    tensors = lax.axis_size("tensor")
    shards = lax.axis_size("store")
    tensor_idx = lax.axis_index("tensor")
    store_idx = lax.axis_index("store")
    tok_count = x_new.shape[0]
    assert tok_count == TURN and lengths.shape[0] == 1
    local_slots = kv_pages.shape[1]
    capacity = local_slots * tensors
    page_len = kv_pages.shape[2]
    kv_heads = kv_pages.shape[3] // (2 * HD)
    group_size = HQ // KVH
    local_heads = w_query.shape[1] // HD
    local_kv = max(1, local_heads // group_size)
    local_group = local_heads // local_kv
    freq_table = inverse_freq(HD)
    kv_first = tensor_idx * local_heads // group_size
    keyval_cols = lax.dynamic_slice_in_dim(w_keyval, kv_first * (2 * HD), local_kv * 2 * HD, 1)
    query_part = jnp.dot(x_new, w_query, preferred_element_type=jnp.float32)
    keyval_part = jnp.dot(x_new, keyval_cols, preferred_element_type=jnp.float32)
    keyval_sum = axis_sum(keyval_part, "store")
    keyval_local = keyval_sum.reshape(tok_count, local_kv, 2, HD)
    tok_ids = jnp.arange(tok_count, dtype=jnp.int32)
    tok_sess = tok_ids // TURN
    tok_pos = table_lookup(lengths, tok_sess) + tok_ids % TURN
    tok_angle = tok_pos.astype(jnp.float32)[:, None, None] * freq_table
    if local_heads % shards == 0 and not shards & (shards - 1):
        s_bits = shards.bit_length() - 1
        heads_major = jnp.transpose(query_part.reshape(tok_count, local_heads, HD), (1, 0, 2))
        block = heads_major.reshape((2,) * s_bits + (local_heads // shards, tok_count, HD))
        block = jnp.transpose(block, tuple(range(s_bits - 1, -1, -1)) + tuple(range(s_bits, s_bits + 3)))
        block = bit_scatter(block, "store")
        block = to_half(rotate(block, jnp.transpose(tok_angle, (1, 0, 2))))
        q_heads = bit_gather(block, "store")
        query_rot = jnp.transpose(q_heads, (1, 0, 2))
        q_all = bit_gather(block, "tensor")
        if tensors & (tensors - 1):
            q_all = None
        else:
            q_all = bit_gather(q_all, "store").reshape((shards, tensors) + block.shape)
            q_all = jnp.transpose(q_all, (1, 0, 2, 3, 4)).reshape((HQ,) + block.shape[1:])
    else:
        query_sum = axis_sum(query_part, "store")
        query_rot = to_half(rotate(query_sum.reshape(tok_count, local_heads, HD), tok_angle))
        q_heads = jnp.transpose(query_rot, (1, 0, 2))
        q_all = None
    key_new = to_half(rotate(keyval_local[:, :, 0], tok_angle))
    value_new = to_half(keyval_local[:, :, 1])

    first_slot = store_idx * capacity + tensor_idx * local_slots
    key_sess, key_ok, key_off = slot_meta(
        page_store, lengths, offsets, shards, capacity, first_slot, local_slots, page_len
    )
    pb = local_slots
    bias = jnp.where(key_ok, 0.0, MASK_FILL).astype(jnp.float32)
    bias = bias.reshape(local_slots // pb, 1, pb * page_len)
    hist_angle = offsets[0].astype(jnp.float32) * freq_table
    kv_local = kv_pages.reshape(local_slots, page_len, kv_pages.shape[3])
    cosine = jnp.cos(hist_angle)
    sine = jnp.sin(hist_angle)
    cos2 = jnp.concatenate([cosine, cosine])[None, :]
    sin2 = jnp.concatenate([-sine, sine])[None, :]

    if q_all is None and tensors & (tensors - 1):
        q_all = lax.all_gather(q_heads, "tensor", axis=0, tiled=True)
    elif q_all is None:
        q_all = bit_gather(q_heads, "tensor")
    q_k = q_all.reshape(kv_heads, group_size * tok_count, HD)
    if local_heads % group_size == 0:
        own = hist_attend(
            kv_first, q_heads.reshape(local_kv, group_size * tok_count, HD), kv_local, bias, cos2, sin2, pb
        )
        rest_first = kv_first + local_kv
        q_rest = lax.dynamic_slice_in_dim(
            jnp.concatenate([q_k, q_k], axis=0), rest_first % kv_heads, kv_heads - local_kv, 0
        )
        rest = hist_attend(rest_first % kv_heads, q_rest, kv_local, bias, cos2, sin2, pb)
        parts = []
        for first, second in zip(own, rest):
            rolled = jnp.concatenate([first, second, first, second], axis=0)
            parts.append(lax.dynamic_slice_in_dim(rolled, kv_heads - kv_first, kv_heads, 0))
        acc, top, total = parts
    else:
        acc, top, total = hist_attend(jnp.int32(0), q_k, kv_local, bias, cos2, sin2, pb)
    acc = acc.reshape(HQ, tok_count, HD)
    top = top.reshape(HQ, tok_count)
    total = total.reshape(HQ, tok_count)

    glob_top = axis_max(top, ("store", "tensor"))
    factor = jnp.exp(top - glob_top)
    packed = jnp.concatenate(
        [(acc * factor[..., None]).reshape(HQ, tok_count * HD), total * factor], axis=1
    )
    new_allowed = (tok_sess[:, None] == tok_sess[None, :]) & (tok_ids[None, :] <= tok_ids[:, None])
    chunk_heads = HQ // (tensors * shards)
    if (
        HQ % (tensors * shards) == 0
        and group_size % chunk_heads == 0
        and not shards & (shards - 1)
        and not tensors & (tensors - 1)
    ):
        width = packed.shape[1]
        s_bits = shards.bit_length() - 1
        t_bits = tensors.bit_length() - 1
        block = packed.reshape((2,) * t_bits + (2,) * s_bits + (chunk_heads, width))
        order = tuple(range(t_bits + s_bits - 1, t_bits - 1, -1)) + tuple(range(t_bits - 1, -1, -1))
        block = jnp.transpose(block, order + (t_bits + s_bits, t_bits + s_bits + 1))
        block = bit_scatter(block, "store")
        block = bit_scatter(block, "tensor")
        acc = block[:, : tok_count * HD].reshape(chunk_heads, tok_count, HD)
        total = block[:, tok_count * HD :]
        chunk_first = (tensor_idx * shards + store_idx) * chunk_heads
        loc_top = lax.dynamic_slice_in_dim(glob_top, chunk_first, chunk_heads, 0)
        hist_part = (jnp.transpose(loc_top), jnp.transpose(total), jnp.transpose(acc, (1, 0, 2)))
        in_group = store_idx * chunk_heads
        query_chunk = lax.dynamic_slice_in_dim(query_rot, in_group, chunk_heads, 1)
        kv_idx = in_group // group_size
        key_chunk = lax.dynamic_slice_in_dim(key_new, kv_idx, 1, 1)
        value_chunk = lax.dynamic_slice_in_dim(value_new, kv_idx, 1, 1)
        new_part = attend(
            query_chunk.reshape(tok_count, 1, chunk_heads, HD), key_chunk, value_chunk, new_allowed
        )
        new_flat = (
            new_part[0].reshape(tok_count, chunk_heads),
            new_part[1].reshape(tok_count, chunk_heads),
            new_part[2].reshape(tok_count, chunk_heads, HD),
        )
        combined = combine(hist_part, new_flat)
        attended = (
            (combined[2] / combined[1][..., None])
            .reshape(tok_count, chunk_heads * HD)
            .astype(jnp.bfloat16)
        )
        attended = lax.all_gather(attended, "store", axis=1, tiled=True)
    else:
        packed = lax.psum_scatter(packed, "tensor", scatter_dimension=0, tiled=True)
        packed = axis_sum(packed, "store")
        acc = packed[:, : tok_count * HD].reshape(local_heads, tok_count, HD)
        total = packed[:, tok_count * HD :]
        loc_top = lax.dynamic_slice_in_dim(glob_top, tensor_idx * local_heads, local_heads, 0)
        hist_part = (
            jnp.transpose(loc_top),
            jnp.transpose(total),
            jnp.transpose(acc, (1, 0, 2)),
        )

        query_local = query_rot.reshape(tok_count, local_kv, local_group, HD)
        new_part = attend(query_local, key_new, value_new, new_allowed)
        new_flat = (
            new_part[0].reshape(tok_count, local_heads),
            new_part[1].reshape(tok_count, local_heads),
            new_part[2].reshape(tok_count, local_heads, HD),
        )
        combined = combine(hist_part, new_flat)
        attended = (
            (combined[2] / combined[1][..., None])
            .reshape(tok_count, local_heads * HD)
            .astype(jnp.bfloat16)
        )
    result = scatter_rows(jnp.dot(attended, w_out, preferred_element_type=jnp.float32), "tensor")
    return result.astype(jnp.bfloat16)


def solution(mesh):
    in_specs = (
        P("groups", "store"),
        P(("groups", "store"), "tensor", None, None),
        P("store", "tensor"),
        P("store", None),
        P("tensor", "store"),
        P("groups"),
        P("groups", None),
        P("groups"),
    )
    out_specs = P(("groups", "tensor"), "store")
    return jax.shard_map(body, mesh=mesh, in_specs=in_specs, out_specs=out_specs, check_vma=False)
```

```python
import math

import jax
import jax.numpy as jnp
import numpy as np
from jax import lax
from jax.sharding import PartitionSpec as P
from jax.experimental import pallas as pl
from jax.experimental.pallas import tpu as pltpu
import functools

HQ = 64
KVH = 8
HD = 128
TURN = 64
MAXPAGES = 256


THETA = 500000.0
NEG_FILL = -1e30
ROPE_FACTOR = 8.0
LOW_FACTOR = 1.0
HIGH_FACTOR = 4.0
INITIAL_CONTEXT = 8192.0


def joined(x, axis, combine):
    everything = jax.tree.map(lambda part: lax.all_gather(part, axis), x)
    first = jax.tree.map(lambda part: part[0], everything)

    def step(k, so_far):
        return combine(so_far, jax.tree.map(lambda part: part[k], everything))

    return lax.fori_loop(1, lax.axis_size(axis), step, first)


def inverse_freq(width):
    steps_half = jnp.arange(width // 2, dtype=jnp.float32)
    base_freq = jnp.exp(-(steps_half * (2.0 / width)) * jnp.log(jnp.float32(THETA)))
    wavelength = 2.0 * math.pi / base_freq
    low_wave = INITIAL_CONTEXT / LOW_FACTOR
    high_wave = INITIAL_CONTEXT / HIGH_FACTOR
    smooth = (INITIAL_CONTEXT / wavelength - LOW_FACTOR) / (HIGH_FACTOR - LOW_FACTOR)
    blended = (1.0 - smooth) * base_freq / ROPE_FACTOR + smooth * base_freq
    scaled = jnp.where(wavelength > low_wave, base_freq / ROPE_FACTOR, blended)
    return jnp.where(wavelength < high_wave, base_freq, scaled)


def rotate(values, rot_angle):
    half_width = values.shape[-1] // 2
    first_half = values[..., :half_width]
    second_half = values[..., half_width:]
    cosine = jnp.cos(rot_angle)
    sine_part = jnp.sin(rot_angle)
    return jnp.concatenate(
        [
            first_half * cosine - second_half * sine_part,
            second_half * cosine + first_half * sine_part,
        ],
        axis=-1,
    )


def to_half(values):
    return values.astype(jnp.bfloat16)


def table_lookup(table, index):
    hits = index[..., None] == jnp.arange(table.shape[0], dtype=jnp.int32)
    return jnp.sum(jnp.where(hits, table, 0), axis=-1)


def page_positions(page_store, shards, capacity):
    store_of = page_store[:, 0]
    onehot = (store_of[:, None] == jnp.arange(shards, dtype=jnp.int32)[None, :]).astype(jnp.int32)
    ranks = jnp.sum((jnp.cumsum(onehot, axis=0) - onehot) * onehot, axis=1)
    return store_of * capacity + ranks


def slot_meta(page_store, lengths, offsets, shards, capacity, first_slot, slot_count, page_len):
    positions = page_positions(page_store, shards, capacity)
    wanted = first_slot + jnp.arange(slot_count, dtype=jnp.int32)
    matches = (positions[:, None] == wanted[None, :]).astype(jnp.int32)
    page_ids = jnp.sum(matches * jnp.arange(positions.shape[0], dtype=jnp.int32)[:, None], axis=0)
    filled = jnp.sum(matches, axis=0) > 0
    slot_sess = page_ids // MAXPAGES
    slot_page = page_ids % MAXPAGES
    key_pos = slot_page[:, None] * page_len + jnp.arange(page_len, dtype=jnp.int32)[None, :]
    key_ok = filled[:, None] & (key_pos < table_lookup(lengths, slot_sess)[:, None])
    key_sess = jnp.broadcast_to(slot_sess[:, None], (slot_count, page_len))
    key_off = jnp.broadcast_to(table_lookup(offsets, slot_sess)[:, None], (slot_count, page_len))
    return (key_sess.reshape(-1), key_ok.reshape(-1), key_off.reshape(-1))


def attend(query, key_rows, value_rows, allowed):
    score_scale = 1.0 / query.shape[-1] ** 0.5
    scores = (
        jnp.einsum("tkgd,nkd->tkgn", query, key_rows, preferred_element_type=jnp.float32)
        * score_scale
    )
    wide_mask = allowed[:, None, None, :]
    scores = jnp.where(wide_mask, scores, NEG_FILL)
    row_top = jnp.max(scores, axis=-1)
    weights = jnp.where(wide_mask, jnp.exp(scores - row_top[..., None]), 0.0)
    weight_sum = jnp.sum(weights, axis=-1)
    head_mix = jnp.einsum(
        "tkgn,nkd->tkgd",
        weights.astype(jnp.bfloat16),
        value_rows,
        preferred_element_type=jnp.float32,
    )
    return (row_top, weight_sum, head_mix)


def combine(first_part, second_part):
    new_top = jnp.maximum(first_part[0], second_part[0])
    first_factor = jnp.exp(first_part[0] - new_top)
    second_factor = jnp.exp(second_part[0] - new_top)
    summed = first_part[1] * first_factor + second_part[1] * second_factor
    mixed_sum = first_part[2] * first_factor[..., None] + second_part[2] * second_factor[..., None]
    return (new_top, summed, mixed_sum)


MASK_FILL = -3e30


def hist_kernel(kv0_ref, q_ref, k_ref, v_ref, bias_ref, cos_ref, sin_ref, acc_out, m_out, l_out, m_sc, l_sc, acc_sc, *, scale, blocks):
    j = pl.program_id(1)

    @pl.when(j == 0)
    def _():
        m_sc[...] = jnp.full(m_sc.shape, NEG_FILL, jnp.float32)
        l_sc[...] = jnp.zeros(l_sc.shape, jnp.float32)
        acc_sc[...] = jnp.zeros(acc_sc.shape, jnp.float32)

    pages, page_len, hd = k_ref.shape
    n = pages * page_len
    keys = k_ref[...].reshape(n, hd).astype(jnp.float32)
    vals = v_ref[...].reshape(n, hd)
    keys = (keys * cos_ref[...] + pltpu.roll(keys, hd // 2, 1) * sin_ref[...]).astype(jnp.bfloat16)
    scores = lax.dot_general(
        q_ref[0], keys, (((1,), (1,)), ((), ())), preferred_element_type=jnp.float32
    )
    scores = scores * scale + bias_ref[0]
    m_old = m_sc[...]
    m_new = jnp.maximum(m_old, jnp.max(scores, axis=1, keepdims=True))
    alpha = jnp.exp(m_old - m_new)
    weights = jnp.exp(scores - m_new)
    l_sc[...] = alpha * l_sc[...] + jnp.sum(weights, axis=1, keepdims=True)
    acc_sc[...] = alpha * acc_sc[...] + jnp.dot(
        weights.astype(jnp.bfloat16), vals, preferred_element_type=jnp.float32
    )
    m_sc[...] = m_new

    @pl.when(j == blocks - 1)
    def _():
        acc_out[0] = acc_sc[...]
        m_out[0] = m_sc[...]
        l_out[0] = l_sc[...]


def hist_attend(kv0, q_k, kv_local, bias, cos2, sin2, pb):
    heads, rows, hd = q_k.shape
    slots, page_len, width = kv_local.shape
    kv_heads = width // (2 * hd)
    blocks = slots // pb
    kernel = functools.partial(hist_kernel, scale=1.0 / hd ** 0.5, blocks=blocks)

    def head_of(h, kv0_ref):
        return (kv0_ref[0] + h) % kv_heads

    grid_spec = pltpu.PrefetchScalarGridSpec(
        num_scalar_prefetch=1,
        grid=(heads, blocks),
        in_specs=[
            pl.BlockSpec((1, rows, hd), lambda h, j, r: (h, 0, 0)),
            pl.BlockSpec((pb, page_len, hd), lambda h, j, r: (j, 0, 2 * head_of(h, r))),
            pl.BlockSpec((pb, page_len, hd), lambda h, j, r: (j, 0, 2 * head_of(h, r) + 1)),
            pl.BlockSpec((1, 1, pb * page_len), lambda h, j, r: (j, 0, 0)),
            pl.BlockSpec((1, hd), lambda h, j, r: (0, 0)),
            pl.BlockSpec((1, hd), lambda h, j, r: (0, 0)),
        ],
        out_specs=[
            pl.BlockSpec((1, rows, hd), lambda h, j, r: (h, 0, 0)),
            pl.BlockSpec((1, rows, 1), lambda h, j, r: (h, 0, 0)),
            pl.BlockSpec((1, rows, 1), lambda h, j, r: (h, 0, 0)),
        ],
        scratch_shapes=[
            pltpu.VMEM((rows, 1), jnp.float32),
            pltpu.VMEM((rows, 1), jnp.float32),
            pltpu.VMEM((rows, hd), jnp.float32),
        ],
    )
    return pl.pallas_call(
        kernel,
        grid_spec=grid_spec,
        out_shape=[
            jax.ShapeDtypeStruct((heads, rows, hd), jnp.float32),
            jax.ShapeDtypeStruct((heads, rows, 1), jnp.float32),
            jax.ShapeDtypeStruct((heads, rows, 1), jnp.float32),
        ],
        compiler_params=pltpu.CompilerParams(dimension_semantics=("arbitrary", "arbitrary")),
        cost_estimate=pl.CostEstimate(
            flops=4 * heads * rows * slots * page_len * hd,
            transcendentals=heads * rows * slots * page_len,
            bytes_accessed=heads * (slots * page_len * 2 * hd * 2 + rows * hd * 6),
        ),
    )(jnp.reshape(kv0, (1,)).astype(jnp.int32), q_k, kv_local, kv_local, bias, cos2, sin2)


def axis_reduce(x, axis, op):
    n = lax.axis_size(axis)
    d = 1
    while d < n:
        x = op(x, lax.ppermute(x, axis, perm=[(i, i ^ d) for i in range(n)]))
        d *= 2
    return x


def bit_scatter(block, axis):
    n = lax.axis_size(axis)
    idx = lax.axis_index(axis)
    d = 1
    while d < n:
        bit = (idx // d) % 2
        keep = lax.dynamic_index_in_dim(block, bit, 0, keepdims=False)
        send = lax.dynamic_index_in_dim(block, 1 - bit, 0, keepdims=False)
        block = keep + lax.ppermute(send, axis, perm=[(i, i ^ d) for i in range(n)])
        d *= 2
    return block


def bit_gather(x, axis):
    n = lax.axis_size(axis)
    idx = lax.axis_index(axis)
    dists = []
    d = n // 2
    while d >= 1:
        other = lax.ppermute(x, axis, perm=[(i, i ^ d) for i in range(n)])
        low = (idx // d) % 2 == 0
        x = jnp.stack([jnp.where(low, x, other), jnp.where(low, other, x)])
        dists.insert(0, d)
        d //= 2
    k = len(dists)
    order = sorted(range(k), key=lambda j: -dists[j])
    x = jnp.transpose(x, tuple(order) + tuple(range(k, x.ndim)))
    return x.reshape((n * x.shape[k],) + x.shape[k + 1 :])


def scatter_rows(x, axis):
    n = lax.axis_size(axis)
    if n & (n - 1):
        return lax.psum_scatter(x, axis, scatter_dimension=0, tiled=True)
    bits = n.bit_length() - 1
    x = x.reshape((2,) * bits + (x.shape[0] // n,) + x.shape[1:])
    x = jnp.transpose(x, tuple(range(bits - 1, -1, -1)) + tuple(range(bits, x.ndim)))
    return bit_scatter(x, axis)


def axis_sum(x, axis):
    n = lax.axis_size(axis)
    if n & (n - 1):
        return lax.psum(x, axis)
    return axis_reduce(x, axis, jnp.add)


def axis_max(x, axes):
    if any(lax.axis_size(a) & (lax.axis_size(a) - 1) for a in axes):
        return jnp.max(lax.all_gather(x, axes), axis=0)
    for a in axes:
        x = axis_reduce(x, a, jnp.maximum)
    return x


def body(x_new, kv_pages, w_query, w_keyval, w_out, lengths, page_store, offsets):
    tensors = lax.axis_size("tensor")
    shards = lax.axis_size("store")
    tensor_idx = lax.axis_index("tensor")
    store_idx = lax.axis_index("store")
    tok_count = x_new.shape[0]
    assert tok_count == TURN and lengths.shape[0] == 1
    local_slots = kv_pages.shape[1]
    capacity = local_slots * tensors
    page_len = kv_pages.shape[2]
    kv_heads = kv_pages.shape[3] // (2 * HD)
    group_size = HQ // KVH
    local_heads = w_query.shape[1] // HD
    local_kv = max(1, local_heads // group_size)
    local_group = local_heads // local_kv
    freq_table = inverse_freq(HD)
    kv_first = tensor_idx * local_heads // group_size
    keyval_cols = lax.dynamic_slice_in_dim(w_keyval, kv_first * (2 * HD), local_kv * 2 * HD, 1)
    query_part = jnp.dot(x_new, w_query, preferred_element_type=jnp.float32)
    keyval_part = jnp.dot(x_new, keyval_cols, preferred_element_type=jnp.float32)
    keyval_sum = axis_sum(keyval_part, "store")
    keyval_local = keyval_sum.reshape(tok_count, local_kv, 2, HD)
    tok_ids = jnp.arange(tok_count, dtype=jnp.int32)
    tok_sess = tok_ids // TURN
    tok_pos = table_lookup(lengths, tok_sess) + tok_ids % TURN
    tok_angle = tok_pos.astype(jnp.float32)[:, None, None] * freq_table
    if local_heads % shards == 0 and not shards & (shards - 1):
        s_bits = shards.bit_length() - 1
        heads_major = jnp.transpose(query_part.reshape(tok_count, local_heads, HD), (1, 0, 2))
        block = heads_major.reshape((2,) * s_bits + (local_heads // shards, tok_count, HD))
        block = jnp.transpose(block, tuple(range(s_bits - 1, -1, -1)) + tuple(range(s_bits, s_bits + 3)))
        block = bit_scatter(block, "store")
        block = to_half(rotate(block, jnp.transpose(tok_angle, (1, 0, 2))))
        q_heads = bit_gather(block, "store")
        query_rot = jnp.transpose(q_heads, (1, 0, 2))
        q_all = bit_gather(block, "tensor")
        if tensors & (tensors - 1):
            q_all = None
        else:
            q_all = bit_gather(q_all, "store").reshape((shards, tensors) + block.shape)
            q_all = jnp.transpose(q_all, (1, 0, 2, 3, 4)).reshape((HQ,) + block.shape[1:])
    else:
        query_sum = axis_sum(query_part, "store")
        query_rot = to_half(rotate(query_sum.reshape(tok_count, local_heads, HD), tok_angle))
        q_heads = jnp.transpose(query_rot, (1, 0, 2))
        q_all = None
    key_new = to_half(rotate(keyval_local[:, :, 0], tok_angle))
    value_new = to_half(keyval_local[:, :, 1])

    first_slot = store_idx * capacity + tensor_idx * local_slots
    key_sess, key_ok, key_off = slot_meta(
        page_store, lengths, offsets, shards, capacity, first_slot, local_slots, page_len
    )
    pb = local_slots
    bias = jnp.where(key_ok, 0.0, MASK_FILL).astype(jnp.float32)
    bias = bias.reshape(local_slots // pb, 1, pb * page_len)
    hist_angle = offsets[0].astype(jnp.float32) * freq_table
    kv_local = kv_pages.reshape(local_slots, page_len, kv_pages.shape[3])
    cosine = jnp.cos(hist_angle)
    sine = jnp.sin(hist_angle)
    cos2 = jnp.concatenate([cosine, cosine])[None, :]
    sin2 = jnp.concatenate([-sine, sine])[None, :]

    if q_all is None and tensors & (tensors - 1):
        q_all = lax.all_gather(q_heads, "tensor", axis=0, tiled=True)
    elif q_all is None:
        q_all = bit_gather(q_heads, "tensor")
    q_k = q_all.reshape(kv_heads, group_size * tok_count, HD)
    if local_heads % group_size == 0:
        own = hist_attend(
            kv_first, q_heads.reshape(local_kv, group_size * tok_count, HD), kv_local, bias, cos2, sin2, pb
        )
        rest_first = kv_first + local_kv
        q_rest = lax.dynamic_slice_in_dim(
            jnp.concatenate([q_k, q_k], axis=0), rest_first % kv_heads, kv_heads - local_kv, 0
        )
        rest = hist_attend(rest_first % kv_heads, q_rest, kv_local, bias, cos2, sin2, pb)
        parts = []
        for first, second in zip(own, rest):
            rolled = jnp.concatenate([first, second, first, second], axis=0)
            parts.append(lax.dynamic_slice_in_dim(rolled, kv_heads - kv_first, kv_heads, 0))
        acc, top, total = parts
    else:
        acc, top, total = hist_attend(jnp.int32(0), q_k, kv_local, bias, cos2, sin2, pb)
    acc = acc.reshape(HQ, tok_count, HD)
    top = top.reshape(HQ, tok_count)
    total = total.reshape(HQ, tok_count)

    glob_top = axis_max(top, ("store", "tensor"))
    factor = jnp.exp(top - glob_top)
    packed = jnp.concatenate(
        [(acc * factor[..., None]).reshape(HQ, tok_count * HD), total * factor], axis=1
    )
    new_allowed = (tok_sess[:, None] == tok_sess[None, :]) & (tok_ids[None, :] <= tok_ids[:, None])
    chunk_heads = HQ // (tensors * shards)
    if (
        HQ % (tensors * shards) == 0
        and group_size % chunk_heads == 0
        and not shards & (shards - 1)
        and not tensors & (tensors - 1)
    ):
        width = packed.shape[1]
        s_bits = shards.bit_length() - 1
        t_bits = tensors.bit_length() - 1
        block = packed.reshape((2,) * t_bits + (2,) * s_bits + (chunk_heads, width))
        order = tuple(range(t_bits + s_bits - 1, t_bits - 1, -1)) + tuple(range(t_bits - 1, -1, -1))
        block = jnp.transpose(block, order + (t_bits + s_bits, t_bits + s_bits + 1))
        block = bit_scatter(block, "store")
        block = bit_scatter(block, "tensor")
        acc = block[:, : tok_count * HD].reshape(chunk_heads, tok_count, HD)
        total = block[:, tok_count * HD :]
        chunk_first = (tensor_idx * shards + store_idx) * chunk_heads
        loc_top = lax.dynamic_slice_in_dim(glob_top, chunk_first, chunk_heads, 0)
        hist_part = (jnp.transpose(loc_top), jnp.transpose(total), jnp.transpose(acc, (1, 0, 2)))
        in_group = store_idx * chunk_heads
        query_chunk = lax.dynamic_slice_in_dim(query_rot, in_group, chunk_heads, 1)
        kv_idx = in_group // group_size
        key_chunk = lax.dynamic_slice_in_dim(key_new, kv_idx, 1, 1)
        value_chunk = lax.dynamic_slice_in_dim(value_new, kv_idx, 1, 1)
        new_part = attend(
            query_chunk.reshape(tok_count, 1, chunk_heads, HD), key_chunk, value_chunk, new_allowed
        )
        new_flat = (
            new_part[0].reshape(tok_count, chunk_heads),
            new_part[1].reshape(tok_count, chunk_heads),
            new_part[2].reshape(tok_count, chunk_heads, HD),
        )
        combined = combine(hist_part, new_flat)
        attended = (
            (combined[2] / combined[1][..., None])
            .reshape(tok_count, chunk_heads * HD)
            .astype(jnp.bfloat16)
        )
        attended = jnp.transpose(bit_gather(jnp.transpose(attended), "store"))
    else:
        packed = lax.psum_scatter(packed, "tensor", scatter_dimension=0, tiled=True)
        packed = axis_sum(packed, "store")
        acc = packed[:, : tok_count * HD].reshape(local_heads, tok_count, HD)
        total = packed[:, tok_count * HD :]
        loc_top = lax.dynamic_slice_in_dim(glob_top, tensor_idx * local_heads, local_heads, 0)
        hist_part = (
            jnp.transpose(loc_top),
            jnp.transpose(total),
            jnp.transpose(acc, (1, 0, 2)),
        )

        query_local = query_rot.reshape(tok_count, local_kv, local_group, HD)
        new_part = attend(query_local, key_new, value_new, new_allowed)
        new_flat = (
            new_part[0].reshape(tok_count, local_heads),
            new_part[1].reshape(tok_count, local_heads),
            new_part[2].reshape(tok_count, local_heads, HD),
        )
        combined = combine(hist_part, new_flat)
        attended = (
            (combined[2] / combined[1][..., None])
            .reshape(tok_count, local_heads * HD)
            .astype(jnp.bfloat16)
        )
    result = scatter_rows(jnp.dot(attended, w_out, preferred_element_type=jnp.float32), "tensor")
    return result.astype(jnp.bfloat16)


def solution(mesh):
    in_specs = (
        P("groups", "store"),
        P(("groups", "store"), "tensor", None, None),
        P("store", "tensor"),
        P("store", None),
        P("tensor", "store"),
        P("groups"),
        P("groups", None),
        P("groups"),
    )
    out_specs = P(("groups", "tensor"), "store")
    return jax.shard_map(body, mesh=mesh, in_specs=in_specs, out_specs=out_specs, check_vma=False)
```

```python
import math

import jax
import jax.numpy as jnp
import numpy as np
from jax import lax
from jax.sharding import PartitionSpec as P
from jax.experimental import pallas as pl
from jax.experimental.pallas import tpu as pltpu
import functools

HQ = 64
KVH = 8
HD = 128
TURN = 64
MAXPAGES = 256


THETA = 500000.0
NEG_FILL = -1e30
ROPE_FACTOR = 8.0
LOW_FACTOR = 1.0
HIGH_FACTOR = 4.0
INITIAL_CONTEXT = 8192.0


def joined(x, axis, combine):
    everything = jax.tree.map(lambda part: lax.all_gather(part, axis), x)
    first = jax.tree.map(lambda part: part[0], everything)

    def step(k, so_far):
        return combine(so_far, jax.tree.map(lambda part: part[k], everything))

    return lax.fori_loop(1, lax.axis_size(axis), step, first)


def inverse_freq(width):
    steps_half = jnp.arange(width // 2, dtype=jnp.float32)
    base_freq = jnp.exp(-(steps_half * (2.0 / width)) * jnp.log(jnp.float32(THETA)))
    wavelength = 2.0 * math.pi / base_freq
    low_wave = INITIAL_CONTEXT / LOW_FACTOR
    high_wave = INITIAL_CONTEXT / HIGH_FACTOR
    smooth = (INITIAL_CONTEXT / wavelength - LOW_FACTOR) / (HIGH_FACTOR - LOW_FACTOR)
    blended = (1.0 - smooth) * base_freq / ROPE_FACTOR + smooth * base_freq
    scaled = jnp.where(wavelength > low_wave, base_freq / ROPE_FACTOR, blended)
    return jnp.where(wavelength < high_wave, base_freq, scaled)


def rotate(values, rot_angle):
    half_width = values.shape[-1] // 2
    first_half = values[..., :half_width]
    second_half = values[..., half_width:]
    cosine = jnp.cos(rot_angle)
    sine_part = jnp.sin(rot_angle)
    return jnp.concatenate(
        [
            first_half * cosine - second_half * sine_part,
            second_half * cosine + first_half * sine_part,
        ],
        axis=-1,
    )


def to_half(values):
    return values.astype(jnp.bfloat16)


def table_lookup(table, index):
    hits = index[..., None] == jnp.arange(table.shape[0], dtype=jnp.int32)
    return jnp.sum(jnp.where(hits, table, 0), axis=-1)


def page_positions(page_store, shards, capacity):
    store_of = page_store[:, 0]
    onehot = (store_of[:, None] == jnp.arange(shards, dtype=jnp.int32)[None, :]).astype(jnp.int32)
    ranks = jnp.sum((jnp.cumsum(onehot, axis=0) - onehot) * onehot, axis=1)
    return store_of * capacity + ranks


def slot_meta(page_store, lengths, offsets, shards, capacity, first_slot, slot_count, page_len):
    positions = page_positions(page_store, shards, capacity)
    wanted = first_slot + jnp.arange(slot_count, dtype=jnp.int32)
    matches = (positions[:, None] == wanted[None, :]).astype(jnp.int32)
    page_ids = jnp.sum(matches * jnp.arange(positions.shape[0], dtype=jnp.int32)[:, None], axis=0)
    filled = jnp.sum(matches, axis=0) > 0
    slot_sess = page_ids // MAXPAGES
    slot_page = page_ids % MAXPAGES
    key_pos = slot_page[:, None] * page_len + jnp.arange(page_len, dtype=jnp.int32)[None, :]
    key_ok = filled[:, None] & (key_pos < table_lookup(lengths, slot_sess)[:, None])
    key_sess = jnp.broadcast_to(slot_sess[:, None], (slot_count, page_len))
    key_off = jnp.broadcast_to(table_lookup(offsets, slot_sess)[:, None], (slot_count, page_len))
    return (key_sess.reshape(-1), key_ok.reshape(-1), key_off.reshape(-1))


def attend(query, key_rows, value_rows, allowed):
    score_scale = 1.0 / query.shape[-1] ** 0.5
    scores = (
        jnp.einsum("tkgd,nkd->tkgn", query, key_rows, preferred_element_type=jnp.float32)
        * score_scale
    )
    wide_mask = allowed[:, None, None, :]
    scores = jnp.where(wide_mask, scores, NEG_FILL)
    row_top = jnp.max(scores, axis=-1)
    weights = jnp.where(wide_mask, jnp.exp(scores - row_top[..., None]), 0.0)
    weight_sum = jnp.sum(weights, axis=-1)
    head_mix = jnp.einsum(
        "tkgn,nkd->tkgd",
        weights.astype(jnp.bfloat16),
        value_rows,
        preferred_element_type=jnp.float32,
    )
    return (row_top, weight_sum, head_mix)


def combine(first_part, second_part):
    new_top = jnp.maximum(first_part[0], second_part[0])
    first_factor = jnp.exp(first_part[0] - new_top)
    second_factor = jnp.exp(second_part[0] - new_top)
    summed = first_part[1] * first_factor + second_part[1] * second_factor
    mixed_sum = first_part[2] * first_factor[..., None] + second_part[2] * second_factor[..., None]
    return (new_top, summed, mixed_sum)


MASK_FILL = -3e30


def hist_kernel(kv0_ref, q_ref, k_ref, v_ref, bias_ref, cos_ref, sin_ref, acc_out, m_out, l_out, m_sc, l_sc, acc_sc, *, scale, blocks):
    j = pl.program_id(1)

    @pl.when(j == 0)
    def _():
        m_sc[...] = jnp.full(m_sc.shape, NEG_FILL, jnp.float32)
        l_sc[...] = jnp.zeros(l_sc.shape, jnp.float32)
        acc_sc[...] = jnp.zeros(acc_sc.shape, jnp.float32)

    pages, page_len, hd = k_ref.shape
    n = pages * page_len
    keys = k_ref[...].reshape(n, hd).astype(jnp.float32)
    vals = v_ref[...].reshape(n, hd)
    keys = (keys * cos_ref[...] + pltpu.roll(keys, hd // 2, 1) * sin_ref[...]).astype(jnp.bfloat16)
    scores = lax.dot_general(
        q_ref[0], keys, (((1,), (1,)), ((), ())), preferred_element_type=jnp.float32
    )
    scores = scores + bias_ref[0]
    m_old = m_sc[...]
    m_new = jnp.maximum(m_old, jnp.max(scores, axis=1, keepdims=True))
    alpha = jnp.exp((m_old - m_new) * scale)
    weights = jnp.exp((scores - m_new) * scale)
    l_sc[...] = alpha * l_sc[...] + jnp.sum(weights, axis=1, keepdims=True)
    acc_sc[...] = alpha * acc_sc[...] + jnp.dot(
        weights.astype(jnp.bfloat16), vals, preferred_element_type=jnp.float32
    )
    m_sc[...] = m_new

    @pl.when(j == blocks - 1)
    def _():
        acc_out[0] = acc_sc[...]
        m_out[0] = m_sc[...] * scale
        l_out[0] = l_sc[...]


def hist_attend(kv0, q_k, kv_local, bias, cos2, sin2, pb):
    heads, rows, hd = q_k.shape
    slots, page_len, width = kv_local.shape
    kv_heads = width // (2 * hd)
    blocks = slots // pb
    kernel = functools.partial(hist_kernel, scale=1.0 / hd ** 0.5, blocks=blocks)

    def head_of(h, kv0_ref):
        return (kv0_ref[0] + h) % kv_heads

    grid_spec = pltpu.PrefetchScalarGridSpec(
        num_scalar_prefetch=1,
        grid=(heads, blocks),
        in_specs=[
            pl.BlockSpec((1, rows, hd), lambda h, j, r: (h, 0, 0)),
            pl.BlockSpec((pb, page_len, hd), lambda h, j, r: (j, 0, 2 * head_of(h, r))),
            pl.BlockSpec((pb, page_len, hd), lambda h, j, r: (j, 0, 2 * head_of(h, r) + 1)),
            pl.BlockSpec((1, 1, pb * page_len), lambda h, j, r: (j, 0, 0)),
            pl.BlockSpec((1, hd), lambda h, j, r: (0, 0)),
            pl.BlockSpec((1, hd), lambda h, j, r: (0, 0)),
        ],
        out_specs=[
            pl.BlockSpec((1, rows, hd), lambda h, j, r: (h, 0, 0)),
            pl.BlockSpec((1, rows, 1), lambda h, j, r: (h, 0, 0)),
            pl.BlockSpec((1, rows, 1), lambda h, j, r: (h, 0, 0)),
        ],
        scratch_shapes=[
            pltpu.VMEM((rows, 1), jnp.float32),
            pltpu.VMEM((rows, 1), jnp.float32),
            pltpu.VMEM((rows, hd), jnp.float32),
        ],
    )
    return pl.pallas_call(
        kernel,
        grid_spec=grid_spec,
        out_shape=[
            jax.ShapeDtypeStruct((heads, rows, hd), jnp.float32),
            jax.ShapeDtypeStruct((heads, rows, 1), jnp.float32),
            jax.ShapeDtypeStruct((heads, rows, 1), jnp.float32),
        ],
        compiler_params=pltpu.CompilerParams(dimension_semantics=("arbitrary", "arbitrary")),
        cost_estimate=pl.CostEstimate(
            flops=4 * heads * rows * slots * page_len * hd,
            transcendentals=heads * rows * slots * page_len,
            bytes_accessed=heads * (slots * page_len * 2 * hd * 2 + rows * hd * 6),
        ),
    )(jnp.reshape(kv0, (1,)).astype(jnp.int32), q_k, kv_local, kv_local, bias, cos2, sin2)


def axis_reduce(x, axis, op):
    n = lax.axis_size(axis)
    d = 1
    while d < n:
        x = op(x, lax.ppermute(x, axis, perm=[(i, i ^ d) for i in range(n)]))
        d *= 2
    return x


def bit_scatter(block, axis):
    n = lax.axis_size(axis)
    idx = lax.axis_index(axis)
    d = 1
    while d < n:
        bit = (idx // d) % 2
        keep = lax.dynamic_index_in_dim(block, bit, 0, keepdims=False)
        send = lax.dynamic_index_in_dim(block, 1 - bit, 0, keepdims=False)
        block = keep + lax.ppermute(send, axis, perm=[(i, i ^ d) for i in range(n)])
        d *= 2
    return block


def bit_gather(x, axis):
    n = lax.axis_size(axis)
    idx = lax.axis_index(axis)
    dists = []
    d = n // 2
    while d >= 1:
        other = lax.ppermute(x, axis, perm=[(i, i ^ d) for i in range(n)])
        low = (idx // d) % 2 == 0
        x = jnp.stack([jnp.where(low, x, other), jnp.where(low, other, x)])
        dists.insert(0, d)
        d //= 2
    k = len(dists)
    order = sorted(range(k), key=lambda j: -dists[j])
    x = jnp.transpose(x, tuple(order) + tuple(range(k, x.ndim)))
    return x.reshape((n * x.shape[k],) + x.shape[k + 1 :])


def scatter_rows(x, axis):
    n = lax.axis_size(axis)
    if n & (n - 1):
        return lax.psum_scatter(x, axis, scatter_dimension=0, tiled=True)
    bits = n.bit_length() - 1
    x = x.reshape((2,) * bits + (x.shape[0] // n,) + x.shape[1:])
    x = jnp.transpose(x, tuple(range(bits - 1, -1, -1)) + tuple(range(bits, x.ndim)))
    return bit_scatter(x, axis)


def axis_sum(x, axis):
    n = lax.axis_size(axis)
    if n & (n - 1):
        return lax.psum(x, axis)
    return axis_reduce(x, axis, jnp.add)


def axis_max(x, axes):
    if any(lax.axis_size(a) & (lax.axis_size(a) - 1) for a in axes):
        return jnp.max(lax.all_gather(x, axes), axis=0)
    for a in axes:
        x = axis_reduce(x, a, jnp.maximum)
    return x


def body(x_new, kv_pages, w_query, w_keyval, w_out, lengths, page_store, offsets):
    tensors = lax.axis_size("tensor")
    shards = lax.axis_size("store")
    tensor_idx = lax.axis_index("tensor")
    store_idx = lax.axis_index("store")
    tok_count = x_new.shape[0]
    assert tok_count == TURN and lengths.shape[0] == 1
    local_slots = kv_pages.shape[1]
    capacity = local_slots * tensors
    page_len = kv_pages.shape[2]
    kv_heads = kv_pages.shape[3] // (2 * HD)
    group_size = HQ // KVH
    local_heads = w_query.shape[1] // HD
    local_kv = max(1, local_heads // group_size)
    local_group = local_heads // local_kv
    freq_table = inverse_freq(HD)
    kv_first = tensor_idx * local_heads // group_size
    keyval_cols = lax.dynamic_slice_in_dim(w_keyval, kv_first * (2 * HD), local_kv * 2 * HD, 1)
    query_part = jnp.dot(x_new, w_query, preferred_element_type=jnp.float32)
    keyval_part = jnp.dot(x_new, keyval_cols, preferred_element_type=jnp.float32)
    keyval_sum = axis_sum(keyval_part, "store")
    keyval_local = keyval_sum.reshape(tok_count, local_kv, 2, HD)
    tok_ids = jnp.arange(tok_count, dtype=jnp.int32)
    tok_sess = tok_ids // TURN
    tok_pos = table_lookup(lengths, tok_sess) + tok_ids % TURN
    tok_angle = tok_pos.astype(jnp.float32)[:, None, None] * freq_table
    if local_heads % shards == 0 and not shards & (shards - 1):
        s_bits = shards.bit_length() - 1
        heads_major = jnp.transpose(query_part.reshape(tok_count, local_heads, HD), (1, 0, 2))
        block = heads_major.reshape((2,) * s_bits + (local_heads // shards, tok_count, HD))
        block = jnp.transpose(block, tuple(range(s_bits - 1, -1, -1)) + tuple(range(s_bits, s_bits + 3)))
        block = bit_scatter(block, "store")
        block = to_half(rotate(block, jnp.transpose(tok_angle, (1, 0, 2))))
        q_heads = bit_gather(block, "store")
        query_rot = jnp.transpose(q_heads, (1, 0, 2))
        q_all = bit_gather(block, "tensor")
        if tensors & (tensors - 1):
            q_all = None
        else:
            q_all = bit_gather(q_all, "store").reshape((shards, tensors) + block.shape)
            q_all = jnp.transpose(q_all, (1, 0, 2, 3, 4)).reshape((HQ,) + block.shape[1:])
    else:
        query_sum = axis_sum(query_part, "store")
        query_rot = to_half(rotate(query_sum.reshape(tok_count, local_heads, HD), tok_angle))
        q_heads = jnp.transpose(query_rot, (1, 0, 2))
        q_all = None
    key_new = to_half(rotate(keyval_local[:, :, 0], tok_angle))
    value_new = to_half(keyval_local[:, :, 1])

    first_slot = store_idx * capacity + tensor_idx * local_slots
    key_sess, key_ok, key_off = slot_meta(
        page_store, lengths, offsets, shards, capacity, first_slot, local_slots, page_len
    )
    pb = local_slots
    bias = jnp.where(key_ok, 0.0, MASK_FILL).astype(jnp.float32)
    bias = bias.reshape(local_slots // pb, 1, pb * page_len)
    hist_angle = offsets[0].astype(jnp.float32) * freq_table
    kv_local = kv_pages.reshape(local_slots, page_len, kv_pages.shape[3])
    cosine = jnp.cos(hist_angle)
    sine = jnp.sin(hist_angle)
    cos2 = jnp.concatenate([cosine, cosine])[None, :]
    sin2 = jnp.concatenate([-sine, sine])[None, :]

    if q_all is None and tensors & (tensors - 1):
        q_all = lax.all_gather(q_heads, "tensor", axis=0, tiled=True)
    elif q_all is None:
        q_all = bit_gather(q_heads, "tensor")
    q_k = q_all.reshape(kv_heads, group_size * tok_count, HD)
    if local_heads % group_size == 0:
        own = hist_attend(
            kv_first, q_heads.reshape(local_kv, group_size * tok_count, HD), kv_local, bias, cos2, sin2, pb
        )
        rest_first = kv_first + local_kv
        q_rest = lax.dynamic_slice_in_dim(
            jnp.concatenate([q_k, q_k], axis=0), rest_first % kv_heads, kv_heads - local_kv, 0
        )
        rest = hist_attend(rest_first % kv_heads, q_rest, kv_local, bias, cos2, sin2, pb)
        parts = []
        for first, second in zip(own, rest):
            rolled = jnp.concatenate([first, second, first, second], axis=0)
            parts.append(lax.dynamic_slice_in_dim(rolled, kv_heads - kv_first, kv_heads, 0))
        acc, top, total = parts
    else:
        acc, top, total = hist_attend(jnp.int32(0), q_k, kv_local, bias, cos2, sin2, pb)
    acc = acc.reshape(HQ, tok_count, HD)
    top = top.reshape(HQ, tok_count)
    total = total.reshape(HQ, tok_count)

    glob_top = axis_max(top, ("store", "tensor"))
    factor = jnp.exp(top - glob_top)
    packed = jnp.concatenate(
        [(acc * factor[..., None]).reshape(HQ, tok_count * HD), total * factor], axis=1
    )
    new_allowed = (tok_sess[:, None] == tok_sess[None, :]) & (tok_ids[None, :] <= tok_ids[:, None])
    chunk_heads = HQ // (tensors * shards)
    if (
        HQ % (tensors * shards) == 0
        and group_size % chunk_heads == 0
        and not shards & (shards - 1)
        and not tensors & (tensors - 1)
    ):
        width = packed.shape[1]
        s_bits = shards.bit_length() - 1
        t_bits = tensors.bit_length() - 1
        block = packed.reshape((2,) * t_bits + (2,) * s_bits + (chunk_heads, width))
        order = tuple(range(t_bits + s_bits - 1, t_bits - 1, -1)) + tuple(range(t_bits - 1, -1, -1))
        block = jnp.transpose(block, order + (t_bits + s_bits, t_bits + s_bits + 1))
        block = bit_scatter(block, "store")
        block = bit_scatter(block, "tensor")
        acc = block[:, : tok_count * HD].reshape(chunk_heads, tok_count, HD)
        total = block[:, tok_count * HD :]
        chunk_first = (tensor_idx * shards + store_idx) * chunk_heads
        loc_top = lax.dynamic_slice_in_dim(glob_top, chunk_first, chunk_heads, 0)
        hist_part = (jnp.transpose(loc_top), jnp.transpose(total), jnp.transpose(acc, (1, 0, 2)))
        in_group = store_idx * chunk_heads
        query_chunk = lax.dynamic_slice_in_dim(query_rot, in_group, chunk_heads, 1)
        kv_idx = in_group // group_size
        key_chunk = lax.dynamic_slice_in_dim(key_new, kv_idx, 1, 1)
        value_chunk = lax.dynamic_slice_in_dim(value_new, kv_idx, 1, 1)
        new_part = attend(
            query_chunk.reshape(tok_count, 1, chunk_heads, HD), key_chunk, value_chunk, new_allowed
        )
        new_flat = (
            new_part[0].reshape(tok_count, chunk_heads),
            new_part[1].reshape(tok_count, chunk_heads),
            new_part[2].reshape(tok_count, chunk_heads, HD),
        )
        combined = combine(hist_part, new_flat)
        attended = (
            (combined[2] / combined[1][..., None])
            .reshape(tok_count, chunk_heads * HD)
            .astype(jnp.bfloat16)
        )
        attended = lax.all_gather(attended, "store", axis=1, tiled=True)
    else:
        packed = lax.psum_scatter(packed, "tensor", scatter_dimension=0, tiled=True)
        packed = axis_sum(packed, "store")
        acc = packed[:, : tok_count * HD].reshape(local_heads, tok_count, HD)
        total = packed[:, tok_count * HD :]
        loc_top = lax.dynamic_slice_in_dim(glob_top, tensor_idx * local_heads, local_heads, 0)
        hist_part = (
            jnp.transpose(loc_top),
            jnp.transpose(total),
            jnp.transpose(acc, (1, 0, 2)),
        )

        query_local = query_rot.reshape(tok_count, local_kv, local_group, HD)
        new_part = attend(query_local, key_new, value_new, new_allowed)
        new_flat = (
            new_part[0].reshape(tok_count, local_heads),
            new_part[1].reshape(tok_count, local_heads),
            new_part[2].reshape(tok_count, local_heads, HD),
        )
        combined = combine(hist_part, new_flat)
        attended = (
            (combined[2] / combined[1][..., None])
            .reshape(tok_count, local_heads * HD)
            .astype(jnp.bfloat16)
        )
    result = scatter_rows(jnp.dot(attended, w_out, preferred_element_type=jnp.float32), "tensor")
    return result.astype(jnp.bfloat16)


def solution(mesh):
    in_specs = (
        P("groups", "store"),
        P(("groups", "store"), "tensor", None, None),
        P("store", "tensor"),
        P("store", None),
        P("tensor", "store"),
        P("groups"),
        P("groups", None),
        P("groups"),
    )
    out_specs = P(("groups", "tensor"), "store")
    return jax.shard_map(body, mesh=mesh, in_specs=in_specs, out_specs=out_specs, check_vma=False)
```

```python
import math

import jax
import jax.numpy as jnp
import numpy as np
from jax import lax
from jax.sharding import PartitionSpec as P
from jax.experimental import pallas as pl
from jax.experimental.pallas import tpu as pltpu
import functools

HQ = 64
KVH = 8
HD = 128
TURN = 64
MAXPAGES = 256


THETA = 500000.0
NEG_FILL = -1e30
ROPE_FACTOR = 8.0
LOW_FACTOR = 1.0
HIGH_FACTOR = 4.0
INITIAL_CONTEXT = 8192.0


def joined(x, axis, combine):
    everything = jax.tree.map(lambda part: lax.all_gather(part, axis), x)
    first = jax.tree.map(lambda part: part[0], everything)

    def step(k, so_far):
        return combine(so_far, jax.tree.map(lambda part: part[k], everything))

    return lax.fori_loop(1, lax.axis_size(axis), step, first)


def inverse_freq(width):
    steps_half = jnp.arange(width // 2, dtype=jnp.float32)
    base_freq = jnp.exp(-(steps_half * (2.0 / width)) * jnp.log(jnp.float32(THETA)))
    wavelength = 2.0 * math.pi / base_freq
    low_wave = INITIAL_CONTEXT / LOW_FACTOR
    high_wave = INITIAL_CONTEXT / HIGH_FACTOR
    smooth = (INITIAL_CONTEXT / wavelength - LOW_FACTOR) / (HIGH_FACTOR - LOW_FACTOR)
    blended = (1.0 - smooth) * base_freq / ROPE_FACTOR + smooth * base_freq
    scaled = jnp.where(wavelength > low_wave, base_freq / ROPE_FACTOR, blended)
    return jnp.where(wavelength < high_wave, base_freq, scaled)


def rotate(values, rot_angle):
    half_width = values.shape[-1] // 2
    first_half = values[..., :half_width]
    second_half = values[..., half_width:]
    cosine = jnp.cos(rot_angle)
    sine_part = jnp.sin(rot_angle)
    return jnp.concatenate(
        [
            first_half * cosine - second_half * sine_part,
            second_half * cosine + first_half * sine_part,
        ],
        axis=-1,
    )


def to_half(values):
    return values.astype(jnp.bfloat16)


def table_lookup(table, index):
    hits = index[..., None] == jnp.arange(table.shape[0], dtype=jnp.int32)
    return jnp.sum(jnp.where(hits, table, 0), axis=-1)


def page_positions(page_store, shards, capacity):
    store_of = page_store[:, 0]
    onehot = (store_of[:, None] == jnp.arange(shards, dtype=jnp.int32)[None, :]).astype(jnp.int32)
    ranks = jnp.sum((jnp.cumsum(onehot, axis=0) - onehot) * onehot, axis=1)
    return store_of * capacity + ranks


def slot_meta(page_store, lengths, offsets, shards, capacity, first_slot, slot_count, page_len):
    positions = page_positions(page_store, shards, capacity)
    wanted = first_slot + jnp.arange(slot_count, dtype=jnp.int32)
    matches = (positions[:, None] == wanted[None, :]).astype(jnp.int32)
    page_ids = jnp.sum(matches * jnp.arange(positions.shape[0], dtype=jnp.int32)[:, None], axis=0)
    filled = jnp.sum(matches, axis=0) > 0
    slot_sess = page_ids // MAXPAGES
    slot_page = page_ids % MAXPAGES
    key_pos = slot_page[:, None] * page_len + jnp.arange(page_len, dtype=jnp.int32)[None, :]
    key_ok = filled[:, None] & (key_pos < table_lookup(lengths, slot_sess)[:, None])
    key_sess = jnp.broadcast_to(slot_sess[:, None], (slot_count, page_len))
    key_off = jnp.broadcast_to(table_lookup(offsets, slot_sess)[:, None], (slot_count, page_len))
    return (key_sess.reshape(-1), key_ok.reshape(-1), key_off.reshape(-1))


def attend(query, key_rows, value_rows, allowed):
    score_scale = 1.0 / query.shape[-1] ** 0.5
    scores = (
        jnp.einsum("tkgd,nkd->tkgn", query, key_rows, preferred_element_type=jnp.float32)
        * score_scale
    )
    wide_mask = allowed[:, None, None, :]
    scores = jnp.where(wide_mask, scores, NEG_FILL)
    row_top = jnp.max(scores, axis=-1)
    weights = jnp.where(wide_mask, jnp.exp(scores - row_top[..., None]), 0.0)
    weight_sum = jnp.sum(weights, axis=-1)
    head_mix = jnp.einsum(
        "tkgn,nkd->tkgd",
        weights.astype(jnp.bfloat16),
        value_rows,
        preferred_element_type=jnp.float32,
    )
    return (row_top, weight_sum, head_mix)


def combine(first_part, second_part):
    new_top = jnp.maximum(first_part[0], second_part[0])
    first_factor = jnp.exp(first_part[0] - new_top)
    second_factor = jnp.exp(second_part[0] - new_top)
    summed = first_part[1] * first_factor + second_part[1] * second_factor
    mixed_sum = first_part[2] * first_factor[..., None] + second_part[2] * second_factor[..., None]
    return (new_top, summed, mixed_sum)


MASK_FILL = -3e30


def hist_kernel(kv0_ref, q_ref, k_ref, v_ref, bias_ref, cos_ref, sin_ref, acc_out, m_out, l_out, m_sc, l_sc, acc_sc, *, scale, blocks):
    j = pl.program_id(1)

    @pl.when(j == 0)
    def _():
        m_sc[...] = jnp.full(m_sc.shape, NEG_FILL, jnp.float32)
        l_sc[...] = jnp.zeros(l_sc.shape, jnp.float32)
        acc_sc[...] = jnp.zeros(acc_sc.shape, jnp.float32)

    pages, page_len, hd = k_ref.shape
    n = pages * page_len
    keys = k_ref[...].reshape(n, hd).astype(jnp.float32)
    vals = v_ref[...].reshape(n, hd)
    keys = (keys * cos_ref[...] + pltpu.roll(keys, hd // 2, 1) * sin_ref[...]).astype(jnp.bfloat16)
    scores = lax.dot_general(
        q_ref[0], keys, (((1,), (1,)), ((), ())), preferred_element_type=jnp.float32
    )
    scores = scores * scale + bias_ref[0]
    m_old = m_sc[...]
    m_new = jnp.maximum(m_old, jnp.max(scores, axis=1, keepdims=True))
    alpha = jnp.exp(m_old - m_new)
    weights = jnp.exp(scores - m_new)
    l_sc[...] = alpha * l_sc[...] + jnp.sum(weights, axis=1, keepdims=True)
    acc_sc[...] = alpha * acc_sc[...] + jnp.dot(
        weights.astype(jnp.bfloat16), vals, preferred_element_type=jnp.float32
    )
    m_sc[...] = m_new

    @pl.when(j == blocks - 1)
    def _():
        acc_out[0] = acc_sc[...]
        m_out[0] = m_sc[...]
        l_out[0] = l_sc[...]


def hist_attend(kv0, q_k, kv_local, bias, cos2, sin2, pb):
    heads, rows, hd = q_k.shape
    slots, page_len, width = kv_local.shape
    kv_heads = width // (2 * hd)
    blocks = slots // pb
    kernel = functools.partial(hist_kernel, scale=1.0 / hd ** 0.5, blocks=blocks)

    def head_of(h, kv0_ref):
        return (kv0_ref[0] + h) % kv_heads

    grid_spec = pltpu.PrefetchScalarGridSpec(
        num_scalar_prefetch=1,
        grid=(heads, blocks),
        in_specs=[
            pl.BlockSpec((1, rows, hd), lambda h, j, r: (h, 0, 0)),
            pl.BlockSpec((pb, page_len, hd), lambda h, j, r: (j, 0, 2 * head_of(h, r))),
            pl.BlockSpec((pb, page_len, hd), lambda h, j, r: (j, 0, 2 * head_of(h, r) + 1)),
            pl.BlockSpec((1, 1, pb * page_len), lambda h, j, r: (j, 0, 0)),
            pl.BlockSpec((1, hd), lambda h, j, r: (0, 0)),
            pl.BlockSpec((1, hd), lambda h, j, r: (0, 0)),
        ],
        out_specs=[
            pl.BlockSpec((1, rows, hd), lambda h, j, r: (h, 0, 0)),
            pl.BlockSpec((1, rows, 1), lambda h, j, r: (h, 0, 0)),
            pl.BlockSpec((1, rows, 1), lambda h, j, r: (h, 0, 0)),
        ],
        scratch_shapes=[
            pltpu.VMEM((rows, 1), jnp.float32),
            pltpu.VMEM((rows, 1), jnp.float32),
            pltpu.VMEM((rows, hd), jnp.float32),
        ],
    )
    return pl.pallas_call(
        kernel,
        grid_spec=grid_spec,
        out_shape=[
            jax.ShapeDtypeStruct((heads, rows, hd), jnp.float32),
            jax.ShapeDtypeStruct((heads, rows, 1), jnp.float32),
            jax.ShapeDtypeStruct((heads, rows, 1), jnp.float32),
        ],
        compiler_params=pltpu.CompilerParams(dimension_semantics=("arbitrary", "arbitrary")),
        cost_estimate=pl.CostEstimate(
            flops=4 * heads * rows * slots * page_len * hd,
            transcendentals=heads * rows * slots * page_len,
            bytes_accessed=heads * (slots * page_len * 2 * hd * 2 + rows * hd * 6),
        ),
    )(jnp.reshape(kv0, (1,)).astype(jnp.int32), q_k, kv_local, kv_local, bias, cos2, sin2)


def axis_reduce(x, axis, op):
    n = lax.axis_size(axis)
    d = 1
    while d < n:
        x = op(x, lax.ppermute(x, axis, perm=[(i, i ^ d) for i in range(n)]))
        d *= 2
    return x


def bit_scatter(block, axis):
    n = lax.axis_size(axis)
    idx = lax.axis_index(axis)
    d = 1
    while d < n:
        bit = (idx // d) % 2
        keep = lax.dynamic_index_in_dim(block, bit, 0, keepdims=False)
        send = lax.dynamic_index_in_dim(block, 1 - bit, 0, keepdims=False)
        block = keep + lax.ppermute(send, axis, perm=[(i, i ^ d) for i in range(n)])
        d *= 2
    return block


def bit_gather(x, axis):
    n = lax.axis_size(axis)
    idx = lax.axis_index(axis)
    dists = []
    d = n // 2
    while d >= 1:
        other = lax.ppermute(x, axis, perm=[(i, i ^ d) for i in range(n)])
        low = (idx // d) % 2 == 0
        x = jnp.stack([jnp.where(low, x, other), jnp.where(low, other, x)])
        dists.insert(0, d)
        d //= 2
    k = len(dists)
    order = sorted(range(k), key=lambda j: -dists[j])
    x = jnp.transpose(x, tuple(order) + tuple(range(k, x.ndim)))
    return x.reshape((n * x.shape[k],) + x.shape[k + 1 :])


def scatter_rows(x, axis):
    n = lax.axis_size(axis)
    if n & (n - 1):
        return lax.psum_scatter(x, axis, scatter_dimension=0, tiled=True)
    bits = n.bit_length() - 1
    x = x.reshape((2,) * bits + (x.shape[0] // n,) + x.shape[1:])
    x = jnp.transpose(x, tuple(range(bits - 1, -1, -1)) + tuple(range(bits, x.ndim)))
    return bit_scatter(x, axis)


def axis_sum(x, axis):
    n = lax.axis_size(axis)
    if n & (n - 1):
        return lax.psum(x, axis)
    return axis_reduce(x, axis, jnp.add)


def axis_max(x, axes):
    if any(lax.axis_size(a) & (lax.axis_size(a) - 1) for a in axes):
        return jnp.max(lax.all_gather(x, axes), axis=0)
    for a in axes:
        n = lax.axis_size(a)
        others = [lax.ppermute(x, a, perm=[(i, (i + k) % n) for i in range(n)]) for k in range(1, n)]
        for other in others:
            x = jnp.maximum(x, other)
    return x


def body(x_new, kv_pages, w_query, w_keyval, w_out, lengths, page_store, offsets):
    tensors = lax.axis_size("tensor")
    shards = lax.axis_size("store")
    tensor_idx = lax.axis_index("tensor")
    store_idx = lax.axis_index("store")
    tok_count = x_new.shape[0]
    assert tok_count == TURN and lengths.shape[0] == 1
    local_slots = kv_pages.shape[1]
    capacity = local_slots * tensors
    page_len = kv_pages.shape[2]
    kv_heads = kv_pages.shape[3] // (2 * HD)
    group_size = HQ // KVH
    local_heads = w_query.shape[1] // HD
    local_kv = max(1, local_heads // group_size)
    local_group = local_heads // local_kv
    freq_table = inverse_freq(HD)
    kv_first = tensor_idx * local_heads // group_size
    keyval_cols = lax.dynamic_slice_in_dim(w_keyval, kv_first * (2 * HD), local_kv * 2 * HD, 1)
    query_part = jnp.dot(x_new, w_query, preferred_element_type=jnp.float32)
    keyval_part = jnp.dot(x_new, keyval_cols, preferred_element_type=jnp.float32)
    keyval_sum = axis_sum(keyval_part, "store")
    keyval_local = keyval_sum.reshape(tok_count, local_kv, 2, HD)
    tok_ids = jnp.arange(tok_count, dtype=jnp.int32)
    tok_sess = tok_ids // TURN
    tok_pos = table_lookup(lengths, tok_sess) + tok_ids % TURN
    tok_angle = tok_pos.astype(jnp.float32)[:, None, None] * freq_table
    if local_heads % shards == 0 and not shards & (shards - 1):
        s_bits = shards.bit_length() - 1
        heads_major = jnp.transpose(query_part.reshape(tok_count, local_heads, HD), (1, 0, 2))
        block = heads_major.reshape((2,) * s_bits + (local_heads // shards, tok_count, HD))
        block = jnp.transpose(block, tuple(range(s_bits - 1, -1, -1)) + tuple(range(s_bits, s_bits + 3)))
        block = bit_scatter(block, "store")
        block = to_half(rotate(block, jnp.transpose(tok_angle, (1, 0, 2))))
        q_heads = bit_gather(block, "store")
        query_rot = jnp.transpose(q_heads, (1, 0, 2))
        q_all = bit_gather(block, "tensor")
        if tensors & (tensors - 1):
            q_all = None
        else:
            q_all = bit_gather(q_all, "store").reshape((shards, tensors) + block.shape)
            q_all = jnp.transpose(q_all, (1, 0, 2, 3, 4)).reshape((HQ,) + block.shape[1:])
    else:
        query_sum = axis_sum(query_part, "store")
        query_rot = to_half(rotate(query_sum.reshape(tok_count, local_heads, HD), tok_angle))
        q_heads = jnp.transpose(query_rot, (1, 0, 2))
        q_all = None
    key_new = to_half(rotate(keyval_local[:, :, 0], tok_angle))
    value_new = to_half(keyval_local[:, :, 1])

    first_slot = store_idx * capacity + tensor_idx * local_slots
    key_sess, key_ok, key_off = slot_meta(
        page_store, lengths, offsets, shards, capacity, first_slot, local_slots, page_len
    )
    pb = local_slots
    bias = jnp.where(key_ok, 0.0, MASK_FILL).astype(jnp.float32)
    bias = bias.reshape(local_slots // pb, 1, pb * page_len)
    hist_angle = offsets[0].astype(jnp.float32) * freq_table
    kv_local = kv_pages.reshape(local_slots, page_len, kv_pages.shape[3])
    cosine = jnp.cos(hist_angle)
    sine = jnp.sin(hist_angle)
    cos2 = jnp.concatenate([cosine, cosine])[None, :]
    sin2 = jnp.concatenate([-sine, sine])[None, :]

    if q_all is None and tensors & (tensors - 1):
        q_all = lax.all_gather(q_heads, "tensor", axis=0, tiled=True)
    elif q_all is None:
        q_all = bit_gather(q_heads, "tensor")
    q_k = q_all.reshape(kv_heads, group_size * tok_count, HD)
    if local_heads % group_size == 0:
        own = hist_attend(
            kv_first, q_heads.reshape(local_kv, group_size * tok_count, HD), kv_local, bias, cos2, sin2, pb
        )
        rest_first = kv_first + local_kv
        q_rest = lax.dynamic_slice_in_dim(
            jnp.concatenate([q_k, q_k], axis=0), rest_first % kv_heads, kv_heads - local_kv, 0
        )
        rest = hist_attend(rest_first % kv_heads, q_rest, kv_local, bias, cos2, sin2, pb)
        parts = []
        for first, second in zip(own, rest):
            rolled = jnp.concatenate([first, second, first, second], axis=0)
            parts.append(lax.dynamic_slice_in_dim(rolled, kv_heads - kv_first, kv_heads, 0))
        acc, top, total = parts
    else:
        acc, top, total = hist_attend(jnp.int32(0), q_k, kv_local, bias, cos2, sin2, pb)
    acc = acc.reshape(HQ, tok_count, HD)
    top = top.reshape(HQ, tok_count)
    total = total.reshape(HQ, tok_count)

    glob_top = axis_max(top, ("store", "tensor"))
    factor = jnp.exp(top - glob_top)
    packed = jnp.concatenate(
        [(acc * factor[..., None]).reshape(HQ, tok_count * HD), total * factor], axis=1
    )
    new_allowed = (tok_sess[:, None] == tok_sess[None, :]) & (tok_ids[None, :] <= tok_ids[:, None])
    chunk_heads = HQ // (tensors * shards)
    if (
        HQ % (tensors * shards) == 0
        and group_size % chunk_heads == 0
        and not shards & (shards - 1)
        and not tensors & (tensors - 1)
    ):
        width = packed.shape[1]
        s_bits = shards.bit_length() - 1
        t_bits = tensors.bit_length() - 1
        block = packed.reshape((2,) * t_bits + (2,) * s_bits + (chunk_heads, width))
        order = tuple(range(t_bits + s_bits - 1, t_bits - 1, -1)) + tuple(range(t_bits - 1, -1, -1))
        block = jnp.transpose(block, order + (t_bits + s_bits, t_bits + s_bits + 1))
        block = bit_scatter(block, "store")
        block = bit_scatter(block, "tensor")
        acc = block[:, : tok_count * HD].reshape(chunk_heads, tok_count, HD)
        total = block[:, tok_count * HD :]
        chunk_first = (tensor_idx * shards + store_idx) * chunk_heads
        loc_top = lax.dynamic_slice_in_dim(glob_top, chunk_first, chunk_heads, 0)
        hist_part = (jnp.transpose(loc_top), jnp.transpose(total), jnp.transpose(acc, (1, 0, 2)))
        in_group = store_idx * chunk_heads
        query_chunk = lax.dynamic_slice_in_dim(query_rot, in_group, chunk_heads, 1)
        kv_idx = in_group // group_size
        key_chunk = lax.dynamic_slice_in_dim(key_new, kv_idx, 1, 1)
        value_chunk = lax.dynamic_slice_in_dim(value_new, kv_idx, 1, 1)
        new_part = attend(
            query_chunk.reshape(tok_count, 1, chunk_heads, HD), key_chunk, value_chunk, new_allowed
        )
        new_flat = (
            new_part[0].reshape(tok_count, chunk_heads),
            new_part[1].reshape(tok_count, chunk_heads),
            new_part[2].reshape(tok_count, chunk_heads, HD),
        )
        combined = combine(hist_part, new_flat)
        attended = (
            (combined[2] / combined[1][..., None])
            .reshape(tok_count, chunk_heads * HD)
            .astype(jnp.bfloat16)
        )
        attended = lax.all_gather(attended, "store", axis=1, tiled=True)
    else:
        packed = lax.psum_scatter(packed, "tensor", scatter_dimension=0, tiled=True)
        packed = axis_sum(packed, "store")
        acc = packed[:, : tok_count * HD].reshape(local_heads, tok_count, HD)
        total = packed[:, tok_count * HD :]
        loc_top = lax.dynamic_slice_in_dim(glob_top, tensor_idx * local_heads, local_heads, 0)
        hist_part = (
            jnp.transpose(loc_top),
            jnp.transpose(total),
            jnp.transpose(acc, (1, 0, 2)),
        )

        query_local = query_rot.reshape(tok_count, local_kv, local_group, HD)
        new_part = attend(query_local, key_new, value_new, new_allowed)
        new_flat = (
            new_part[0].reshape(tok_count, local_heads),
            new_part[1].reshape(tok_count, local_heads),
            new_part[2].reshape(tok_count, local_heads, HD),
        )
        combined = combine(hist_part, new_flat)
        attended = (
            (combined[2] / combined[1][..., None])
            .reshape(tok_count, local_heads * HD)
            .astype(jnp.bfloat16)
        )
    result = scatter_rows(jnp.dot(attended, w_out, preferred_element_type=jnp.float32), "tensor")
    return result.astype(jnp.bfloat16)


def solution(mesh):
    in_specs = (
        P("groups", "store"),
        P(("groups", "store"), "tensor", None, None),
        P("store", "tensor"),
        P("store", None),
        P("tensor", "store"),
        P("groups"),
        P("groups", None),
        P("groups"),
    )
    out_specs = P(("groups", "tensor"), "store")
    return jax.shard_map(body, mesh=mesh, in_specs=in_specs, out_specs=out_specs, check_vma=False)
```

```python
import math

import jax
import jax.numpy as jnp
import numpy as np
from jax import lax
from jax.sharding import PartitionSpec as P
from jax.experimental import pallas as pl
from jax.experimental.pallas import tpu as pltpu
import functools

HQ = 64
KVH = 8
HD = 128
TURN = 64
MAXPAGES = 256


THETA = 500000.0
NEG_FILL = -1e30
ROPE_FACTOR = 8.0
LOW_FACTOR = 1.0
HIGH_FACTOR = 4.0
INITIAL_CONTEXT = 8192.0


def joined(x, axis, combine):
    everything = jax.tree.map(lambda part: lax.all_gather(part, axis), x)
    first = jax.tree.map(lambda part: part[0], everything)

    def step(k, so_far):
        return combine(so_far, jax.tree.map(lambda part: part[k], everything))

    return lax.fori_loop(1, lax.axis_size(axis), step, first)


def inverse_freq(width):
    steps_half = jnp.arange(width // 2, dtype=jnp.float32)
    base_freq = jnp.exp(-(steps_half * (2.0 / width)) * jnp.log(jnp.float32(THETA)))
    wavelength = 2.0 * math.pi / base_freq
    low_wave = INITIAL_CONTEXT / LOW_FACTOR
    high_wave = INITIAL_CONTEXT / HIGH_FACTOR
    smooth = (INITIAL_CONTEXT / wavelength - LOW_FACTOR) / (HIGH_FACTOR - LOW_FACTOR)
    blended = (1.0 - smooth) * base_freq / ROPE_FACTOR + smooth * base_freq
    scaled = jnp.where(wavelength > low_wave, base_freq / ROPE_FACTOR, blended)
    return jnp.where(wavelength < high_wave, base_freq, scaled)


def rotate(values, rot_angle):
    half_width = values.shape[-1] // 2
    first_half = values[..., :half_width]
    second_half = values[..., half_width:]
    cosine = jnp.cos(rot_angle)
    sine_part = jnp.sin(rot_angle)
    return jnp.concatenate(
        [
            first_half * cosine - second_half * sine_part,
            second_half * cosine + first_half * sine_part,
        ],
        axis=-1,
    )


def to_half(values):
    return values.astype(jnp.bfloat16)


def table_lookup(table, index):
    hits = index[..., None] == jnp.arange(table.shape[0], dtype=jnp.int32)
    return jnp.sum(jnp.where(hits, table, 0), axis=-1)


def page_positions(page_store, shards, capacity):
    store_of = page_store[:, 0]
    onehot = (store_of[:, None] == jnp.arange(shards, dtype=jnp.int32)[None, :]).astype(jnp.int32)
    ranks = jnp.sum((jnp.cumsum(onehot, axis=0) - onehot) * onehot, axis=1)
    return store_of * capacity + ranks


def slot_meta(page_store, lengths, offsets, shards, capacity, first_slot, slot_count, page_len):
    positions = page_positions(page_store, shards, capacity)
    wanted = first_slot + jnp.arange(slot_count, dtype=jnp.int32)
    matches = (positions[:, None] == wanted[None, :]).astype(jnp.int32)
    page_ids = jnp.sum(matches * jnp.arange(positions.shape[0], dtype=jnp.int32)[:, None], axis=0)
    filled = jnp.sum(matches, axis=0) > 0
    slot_sess = page_ids // MAXPAGES
    slot_page = page_ids % MAXPAGES
    key_pos = slot_page[:, None] * page_len + jnp.arange(page_len, dtype=jnp.int32)[None, :]
    key_ok = filled[:, None] & (key_pos < table_lookup(lengths, slot_sess)[:, None])
    key_sess = jnp.broadcast_to(slot_sess[:, None], (slot_count, page_len))
    key_off = jnp.broadcast_to(table_lookup(offsets, slot_sess)[:, None], (slot_count, page_len))
    return (key_sess.reshape(-1), key_ok.reshape(-1), key_off.reshape(-1))


def attend(query, key_rows, value_rows, allowed):
    score_scale = 1.0 / query.shape[-1] ** 0.5
    scores = (
        jnp.einsum("tkgd,nkd->tkgn", query, key_rows, preferred_element_type=jnp.float32)
        * score_scale
    )
    wide_mask = allowed[:, None, None, :]
    scores = jnp.where(wide_mask, scores, NEG_FILL)
    row_top = jnp.max(scores, axis=-1)
    weights = jnp.where(wide_mask, jnp.exp(scores - row_top[..., None]), 0.0)
    weight_sum = jnp.sum(weights, axis=-1)
    head_mix = jnp.einsum(
        "tkgn,nkd->tkgd",
        weights.astype(jnp.bfloat16),
        value_rows,
        preferred_element_type=jnp.float32,
    )
    return (row_top, weight_sum, head_mix)


def combine(first_part, second_part):
    new_top = jnp.maximum(first_part[0], second_part[0])
    first_factor = jnp.exp(first_part[0] - new_top)
    second_factor = jnp.exp(second_part[0] - new_top)
    summed = first_part[1] * first_factor + second_part[1] * second_factor
    mixed_sum = first_part[2] * first_factor[..., None] + second_part[2] * second_factor[..., None]
    return (new_top, summed, mixed_sum)


MASK_FILL = -3e30


def hist_kernel(kv0_ref, q_ref, k_ref, v_ref, bias_ref, cos_ref, sin_ref, acc_out, m_out, l_out, m_sc, l_sc, acc_sc, *, scale, blocks):
    j = pl.program_id(1)

    @pl.when(j == 0)
    def _():
        m_sc[...] = jnp.full(m_sc.shape, NEG_FILL, jnp.float32)
        l_sc[...] = jnp.zeros(l_sc.shape, jnp.float32)
        acc_sc[...] = jnp.zeros(acc_sc.shape, jnp.float32)

    pages, page_len, hd = k_ref.shape
    n = pages * page_len
    keys = k_ref[...].reshape(n, hd).astype(jnp.float32)
    vals = v_ref[...].reshape(n, hd)
    keys = (keys * cos_ref[...] + pltpu.roll(keys, hd // 2, 1) * sin_ref[...]).astype(jnp.bfloat16)
    scores = lax.dot_general(
        q_ref[0], keys, (((1,), (1,)), ((), ())), preferred_element_type=jnp.float32
    )
    scores = scores * scale + bias_ref[0]
    m_old = m_sc[...]
    m_new = jnp.maximum(m_old, jnp.max(scores, axis=1, keepdims=True))
    alpha = jnp.exp(m_old - m_new)
    weights = jnp.exp(scores - m_new)
    l_sc[...] = alpha * l_sc[...] + jnp.sum(weights, axis=1, keepdims=True)
    acc_sc[...] = alpha * acc_sc[...] + jnp.dot(
        weights.astype(jnp.bfloat16), vals, preferred_element_type=jnp.float32
    )
    m_sc[...] = m_new

    @pl.when(j == blocks - 1)
    def _():
        acc_out[0] = acc_sc[...]
        m_out[0] = m_sc[...]
        l_out[0] = l_sc[...]


def hist_attend(kv0, q_k, kv_local, bias, cos2, sin2, pb):
    heads, rows, hd = q_k.shape
    slots, page_len, width = kv_local.shape
    kv_heads = width // (2 * hd)
    blocks = slots // pb
    kernel = functools.partial(hist_kernel, scale=1.0 / hd ** 0.5, blocks=blocks)

    def head_of(h, kv0_ref):
        return (kv0_ref[0] + h) % kv_heads

    grid_spec = pltpu.PrefetchScalarGridSpec(
        num_scalar_prefetch=1,
        grid=(heads, blocks),
        in_specs=[
            pl.BlockSpec((1, rows, hd), lambda h, j, r: (h, 0, 0)),
            pl.BlockSpec((pb, page_len, hd), lambda h, j, r: (j, 0, 2 * head_of(h, r))),
            pl.BlockSpec((pb, page_len, hd), lambda h, j, r: (j, 0, 2 * head_of(h, r) + 1)),
            pl.BlockSpec((1, 1, pb * page_len), lambda h, j, r: (j, 0, 0)),
            pl.BlockSpec((1, hd), lambda h, j, r: (0, 0)),
            pl.BlockSpec((1, hd), lambda h, j, r: (0, 0)),
        ],
        out_specs=[
            pl.BlockSpec((1, rows, hd), lambda h, j, r: (h, 0, 0)),
            pl.BlockSpec((1, rows, 1), lambda h, j, r: (h, 0, 0)),
            pl.BlockSpec((1, rows, 1), lambda h, j, r: (h, 0, 0)),
        ],
        scratch_shapes=[
            pltpu.VMEM((rows, 1), jnp.float32),
            pltpu.VMEM((rows, 1), jnp.float32),
            pltpu.VMEM((rows, hd), jnp.float32),
        ],
    )
    return pl.pallas_call(
        kernel,
        grid_spec=grid_spec,
        out_shape=[
            jax.ShapeDtypeStruct((heads, rows, hd), jnp.float32),
            jax.ShapeDtypeStruct((heads, rows, 1), jnp.float32),
            jax.ShapeDtypeStruct((heads, rows, 1), jnp.float32),
        ],
        compiler_params=pltpu.CompilerParams(dimension_semantics=("arbitrary", "arbitrary")),
        cost_estimate=pl.CostEstimate(
            flops=4 * heads * rows * slots * page_len * hd,
            transcendentals=heads * rows * slots * page_len,
            bytes_accessed=heads * (slots * page_len * 2 * hd * 2 + rows * hd * 6),
        ),
    )(jnp.reshape(kv0, (1,)).astype(jnp.int32), q_k, kv_local, kv_local, bias, cos2, sin2)


def axis_reduce(x, axis, op):
    n = lax.axis_size(axis)
    d = 1
    while d < n:
        x = op(x, lax.ppermute(x, axis, perm=[(i, i ^ d) for i in range(n)]))
        d *= 2
    return x


def bit_scatter(block, axis):
    n = lax.axis_size(axis)
    idx = lax.axis_index(axis)
    d = 1
    while d < n:
        bit = (idx // d) % 2
        keep = lax.dynamic_index_in_dim(block, bit, 0, keepdims=False)
        send = lax.dynamic_index_in_dim(block, 1 - bit, 0, keepdims=False)
        block = keep + lax.ppermute(send, axis, perm=[(i, i ^ d) for i in range(n)])
        d *= 2
    return block


def bit_gather(x, axis):
    n = lax.axis_size(axis)
    idx = lax.axis_index(axis)
    dists = []
    d = n // 2
    while d >= 1:
        other = lax.ppermute(x, axis, perm=[(i, i ^ d) for i in range(n)])
        low = (idx // d) % 2 == 0
        x = jnp.stack([jnp.where(low, x, other), jnp.where(low, other, x)])
        dists.insert(0, d)
        d //= 2
    k = len(dists)
    order = sorted(range(k), key=lambda j: -dists[j])
    x = jnp.transpose(x, tuple(order) + tuple(range(k, x.ndim)))
    return x.reshape((n * x.shape[k],) + x.shape[k + 1 :])


def scatter_rows(x, axis):
    n = lax.axis_size(axis)
    if n & (n - 1):
        return lax.psum_scatter(x, axis, scatter_dimension=0, tiled=True)
    bits = n.bit_length() - 1
    x = x.reshape((2,) * bits + (x.shape[0] // n,) + x.shape[1:])
    x = jnp.transpose(x, tuple(range(bits - 1, -1, -1)) + tuple(range(bits, x.ndim)))
    return bit_scatter(x, axis)


def direct_scatter(x, axis):
    n = lax.axis_size(axis)
    idx = lax.axis_index(axis)
    blocks = x.reshape((n, x.shape[0] // n) + x.shape[1:])
    total = lax.dynamic_index_in_dim(blocks, idx, 0, keepdims=False)
    for k in range(1, n):
        piece = lax.dynamic_index_in_dim(blocks, (idx + k) % n, 0, keepdims=False)
        total = total + lax.ppermute(piece, axis, perm=[(i, (i + k) % n) for i in range(n)])
    return total


def axis_sum(x, axis):
    n = lax.axis_size(axis)
    if n & (n - 1):
        return lax.psum(x, axis)
    return axis_reduce(x, axis, jnp.add)


def axis_max(x, axes):
    if any(lax.axis_size(a) & (lax.axis_size(a) - 1) for a in axes):
        return jnp.max(lax.all_gather(x, axes), axis=0)
    for a in axes:
        n = lax.axis_size(a)
        others = [lax.ppermute(x, a, perm=[(i, (i + k) % n) for i in range(n)]) for k in range(1, n)]
        for other in others:
            x = jnp.maximum(x, other)
    return x


def body(x_new, kv_pages, w_query, w_keyval, w_out, lengths, page_store, offsets):
    tensors = lax.axis_size("tensor")
    shards = lax.axis_size("store")
    tensor_idx = lax.axis_index("tensor")
    store_idx = lax.axis_index("store")
    tok_count = x_new.shape[0]
    assert tok_count == TURN and lengths.shape[0] == 1
    local_slots = kv_pages.shape[1]
    capacity = local_slots * tensors
    page_len = kv_pages.shape[2]
    kv_heads = kv_pages.shape[3] // (2 * HD)
    group_size = HQ // KVH
    local_heads = w_query.shape[1] // HD
    local_kv = max(1, local_heads // group_size)
    local_group = local_heads // local_kv
    freq_table = inverse_freq(HD)
    kv_first = tensor_idx * local_heads // group_size
    keyval_cols = lax.dynamic_slice_in_dim(w_keyval, kv_first * (2 * HD), local_kv * 2 * HD, 1)
    query_part = jnp.dot(x_new, w_query, preferred_element_type=jnp.float32)
    keyval_part = jnp.dot(x_new, keyval_cols, preferred_element_type=jnp.float32)
    keyval_sum = axis_sum(keyval_part, "store")
    keyval_local = keyval_sum.reshape(tok_count, local_kv, 2, HD)
    tok_ids = jnp.arange(tok_count, dtype=jnp.int32)
    tok_sess = tok_ids // TURN
    tok_pos = table_lookup(lengths, tok_sess) + tok_ids % TURN
    tok_angle = tok_pos.astype(jnp.float32)[:, None, None] * freq_table
    if local_heads % shards == 0 and not shards & (shards - 1):
        s_bits = shards.bit_length() - 1
        heads_major = jnp.transpose(query_part.reshape(tok_count, local_heads, HD), (1, 0, 2))
        block = heads_major.reshape((2,) * s_bits + (local_heads // shards, tok_count, HD))
        block = jnp.transpose(block, tuple(range(s_bits - 1, -1, -1)) + tuple(range(s_bits, s_bits + 3)))
        block = bit_scatter(block, "store")
        block = to_half(rotate(block, jnp.transpose(tok_angle, (1, 0, 2))))
        q_heads = bit_gather(block, "store")
        query_rot = jnp.transpose(q_heads, (1, 0, 2))
        q_all = bit_gather(block, "tensor")
        if tensors & (tensors - 1):
            q_all = None
        else:
            q_all = bit_gather(q_all, "store").reshape((shards, tensors) + block.shape)
            q_all = jnp.transpose(q_all, (1, 0, 2, 3, 4)).reshape((HQ,) + block.shape[1:])
    else:
        query_sum = axis_sum(query_part, "store")
        query_rot = to_half(rotate(query_sum.reshape(tok_count, local_heads, HD), tok_angle))
        q_heads = jnp.transpose(query_rot, (1, 0, 2))
        q_all = None
    key_new = to_half(rotate(keyval_local[:, :, 0], tok_angle))
    value_new = to_half(keyval_local[:, :, 1])

    first_slot = store_idx * capacity + tensor_idx * local_slots
    key_sess, key_ok, key_off = slot_meta(
        page_store, lengths, offsets, shards, capacity, first_slot, local_slots, page_len
    )
    pb = local_slots
    bias = jnp.where(key_ok, 0.0, MASK_FILL).astype(jnp.float32)
    bias = bias.reshape(local_slots // pb, 1, pb * page_len)
    hist_angle = offsets[0].astype(jnp.float32) * freq_table
    kv_local = kv_pages.reshape(local_slots, page_len, kv_pages.shape[3])
    cosine = jnp.cos(hist_angle)
    sine = jnp.sin(hist_angle)
    cos2 = jnp.concatenate([cosine, cosine])[None, :]
    sin2 = jnp.concatenate([-sine, sine])[None, :]

    if q_all is None and tensors & (tensors - 1):
        q_all = lax.all_gather(q_heads, "tensor", axis=0, tiled=True)
    elif q_all is None:
        q_all = bit_gather(q_heads, "tensor")
    q_k = q_all.reshape(kv_heads, group_size * tok_count, HD)
    if local_heads % group_size == 0:
        own = hist_attend(
            kv_first, q_heads.reshape(local_kv, group_size * tok_count, HD), kv_local, bias, cos2, sin2, pb
        )
        rest_first = kv_first + local_kv
        q_rest = lax.dynamic_slice_in_dim(
            jnp.concatenate([q_k, q_k], axis=0), rest_first % kv_heads, kv_heads - local_kv, 0
        )
        rest = hist_attend(rest_first % kv_heads, q_rest, kv_local, bias, cos2, sin2, pb)
        parts = []
        for first, second in zip(own, rest):
            rolled = jnp.concatenate([first, second, first, second], axis=0)
            parts.append(lax.dynamic_slice_in_dim(rolled, kv_heads - kv_first, kv_heads, 0))
        acc, top, total = parts
    else:
        acc, top, total = hist_attend(jnp.int32(0), q_k, kv_local, bias, cos2, sin2, pb)
    acc = acc.reshape(HQ, tok_count, HD)
    top = top.reshape(HQ, tok_count)
    total = total.reshape(HQ, tok_count)

    glob_top = axis_max(top, ("store", "tensor"))
    factor = jnp.exp(top - glob_top)
    packed = jnp.concatenate(
        [(acc * factor[..., None]).reshape(HQ, tok_count * HD), total * factor], axis=1
    )
    new_allowed = (tok_sess[:, None] == tok_sess[None, :]) & (tok_ids[None, :] <= tok_ids[:, None])
    chunk_heads = HQ // (tensors * shards)
    if (
        HQ % (tensors * shards) == 0
        and group_size % chunk_heads == 0
        and not shards & (shards - 1)
        and not tensors & (tensors - 1)
    ):
        width = packed.shape[1]
        s_bits = shards.bit_length() - 1
        t_bits = tensors.bit_length() - 1
        block = packed.reshape((2,) * t_bits + (2,) * s_bits + (chunk_heads, width))
        order = tuple(range(t_bits + s_bits - 1, t_bits - 1, -1)) + tuple(range(t_bits - 1, -1, -1))
        block = jnp.transpose(block, order + (t_bits + s_bits, t_bits + s_bits + 1))
        block = bit_scatter(block, "store")
        block = bit_scatter(block, "tensor")
        acc = block[:, : tok_count * HD].reshape(chunk_heads, tok_count, HD)
        total = block[:, tok_count * HD :]
        chunk_first = (tensor_idx * shards + store_idx) * chunk_heads
        loc_top = lax.dynamic_slice_in_dim(glob_top, chunk_first, chunk_heads, 0)
        hist_part = (jnp.transpose(loc_top), jnp.transpose(total), jnp.transpose(acc, (1, 0, 2)))
        in_group = store_idx * chunk_heads
        query_chunk = lax.dynamic_slice_in_dim(query_rot, in_group, chunk_heads, 1)
        kv_idx = in_group // group_size
        key_chunk = lax.dynamic_slice_in_dim(key_new, kv_idx, 1, 1)
        value_chunk = lax.dynamic_slice_in_dim(value_new, kv_idx, 1, 1)
        new_part = attend(
            query_chunk.reshape(tok_count, 1, chunk_heads, HD), key_chunk, value_chunk, new_allowed
        )
        new_flat = (
            new_part[0].reshape(tok_count, chunk_heads),
            new_part[1].reshape(tok_count, chunk_heads),
            new_part[2].reshape(tok_count, chunk_heads, HD),
        )
        combined = combine(hist_part, new_flat)
        attended = (
            (combined[2] / combined[1][..., None])
            .reshape(tok_count, chunk_heads * HD)
            .astype(jnp.bfloat16)
        )
        attended = lax.all_gather(attended, "store", axis=1, tiled=True)
    else:
        packed = lax.psum_scatter(packed, "tensor", scatter_dimension=0, tiled=True)
        packed = axis_sum(packed, "store")
        acc = packed[:, : tok_count * HD].reshape(local_heads, tok_count, HD)
        total = packed[:, tok_count * HD :]
        loc_top = lax.dynamic_slice_in_dim(glob_top, tensor_idx * local_heads, local_heads, 0)
        hist_part = (
            jnp.transpose(loc_top),
            jnp.transpose(total),
            jnp.transpose(acc, (1, 0, 2)),
        )

        query_local = query_rot.reshape(tok_count, local_kv, local_group, HD)
        new_part = attend(query_local, key_new, value_new, new_allowed)
        new_flat = (
            new_part[0].reshape(tok_count, local_heads),
            new_part[1].reshape(tok_count, local_heads),
            new_part[2].reshape(tok_count, local_heads, HD),
        )
        combined = combine(hist_part, new_flat)
        attended = (
            (combined[2] / combined[1][..., None])
            .reshape(tok_count, local_heads * HD)
            .astype(jnp.bfloat16)
        )
    result = direct_scatter(jnp.dot(attended, w_out, preferred_element_type=jnp.float32), "tensor")
    return result.astype(jnp.bfloat16)


def solution(mesh):
    in_specs = (
        P("groups", "store"),
        P(("groups", "store"), "tensor", None, None),
        P("store", "tensor"),
        P("store", None),
        P("tensor", "store"),
        P("groups"),
        P("groups", None),
        P("groups"),
    )
    out_specs = P(("groups", "tensor"), "store")
    return jax.shard_map(body, mesh=mesh, in_specs=in_specs, out_specs=out_specs, check_vma=False)
```

```python
import math

import jax
import jax.numpy as jnp
import numpy as np
from jax import lax
from jax.sharding import PartitionSpec as P
from jax.experimental import pallas as pl
from jax.experimental.pallas import tpu as pltpu
import functools

HQ = 64
KVH = 8
HD = 128
TURN = 64
MAXPAGES = 256


THETA = 500000.0
NEG_FILL = -1e30
ROPE_FACTOR = 8.0
LOW_FACTOR = 1.0
HIGH_FACTOR = 4.0
INITIAL_CONTEXT = 8192.0


def joined(x, axis, combine):
    everything = jax.tree.map(lambda part: lax.all_gather(part, axis), x)
    first = jax.tree.map(lambda part: part[0], everything)

    def step(k, so_far):
        return combine(so_far, jax.tree.map(lambda part: part[k], everything))

    return lax.fori_loop(1, lax.axis_size(axis), step, first)


def inverse_freq(width):
    steps_half = jnp.arange(width // 2, dtype=jnp.float32)
    base_freq = jnp.exp(-(steps_half * (2.0 / width)) * jnp.log(jnp.float32(THETA)))
    wavelength = 2.0 * math.pi / base_freq
    low_wave = INITIAL_CONTEXT / LOW_FACTOR
    high_wave = INITIAL_CONTEXT / HIGH_FACTOR
    smooth = (INITIAL_CONTEXT / wavelength - LOW_FACTOR) / (HIGH_FACTOR - LOW_FACTOR)
    blended = (1.0 - smooth) * base_freq / ROPE_FACTOR + smooth * base_freq
    scaled = jnp.where(wavelength > low_wave, base_freq / ROPE_FACTOR, blended)
    return jnp.where(wavelength < high_wave, base_freq, scaled)


def rotate(values, rot_angle):
    half_width = values.shape[-1] // 2
    first_half = values[..., :half_width]
    second_half = values[..., half_width:]
    cosine = jnp.cos(rot_angle)
    sine_part = jnp.sin(rot_angle)
    return jnp.concatenate(
        [
            first_half * cosine - second_half * sine_part,
            second_half * cosine + first_half * sine_part,
        ],
        axis=-1,
    )


def to_half(values):
    return values.astype(jnp.bfloat16)


def table_lookup(table, index):
    hits = index[..., None] == jnp.arange(table.shape[0], dtype=jnp.int32)
    return jnp.sum(jnp.where(hits, table, 0), axis=-1)


def page_positions(page_store, shards, capacity):
    store_of = page_store[:, 0]
    onehot = (store_of[:, None] == jnp.arange(shards, dtype=jnp.int32)[None, :]).astype(jnp.int32)
    ranks = jnp.sum((jnp.cumsum(onehot, axis=0) - onehot) * onehot, axis=1)
    return store_of * capacity + ranks


def slot_meta(page_store, lengths, offsets, shards, capacity, first_slot, slot_count, page_len):
    positions = page_positions(page_store, shards, capacity)
    wanted = first_slot + jnp.arange(slot_count, dtype=jnp.int32)
    matches = (positions[:, None] == wanted[None, :]).astype(jnp.int32)
    page_ids = jnp.sum(matches * jnp.arange(positions.shape[0], dtype=jnp.int32)[:, None], axis=0)
    filled = jnp.sum(matches, axis=0) > 0
    slot_sess = page_ids // MAXPAGES
    slot_page = page_ids % MAXPAGES
    key_pos = slot_page[:, None] * page_len + jnp.arange(page_len, dtype=jnp.int32)[None, :]
    key_ok = filled[:, None] & (key_pos < table_lookup(lengths, slot_sess)[:, None])
    key_sess = jnp.broadcast_to(slot_sess[:, None], (slot_count, page_len))
    key_off = jnp.broadcast_to(table_lookup(offsets, slot_sess)[:, None], (slot_count, page_len))
    return (key_sess.reshape(-1), key_ok.reshape(-1), key_off.reshape(-1))


def attend(query, key_rows, value_rows, allowed):
    score_scale = 1.0 / query.shape[-1] ** 0.5
    scores = (
        jnp.einsum("tkgd,nkd->tkgn", query, key_rows, preferred_element_type=jnp.float32)
        * score_scale
    )
    wide_mask = allowed[:, None, None, :]
    scores = jnp.where(wide_mask, scores, NEG_FILL)
    row_top = jnp.max(scores, axis=-1)
    weights = jnp.where(wide_mask, jnp.exp(scores - row_top[..., None]), 0.0)
    weight_sum = jnp.sum(weights, axis=-1)
    head_mix = jnp.einsum(
        "tkgn,nkd->tkgd",
        weights.astype(jnp.bfloat16),
        value_rows,
        preferred_element_type=jnp.float32,
    )
    return (row_top, weight_sum, head_mix)


def combine(first_part, second_part):
    new_top = jnp.maximum(first_part[0], second_part[0])
    first_factor = jnp.exp(first_part[0] - new_top)
    second_factor = jnp.exp(second_part[0] - new_top)
    summed = first_part[1] * first_factor + second_part[1] * second_factor
    mixed_sum = first_part[2] * first_factor[..., None] + second_part[2] * second_factor[..., None]
    return (new_top, summed, mixed_sum)


MASK_FILL = -3e30


def hist_kernel(kv0_ref, q_ref, k_ref, v_ref, bias_ref, cos_ref, sin_ref, acc_out, m_out, l_out, m_sc, l_sc, acc_sc, *, scale, blocks):
    j = pl.program_id(1)

    @pl.when(j == 0)
    def _():
        m_sc[...] = jnp.full(m_sc.shape, NEG_FILL, jnp.float32)
        l_sc[...] = jnp.zeros(l_sc.shape, jnp.float32)
        acc_sc[...] = jnp.zeros(acc_sc.shape, jnp.float32)

    pages, page_len, hd = k_ref.shape
    n = pages * page_len
    keys = k_ref[...].reshape(n, hd).astype(jnp.float32)
    vals = v_ref[...].reshape(n, hd)
    keys = (keys * cos_ref[...] + pltpu.roll(keys, hd // 2, 1) * sin_ref[...]).astype(jnp.bfloat16)
    scores = lax.dot_general(
        q_ref[0], keys, (((1,), (1,)), ((), ())), preferred_element_type=jnp.float32
    )
    scores = scores * scale + bias_ref[0]
    m_old = m_sc[...]
    m_new = jnp.maximum(m_old, jnp.max(scores, axis=1, keepdims=True))
    alpha = jnp.exp(m_old - m_new)
    weights = jnp.exp(scores - m_new)
    l_sc[...] = alpha * l_sc[...] + jnp.sum(weights, axis=1, keepdims=True)
    acc_sc[...] = alpha * acc_sc[...] + jnp.dot(
        weights.astype(jnp.bfloat16), vals, preferred_element_type=jnp.float32
    )
    m_sc[...] = m_new

    @pl.when(j == blocks - 1)
    def _():
        acc_out[0] = acc_sc[...]
        m_out[0] = m_sc[...]
        l_out[0] = l_sc[...]


def hist_attend(kv0, q_k, kv_local, bias, cos2, sin2, pb):
    heads, rows, hd = q_k.shape
    slots, page_len, width = kv_local.shape
    kv_heads = width // (2 * hd)
    blocks = slots // pb
    kernel = functools.partial(hist_kernel, scale=1.0 / hd ** 0.5, blocks=blocks)

    def head_of(h, kv0_ref):
        return (kv0_ref[0] + h) % kv_heads

    grid_spec = pltpu.PrefetchScalarGridSpec(
        num_scalar_prefetch=1,
        grid=(heads, blocks),
        in_specs=[
            pl.BlockSpec((1, rows, hd), lambda h, j, r: (h, 0, 0)),
            pl.BlockSpec((pb, page_len, hd), lambda h, j, r: (j, 0, 2 * head_of(h, r))),
            pl.BlockSpec((pb, page_len, hd), lambda h, j, r: (j, 0, 2 * head_of(h, r) + 1)),
            pl.BlockSpec((1, 1, pb * page_len), lambda h, j, r: (j, 0, 0)),
            pl.BlockSpec((1, hd), lambda h, j, r: (0, 0)),
            pl.BlockSpec((1, hd), lambda h, j, r: (0, 0)),
        ],
        out_specs=[
            pl.BlockSpec((1, rows, hd), lambda h, j, r: (h, 0, 0)),
            pl.BlockSpec((1, rows, 1), lambda h, j, r: (h, 0, 0)),
            pl.BlockSpec((1, rows, 1), lambda h, j, r: (h, 0, 0)),
        ],
        scratch_shapes=[
            pltpu.VMEM((rows, 1), jnp.float32),
            pltpu.VMEM((rows, 1), jnp.float32),
            pltpu.VMEM((rows, hd), jnp.float32),
        ],
    )
    return pl.pallas_call(
        kernel,
        grid_spec=grid_spec,
        out_shape=[
            jax.ShapeDtypeStruct((heads, rows, hd), jnp.float32),
            jax.ShapeDtypeStruct((heads, rows, 1), jnp.float32),
            jax.ShapeDtypeStruct((heads, rows, 1), jnp.float32),
        ],
        compiler_params=pltpu.CompilerParams(dimension_semantics=("arbitrary", "arbitrary")),
        cost_estimate=pl.CostEstimate(
            flops=4 * heads * rows * slots * page_len * hd,
            transcendentals=heads * rows * slots * page_len,
            bytes_accessed=heads * (slots * page_len * 2 * hd * 2 + rows * hd * 6),
        ),
    )(jnp.reshape(kv0, (1,)).astype(jnp.int32), q_k, kv_local, kv_local, bias, cos2, sin2)


def axis_reduce(x, axis, op):
    n = lax.axis_size(axis)
    d = 1
    while d < n:
        x = op(x, lax.ppermute(x, axis, perm=[(i, i ^ d) for i in range(n)]))
        d *= 2
    return x


def bit_scatter(block, axis):
    n = lax.axis_size(axis)
    idx = lax.axis_index(axis)
    d = 1
    while d < n:
        bit = (idx // d) % 2
        keep = lax.dynamic_index_in_dim(block, bit, 0, keepdims=False)
        send = lax.dynamic_index_in_dim(block, 1 - bit, 0, keepdims=False)
        block = keep + lax.ppermute(send, axis, perm=[(i, i ^ d) for i in range(n)])
        d *= 2
    return block


def bit_gather(x, axis):
    n = lax.axis_size(axis)
    idx = lax.axis_index(axis)
    dists = []
    d = n // 2
    while d >= 1:
        other = lax.ppermute(x, axis, perm=[(i, i ^ d) for i in range(n)])
        low = (idx // d) % 2 == 0
        x = jnp.stack([jnp.where(low, x, other), jnp.where(low, other, x)])
        dists.insert(0, d)
        d //= 2
    k = len(dists)
    order = sorted(range(k), key=lambda j: -dists[j])
    x = jnp.transpose(x, tuple(order) + tuple(range(k, x.ndim)))
    return x.reshape((n * x.shape[k],) + x.shape[k + 1 :])


def scatter_rows(x, axis):
    n = lax.axis_size(axis)
    if n & (n - 1):
        return lax.psum_scatter(x, axis, scatter_dimension=0, tiled=True)
    bits = n.bit_length() - 1
    x = x.reshape((2,) * bits + (x.shape[0] // n,) + x.shape[1:])
    x = jnp.transpose(x, tuple(range(bits - 1, -1, -1)) + tuple(range(bits, x.ndim)))
    return bit_scatter(x, axis)


def direct_scatter(x, axis):
    n = lax.axis_size(axis)
    idx = lax.axis_index(axis)
    blocks = x.reshape((n, x.shape[0] // n) + x.shape[1:])
    total = lax.dynamic_index_in_dim(blocks, idx, 0, keepdims=False)
    for k in range(1, n):
        piece = lax.dynamic_index_in_dim(blocks, (idx + k) % n, 0, keepdims=False)
        total = total + lax.ppermute(piece, axis, perm=[(i, (i + k) % n) for i in range(n)])
    return total


def axis_sum(x, axis):
    n = lax.axis_size(axis)
    if n & (n - 1):
        return lax.psum(x, axis)
    return axis_reduce(x, axis, jnp.add)


def axis_max(x, axes):
    if any(lax.axis_size(a) & (lax.axis_size(a) - 1) for a in axes):
        return jnp.max(lax.all_gather(x, axes), axis=0)
    for a in axes:
        n = lax.axis_size(a)
        others = [lax.ppermute(x, a, perm=[(i, (i + k) % n) for i in range(n)]) for k in range(1, n)]
        for other in others:
            x = jnp.maximum(x, other)
    return x


def body(x_new, kv_pages, w_query, w_keyval, w_out, lengths, page_store, offsets):
    tensors = lax.axis_size("tensor")
    shards = lax.axis_size("store")
    tensor_idx = lax.axis_index("tensor")
    store_idx = lax.axis_index("store")
    tok_count = x_new.shape[0]
    assert tok_count == TURN and lengths.shape[0] == 1
    local_slots = kv_pages.shape[1]
    capacity = local_slots * tensors
    page_len = kv_pages.shape[2]
    kv_heads = kv_pages.shape[3] // (2 * HD)
    group_size = HQ // KVH
    local_heads = w_query.shape[1] // HD
    local_kv = max(1, local_heads // group_size)
    local_group = local_heads // local_kv
    freq_table = inverse_freq(HD)
    kv_first = tensor_idx * local_heads // group_size
    keyval_cols = lax.dynamic_slice_in_dim(w_keyval, kv_first * (2 * HD), local_kv * 2 * HD, 1)
    query_part = jnp.dot(x_new, w_query, preferred_element_type=jnp.float32)
    keyval_part = jnp.dot(x_new, keyval_cols, preferred_element_type=jnp.float32)
    keyval_sum = axis_sum(keyval_part, "store")
    keyval_local = keyval_sum.reshape(tok_count, local_kv, 2, HD)
    tok_ids = jnp.arange(tok_count, dtype=jnp.int32)
    tok_sess = tok_ids // TURN
    tok_pos = table_lookup(lengths, tok_sess) + tok_ids % TURN
    tok_angle = tok_pos.astype(jnp.float32)[:, None, None] * freq_table
    if local_heads % shards == 0 and not shards & (shards - 1):
        s_bits = shards.bit_length() - 1
        heads_major = jnp.transpose(query_part.reshape(tok_count, local_heads, HD), (1, 0, 2))
        block = heads_major.reshape((2,) * s_bits + (local_heads // shards, tok_count, HD))
        block = jnp.transpose(block, tuple(range(s_bits - 1, -1, -1)) + tuple(range(s_bits, s_bits + 3)))
        block = bit_scatter(block, "store")
        block = to_half(rotate(block, jnp.transpose(tok_angle, (1, 0, 2))))
        q_heads = bit_gather(block, "store")
        query_rot = jnp.transpose(q_heads, (1, 0, 2))
        q_all = bit_gather(block, "tensor")
        if tensors & (tensors - 1):
            q_all = None
        else:
            q_all = bit_gather(q_all, "store").reshape((shards, tensors) + block.shape)
            q_all = jnp.transpose(q_all, (1, 0, 2, 3, 4)).reshape((HQ,) + block.shape[1:])
    else:
        query_sum = axis_sum(query_part, "store")
        query_rot = to_half(rotate(query_sum.reshape(tok_count, local_heads, HD), tok_angle))
        q_heads = jnp.transpose(query_rot, (1, 0, 2))
        q_all = None
    key_new = to_half(rotate(keyval_local[:, :, 0], tok_angle))
    value_new = to_half(keyval_local[:, :, 1])

    first_slot = store_idx * capacity + tensor_idx * local_slots
    key_sess, key_ok, key_off = slot_meta(
        page_store, lengths, offsets, shards, capacity, first_slot, local_slots, page_len
    )
    pb = local_slots
    bias = jnp.where(key_ok, 0.0, MASK_FILL).astype(jnp.float32)
    bias = bias.reshape(local_slots // pb, 1, pb * page_len)
    hist_angle = offsets[0].astype(jnp.float32) * freq_table
    kv_local = kv_pages.reshape(local_slots, page_len, kv_pages.shape[3])
    cosine = jnp.cos(hist_angle)
    sine = jnp.sin(hist_angle)
    cos2 = jnp.concatenate([cosine, cosine])[None, :]
    sin2 = jnp.concatenate([-sine, sine])[None, :]

    if q_all is None and tensors & (tensors - 1):
        q_all = lax.all_gather(q_heads, "tensor", axis=0, tiled=True)
    elif q_all is None:
        q_all = bit_gather(q_heads, "tensor")
    q_k = q_all.reshape(kv_heads, group_size * tok_count, HD)
    if local_heads % group_size == 0:
        own = hist_attend(
            kv_first, q_heads.reshape(local_kv, group_size * tok_count, HD), kv_local, bias, cos2, sin2, pb
        )
        rest_first = kv_first + local_kv
        q_rest = lax.dynamic_slice_in_dim(
            jnp.concatenate([q_k, q_k], axis=0), rest_first % kv_heads, kv_heads - local_kv, 0
        )
        rest = hist_attend(rest_first % kv_heads, q_rest, kv_local, bias, cos2, sin2, pb)
        parts = []
        for first, second in zip(own, rest):
            rolled = jnp.concatenate([first, second, first, second], axis=0)
            parts.append(lax.dynamic_slice_in_dim(rolled, kv_heads - kv_first, kv_heads, 0))
        acc, top, total = parts
    else:
        acc, top, total = hist_attend(jnp.int32(0), q_k, kv_local, bias, cos2, sin2, pb)
    acc = acc.reshape(HQ, tok_count, HD)
    top = top.reshape(HQ, tok_count)
    total = total.reshape(HQ, tok_count)

    glob_top = axis_max(top, ("store", "tensor"))
    factor = jnp.exp(top - glob_top)
    packed = jnp.concatenate(
        [(acc * factor[..., None]).reshape(HQ, tok_count * HD), total * factor], axis=1
    )
    new_allowed = (tok_sess[:, None] == tok_sess[None, :]) & (tok_ids[None, :] <= tok_ids[:, None])
    chunk_heads = HQ // (tensors * shards)
    if (
        HQ % (tensors * shards) == 0
        and group_size % chunk_heads == 0
        and not shards & (shards - 1)
        and not tensors & (tensors - 1)
    ):
        width = packed.shape[1]
        s_bits = shards.bit_length() - 1
        t_bits = tensors.bit_length() - 1
        block = packed.reshape((2,) * t_bits + (2,) * s_bits + (chunk_heads, width))
        order = tuple(range(t_bits + s_bits - 1, t_bits - 1, -1)) + tuple(range(t_bits))
        block = jnp.transpose(block, order + (t_bits + s_bits, t_bits + s_bits + 1))
        block = bit_scatter(block, "store")
        block = direct_scatter(block.reshape(tensors * chunk_heads, width), "tensor")
        acc = block[:, : tok_count * HD].reshape(chunk_heads, tok_count, HD)
        total = block[:, tok_count * HD :]
        chunk_first = (tensor_idx * shards + store_idx) * chunk_heads
        loc_top = lax.dynamic_slice_in_dim(glob_top, chunk_first, chunk_heads, 0)
        hist_part = (jnp.transpose(loc_top), jnp.transpose(total), jnp.transpose(acc, (1, 0, 2)))
        in_group = store_idx * chunk_heads
        query_chunk = lax.dynamic_slice_in_dim(query_rot, in_group, chunk_heads, 1)
        kv_idx = in_group // group_size
        key_chunk = lax.dynamic_slice_in_dim(key_new, kv_idx, 1, 1)
        value_chunk = lax.dynamic_slice_in_dim(value_new, kv_idx, 1, 1)
        new_part = attend(
            query_chunk.reshape(tok_count, 1, chunk_heads, HD), key_chunk, value_chunk, new_allowed
        )
        new_flat = (
            new_part[0].reshape(tok_count, chunk_heads),
            new_part[1].reshape(tok_count, chunk_heads),
            new_part[2].reshape(tok_count, chunk_heads, HD),
        )
        combined = combine(hist_part, new_flat)
        attended = (
            (combined[2] / combined[1][..., None])
            .reshape(tok_count, chunk_heads * HD)
            .astype(jnp.bfloat16)
        )
        attended = lax.all_gather(attended, "store", axis=1, tiled=True)
    else:
        packed = lax.psum_scatter(packed, "tensor", scatter_dimension=0, tiled=True)
        packed = axis_sum(packed, "store")
        acc = packed[:, : tok_count * HD].reshape(local_heads, tok_count, HD)
        total = packed[:, tok_count * HD :]
        loc_top = lax.dynamic_slice_in_dim(glob_top, tensor_idx * local_heads, local_heads, 0)
        hist_part = (
            jnp.transpose(loc_top),
            jnp.transpose(total),
            jnp.transpose(acc, (1, 0, 2)),
        )

        query_local = query_rot.reshape(tok_count, local_kv, local_group, HD)
        new_part = attend(query_local, key_new, value_new, new_allowed)
        new_flat = (
            new_part[0].reshape(tok_count, local_heads),
            new_part[1].reshape(tok_count, local_heads),
            new_part[2].reshape(tok_count, local_heads, HD),
        )
        combined = combine(hist_part, new_flat)
        attended = (
            (combined[2] / combined[1][..., None])
            .reshape(tok_count, local_heads * HD)
            .astype(jnp.bfloat16)
        )
    result = direct_scatter(jnp.dot(attended, w_out, preferred_element_type=jnp.float32), "tensor")
    return result.astype(jnp.bfloat16)


def solution(mesh):
    in_specs = (
        P("groups", "store"),
        P(("groups", "store"), "tensor", None, None),
        P("store", "tensor"),
        P("store", None),
        P("tensor", "store"),
        P("groups"),
        P("groups", None),
        P("groups"),
    )
    out_specs = P(("groups", "tensor"), "store")
    return jax.shard_map(body, mesh=mesh, in_specs=in_specs, out_specs=out_specs, check_vma=False)
```

```python
import math

import jax
import jax.numpy as jnp
import numpy as np
from jax import lax
from jax.sharding import PartitionSpec as P
from jax.experimental import pallas as pl
from jax.experimental.pallas import tpu as pltpu
import functools

HQ = 64
KVH = 8
HD = 128
TURN = 64
MAXPAGES = 256


THETA = 500000.0
NEG_FILL = -1e30
ROPE_FACTOR = 8.0
LOW_FACTOR = 1.0
HIGH_FACTOR = 4.0
INITIAL_CONTEXT = 8192.0


def joined(x, axis, combine):
    everything = jax.tree.map(lambda part: lax.all_gather(part, axis), x)
    first = jax.tree.map(lambda part: part[0], everything)

    def step(k, so_far):
        return combine(so_far, jax.tree.map(lambda part: part[k], everything))

    return lax.fori_loop(1, lax.axis_size(axis), step, first)


def inverse_freq(width):
    steps_half = jnp.arange(width // 2, dtype=jnp.float32)
    base_freq = jnp.exp(-(steps_half * (2.0 / width)) * jnp.log(jnp.float32(THETA)))
    wavelength = 2.0 * math.pi / base_freq
    low_wave = INITIAL_CONTEXT / LOW_FACTOR
    high_wave = INITIAL_CONTEXT / HIGH_FACTOR
    smooth = (INITIAL_CONTEXT / wavelength - LOW_FACTOR) / (HIGH_FACTOR - LOW_FACTOR)
    blended = (1.0 - smooth) * base_freq / ROPE_FACTOR + smooth * base_freq
    scaled = jnp.where(wavelength > low_wave, base_freq / ROPE_FACTOR, blended)
    return jnp.where(wavelength < high_wave, base_freq, scaled)


def rotate(values, rot_angle):
    half_width = values.shape[-1] // 2
    first_half = values[..., :half_width]
    second_half = values[..., half_width:]
    cosine = jnp.cos(rot_angle)
    sine_part = jnp.sin(rot_angle)
    return jnp.concatenate(
        [
            first_half * cosine - second_half * sine_part,
            second_half * cosine + first_half * sine_part,
        ],
        axis=-1,
    )


def to_half(values):
    return values.astype(jnp.bfloat16)


def table_lookup(table, index):
    hits = index[..., None] == jnp.arange(table.shape[0], dtype=jnp.int32)
    return jnp.sum(jnp.where(hits, table, 0), axis=-1)


def page_positions(page_store, shards, capacity):
    store_of = page_store[:, 0]
    onehot = (store_of[:, None] == jnp.arange(shards, dtype=jnp.int32)[None, :]).astype(jnp.int32)
    ranks = jnp.sum((jnp.cumsum(onehot, axis=0) - onehot) * onehot, axis=1)
    return store_of * capacity + ranks


def slot_meta(page_store, lengths, offsets, shards, capacity, first_slot, slot_count, page_len):
    positions = page_positions(page_store, shards, capacity)
    wanted = first_slot + jnp.arange(slot_count, dtype=jnp.int32)
    matches = (positions[:, None] == wanted[None, :]).astype(jnp.int32)
    page_ids = jnp.sum(matches * jnp.arange(positions.shape[0], dtype=jnp.int32)[:, None], axis=0)
    filled = jnp.sum(matches, axis=0) > 0
    slot_sess = page_ids // MAXPAGES
    slot_page = page_ids % MAXPAGES
    key_pos = slot_page[:, None] * page_len + jnp.arange(page_len, dtype=jnp.int32)[None, :]
    key_ok = filled[:, None] & (key_pos < table_lookup(lengths, slot_sess)[:, None])
    key_sess = jnp.broadcast_to(slot_sess[:, None], (slot_count, page_len))
    key_off = jnp.broadcast_to(table_lookup(offsets, slot_sess)[:, None], (slot_count, page_len))
    return (key_sess.reshape(-1), key_ok.reshape(-1), key_off.reshape(-1))


def attend(query, key_rows, value_rows, allowed):
    score_scale = 1.0 / query.shape[-1] ** 0.5
    scores = (
        jnp.einsum("tkgd,nkd->tkgn", query, key_rows, preferred_element_type=jnp.float32)
        * score_scale
    )
    wide_mask = allowed[:, None, None, :]
    scores = jnp.where(wide_mask, scores, NEG_FILL)
    row_top = jnp.max(scores, axis=-1)
    weights = jnp.where(wide_mask, jnp.exp(scores - row_top[..., None]), 0.0)
    weight_sum = jnp.sum(weights, axis=-1)
    head_mix = jnp.einsum(
        "tkgn,nkd->tkgd",
        weights.astype(jnp.bfloat16),
        value_rows,
        preferred_element_type=jnp.float32,
    )
    return (row_top, weight_sum, head_mix)


def combine(first_part, second_part):
    new_top = jnp.maximum(first_part[0], second_part[0])
    first_factor = jnp.exp(first_part[0] - new_top)
    second_factor = jnp.exp(second_part[0] - new_top)
    summed = first_part[1] * first_factor + second_part[1] * second_factor
    mixed_sum = first_part[2] * first_factor[..., None] + second_part[2] * second_factor[..., None]
    return (new_top, summed, mixed_sum)


MASK_FILL = -3e30


def hist_kernel(kv0_ref, q_ref, k_ref, v_ref, bias_ref, cos_ref, sin_ref, acc_out, m_out, l_out, m_sc, l_sc, acc_sc, *, scale, blocks):
    j = pl.program_id(1)

    @pl.when(j == 0)
    def _():
        m_sc[...] = jnp.full(m_sc.shape, NEG_FILL, jnp.float32)
        l_sc[...] = jnp.zeros(l_sc.shape, jnp.float32)
        acc_sc[...] = jnp.zeros(acc_sc.shape, jnp.float32)

    pages, page_len, hd = k_ref.shape
    n = pages * page_len
    keys = k_ref[...].reshape(n, hd).astype(jnp.float32)
    vals = v_ref[...].reshape(n, hd)
    keys = (keys * cos_ref[...] + pltpu.roll(keys, hd // 2, 1) * sin_ref[...]).astype(jnp.bfloat16)
    scores = lax.dot_general(
        q_ref[0], keys, (((1,), (1,)), ((), ())), preferred_element_type=jnp.float32
    )
    scores = scores * scale + bias_ref[0]
    m_old = m_sc[...]
    m_new = jnp.maximum(m_old, jnp.max(scores, axis=1, keepdims=True))
    alpha = jnp.exp(m_old - m_new)
    weights = jnp.exp(scores - m_new)
    l_sc[...] = alpha * l_sc[...] + jnp.sum(weights, axis=1, keepdims=True)
    acc_sc[...] = alpha * acc_sc[...] + jnp.dot(
        weights.astype(jnp.bfloat16), vals, preferred_element_type=jnp.float32
    )
    m_sc[...] = m_new

    @pl.when(j == blocks - 1)
    def _():
        acc_out[0] = acc_sc[...]
        m_out[0] = m_sc[...]
        l_out[0] = l_sc[...]


def hist_attend(kv0, q_k, kv_local, bias, cos2, sin2, pb):
    heads, rows, hd = q_k.shape
    slots, page_len, width = kv_local.shape
    kv_heads = width // (2 * hd)
    blocks = slots // pb
    kernel = functools.partial(hist_kernel, scale=1.0 / hd ** 0.5, blocks=blocks)

    def head_of(h, kv0_ref):
        return (kv0_ref[0] + h) % kv_heads

    grid_spec = pltpu.PrefetchScalarGridSpec(
        num_scalar_prefetch=1,
        grid=(heads, blocks),
        in_specs=[
            pl.BlockSpec((1, rows, hd), lambda h, j, r: (h, 0, 0)),
            pl.BlockSpec((pb, page_len, hd), lambda h, j, r: (j, 0, 2 * head_of(h, r))),
            pl.BlockSpec((pb, page_len, hd), lambda h, j, r: (j, 0, 2 * head_of(h, r) + 1)),
            pl.BlockSpec((1, 1, pb * page_len), lambda h, j, r: (j, 0, 0)),
            pl.BlockSpec((1, hd), lambda h, j, r: (0, 0)),
            pl.BlockSpec((1, hd), lambda h, j, r: (0, 0)),
        ],
        out_specs=[
            pl.BlockSpec((1, rows, hd), lambda h, j, r: (h, 0, 0)),
            pl.BlockSpec((1, rows, 1), lambda h, j, r: (h, 0, 0)),
            pl.BlockSpec((1, rows, 1), lambda h, j, r: (h, 0, 0)),
        ],
        scratch_shapes=[
            pltpu.VMEM((rows, 1), jnp.float32),
            pltpu.VMEM((rows, 1), jnp.float32),
            pltpu.VMEM((rows, hd), jnp.float32),
        ],
    )
    return pl.pallas_call(
        kernel,
        grid_spec=grid_spec,
        out_shape=[
            jax.ShapeDtypeStruct((heads, rows, hd), jnp.float32),
            jax.ShapeDtypeStruct((heads, rows, 1), jnp.float32),
            jax.ShapeDtypeStruct((heads, rows, 1), jnp.float32),
        ],
        compiler_params=pltpu.CompilerParams(dimension_semantics=("arbitrary", "arbitrary")),
        cost_estimate=pl.CostEstimate(
            flops=4 * heads * rows * slots * page_len * hd,
            transcendentals=heads * rows * slots * page_len,
            bytes_accessed=heads * (slots * page_len * 2 * hd * 2 + rows * hd * 6),
        ),
    )(jnp.reshape(kv0, (1,)).astype(jnp.int32), q_k, kv_local, kv_local, bias, cos2, sin2)


def axis_reduce(x, axis, op):
    n = lax.axis_size(axis)
    d = 1
    while d < n:
        x = op(x, lax.ppermute(x, axis, perm=[(i, i ^ d) for i in range(n)]))
        d *= 2
    return x


def bit_scatter(block, axis):
    n = lax.axis_size(axis)
    idx = lax.axis_index(axis)
    d = 1
    while d < n:
        bit = (idx // d) % 2
        keep = lax.dynamic_index_in_dim(block, bit, 0, keepdims=False)
        send = lax.dynamic_index_in_dim(block, 1 - bit, 0, keepdims=False)
        block = keep + lax.ppermute(send, axis, perm=[(i, i ^ d) for i in range(n)])
        d *= 2
    return block


def bit_gather(x, axis):
    n = lax.axis_size(axis)
    idx = lax.axis_index(axis)
    dists = []
    d = n // 2
    while d >= 1:
        other = lax.ppermute(x, axis, perm=[(i, i ^ d) for i in range(n)])
        low = (idx // d) % 2 == 0
        x = jnp.stack([jnp.where(low, x, other), jnp.where(low, other, x)])
        dists.insert(0, d)
        d //= 2
    k = len(dists)
    order = sorted(range(k), key=lambda j: -dists[j])
    x = jnp.transpose(x, tuple(order) + tuple(range(k, x.ndim)))
    return x.reshape((n * x.shape[k],) + x.shape[k + 1 :])


def scatter_rows(x, axis):
    n = lax.axis_size(axis)
    if n & (n - 1):
        return lax.psum_scatter(x, axis, scatter_dimension=0, tiled=True)
    bits = n.bit_length() - 1
    x = x.reshape((2,) * bits + (x.shape[0] // n,) + x.shape[1:])
    x = jnp.transpose(x, tuple(range(bits - 1, -1, -1)) + tuple(range(bits, x.ndim)))
    return bit_scatter(x, axis)


def direct_scatter(x, axis):
    n = lax.axis_size(axis)
    idx = lax.axis_index(axis)
    blocks = x.reshape((n, x.shape[0] // n) + x.shape[1:])
    total = lax.dynamic_index_in_dim(blocks, idx, 0, keepdims=False)
    for k in range(1, n):
        piece = lax.dynamic_index_in_dim(blocks, (idx + k) % n, 0, keepdims=False)
        total = total + lax.ppermute(piece, axis, perm=[(i, (i + k) % n) for i in range(n)])
    return total


def direct_gather(x, axis):
    n = lax.axis_size(axis)
    idx = lax.axis_index(axis)
    out = jnp.zeros((n,) + x.shape, x.dtype)
    out = lax.dynamic_update_index_in_dim(out, x, idx, 0)
    for k in range(1, n):
        got = lax.ppermute(x, axis, perm=[(i, (i + k) % n) for i in range(n)])
        out = lax.dynamic_update_index_in_dim(out, got, (idx - k) % n, 0)
    return out.reshape((n * x.shape[0],) + x.shape[1:])


def axis_sum(x, axis):
    n = lax.axis_size(axis)
    if n & (n - 1):
        return lax.psum(x, axis)
    return axis_reduce(x, axis, jnp.add)


def axis_max(x, axes):
    if any(lax.axis_size(a) & (lax.axis_size(a) - 1) for a in axes):
        return jnp.max(lax.all_gather(x, axes), axis=0)
    for a in axes:
        n = lax.axis_size(a)
        others = [lax.ppermute(x, a, perm=[(i, (i + k) % n) for i in range(n)]) for k in range(1, n)]
        for other in others:
            x = jnp.maximum(x, other)
    return x


def body(x_new, kv_pages, w_query, w_keyval, w_out, lengths, page_store, offsets):
    tensors = lax.axis_size("tensor")
    shards = lax.axis_size("store")
    tensor_idx = lax.axis_index("tensor")
    store_idx = lax.axis_index("store")
    tok_count = x_new.shape[0]
    assert tok_count == TURN and lengths.shape[0] == 1
    local_slots = kv_pages.shape[1]
    capacity = local_slots * tensors
    page_len = kv_pages.shape[2]
    kv_heads = kv_pages.shape[3] // (2 * HD)
    group_size = HQ // KVH
    local_heads = w_query.shape[1] // HD
    local_kv = max(1, local_heads // group_size)
    local_group = local_heads // local_kv
    freq_table = inverse_freq(HD)
    kv_first = tensor_idx * local_heads // group_size
    keyval_cols = lax.dynamic_slice_in_dim(w_keyval, kv_first * (2 * HD), local_kv * 2 * HD, 1)
    query_part = jnp.dot(x_new, w_query, preferred_element_type=jnp.float32)
    keyval_part = jnp.dot(x_new, keyval_cols, preferred_element_type=jnp.float32)
    keyval_sum = axis_sum(keyval_part, "store")
    keyval_local = keyval_sum.reshape(tok_count, local_kv, 2, HD)
    tok_ids = jnp.arange(tok_count, dtype=jnp.int32)
    tok_sess = tok_ids // TURN
    tok_pos = table_lookup(lengths, tok_sess) + tok_ids % TURN
    tok_angle = tok_pos.astype(jnp.float32)[:, None, None] * freq_table
    if local_heads % shards == 0 and not shards & (shards - 1):
        s_bits = shards.bit_length() - 1
        heads_major = jnp.transpose(query_part.reshape(tok_count, local_heads, HD), (1, 0, 2))
        block = heads_major.reshape((2,) * s_bits + (local_heads // shards, tok_count, HD))
        block = jnp.transpose(block, tuple(range(s_bits - 1, -1, -1)) + tuple(range(s_bits, s_bits + 3)))
        block = bit_scatter(block, "store")
        block = to_half(rotate(block, jnp.transpose(tok_angle, (1, 0, 2))))
        q_heads = bit_gather(block, "store")
        query_rot = jnp.transpose(q_heads, (1, 0, 2))
        q_all = direct_gather(block, "tensor")
        if tensors & (tensors - 1):
            q_all = None
        else:
            q_all = bit_gather(q_all, "store").reshape((shards, tensors) + block.shape)
            q_all = jnp.transpose(q_all, (1, 0, 2, 3, 4)).reshape((HQ,) + block.shape[1:])
    else:
        query_sum = axis_sum(query_part, "store")
        query_rot = to_half(rotate(query_sum.reshape(tok_count, local_heads, HD), tok_angle))
        q_heads = jnp.transpose(query_rot, (1, 0, 2))
        q_all = None
    key_new = to_half(rotate(keyval_local[:, :, 0], tok_angle))
    value_new = to_half(keyval_local[:, :, 1])

    first_slot = store_idx * capacity + tensor_idx * local_slots
    key_sess, key_ok, key_off = slot_meta(
        page_store, lengths, offsets, shards, capacity, first_slot, local_slots, page_len
    )
    pb = local_slots
    bias = jnp.where(key_ok, 0.0, MASK_FILL).astype(jnp.float32)
    bias = bias.reshape(local_slots // pb, 1, pb * page_len)
    hist_angle = offsets[0].astype(jnp.float32) * freq_table
    kv_local = kv_pages.reshape(local_slots, page_len, kv_pages.shape[3])
    cosine = jnp.cos(hist_angle)
    sine = jnp.sin(hist_angle)
    cos2 = jnp.concatenate([cosine, cosine])[None, :]
    sin2 = jnp.concatenate([-sine, sine])[None, :]

    if q_all is None and tensors & (tensors - 1):
        q_all = lax.all_gather(q_heads, "tensor", axis=0, tiled=True)
    elif q_all is None:
        q_all = bit_gather(q_heads, "tensor")
    q_k = q_all.reshape(kv_heads, group_size * tok_count, HD)
    if local_heads % group_size == 0:
        own = hist_attend(
            kv_first, q_heads.reshape(local_kv, group_size * tok_count, HD), kv_local, bias, cos2, sin2, pb
        )
        rest_first = kv_first + local_kv
        q_rest = lax.dynamic_slice_in_dim(
            jnp.concatenate([q_k, q_k], axis=0), rest_first % kv_heads, kv_heads - local_kv, 0
        )
        rest = hist_attend(rest_first % kv_heads, q_rest, kv_local, bias, cos2, sin2, pb)
        parts = []
        for first, second in zip(own, rest):
            rolled = jnp.concatenate([first, second, first, second], axis=0)
            parts.append(lax.dynamic_slice_in_dim(rolled, kv_heads - kv_first, kv_heads, 0))
        acc, top, total = parts
    else:
        acc, top, total = hist_attend(jnp.int32(0), q_k, kv_local, bias, cos2, sin2, pb)
    acc = acc.reshape(HQ, tok_count, HD)
    top = top.reshape(HQ, tok_count)
    total = total.reshape(HQ, tok_count)

    glob_top = axis_max(top, ("store", "tensor"))
    factor = jnp.exp(top - glob_top)
    packed = jnp.concatenate(
        [(acc * factor[..., None]).reshape(HQ, tok_count * HD), total * factor], axis=1
    )
    new_allowed = (tok_sess[:, None] == tok_sess[None, :]) & (tok_ids[None, :] <= tok_ids[:, None])
    chunk_heads = HQ // (tensors * shards)
    if (
        HQ % (tensors * shards) == 0
        and group_size % chunk_heads == 0
        and not shards & (shards - 1)
        and not tensors & (tensors - 1)
    ):
        width = packed.shape[1]
        s_bits = shards.bit_length() - 1
        t_bits = tensors.bit_length() - 1
        block = packed.reshape((2,) * t_bits + (2,) * s_bits + (chunk_heads, width))
        order = tuple(range(t_bits + s_bits - 1, t_bits - 1, -1)) + tuple(range(t_bits))
        block = jnp.transpose(block, order + (t_bits + s_bits, t_bits + s_bits + 1))
        block = bit_scatter(block, "store")
        block = direct_scatter(block.reshape(tensors * chunk_heads, width), "tensor")
        acc = block[:, : tok_count * HD].reshape(chunk_heads, tok_count, HD)
        total = block[:, tok_count * HD :]
        chunk_first = (tensor_idx * shards + store_idx) * chunk_heads
        loc_top = lax.dynamic_slice_in_dim(glob_top, chunk_first, chunk_heads, 0)
        hist_part = (jnp.transpose(loc_top), jnp.transpose(total), jnp.transpose(acc, (1, 0, 2)))
        in_group = store_idx * chunk_heads
        query_chunk = lax.dynamic_slice_in_dim(query_rot, in_group, chunk_heads, 1)
        kv_idx = in_group // group_size
        key_chunk = lax.dynamic_slice_in_dim(key_new, kv_idx, 1, 1)
        value_chunk = lax.dynamic_slice_in_dim(value_new, kv_idx, 1, 1)
        new_part = attend(
            query_chunk.reshape(tok_count, 1, chunk_heads, HD), key_chunk, value_chunk, new_allowed
        )
        new_flat = (
            new_part[0].reshape(tok_count, chunk_heads),
            new_part[1].reshape(tok_count, chunk_heads),
            new_part[2].reshape(tok_count, chunk_heads, HD),
        )
        combined = combine(hist_part, new_flat)
        attended = (
            (combined[2] / combined[1][..., None])
            .reshape(tok_count, chunk_heads * HD)
            .astype(jnp.bfloat16)
        )
        attended = lax.all_gather(attended, "store", axis=1, tiled=True)
    else:
        packed = lax.psum_scatter(packed, "tensor", scatter_dimension=0, tiled=True)
        packed = axis_sum(packed, "store")
        acc = packed[:, : tok_count * HD].reshape(local_heads, tok_count, HD)
        total = packed[:, tok_count * HD :]
        loc_top = lax.dynamic_slice_in_dim(glob_top, tensor_idx * local_heads, local_heads, 0)
        hist_part = (
            jnp.transpose(loc_top),
            jnp.transpose(total),
            jnp.transpose(acc, (1, 0, 2)),
        )

        query_local = query_rot.reshape(tok_count, local_kv, local_group, HD)
        new_part = attend(query_local, key_new, value_new, new_allowed)
        new_flat = (
            new_part[0].reshape(tok_count, local_heads),
            new_part[1].reshape(tok_count, local_heads),
            new_part[2].reshape(tok_count, local_heads, HD),
        )
        combined = combine(hist_part, new_flat)
        attended = (
            (combined[2] / combined[1][..., None])
            .reshape(tok_count, local_heads * HD)
            .astype(jnp.bfloat16)
        )
    result = direct_scatter(jnp.dot(attended, w_out, preferred_element_type=jnp.float32), "tensor")
    return result.astype(jnp.bfloat16)


def solution(mesh):
    in_specs = (
        P("groups", "store"),
        P(("groups", "store"), "tensor", None, None),
        P("store", "tensor"),
        P("store", None),
        P("tensor", "store"),
        P("groups"),
        P("groups", None),
        P("groups"),
    )
    out_specs = P(("groups", "tensor"), "store")
    return jax.shard_map(body, mesh=mesh, in_specs=in_specs, out_specs=out_specs, check_vma=False)
```

```python
import math

import jax
import jax.numpy as jnp
import numpy as np
from jax import lax
from jax.sharding import PartitionSpec as P
from jax.experimental import pallas as pl
from jax.experimental.pallas import tpu as pltpu
import functools

HQ = 64
KVH = 8
HD = 128
TURN = 64
MAXPAGES = 256


THETA = 500000.0
NEG_FILL = -1e30
ROPE_FACTOR = 8.0
LOW_FACTOR = 1.0
HIGH_FACTOR = 4.0
INITIAL_CONTEXT = 8192.0


def joined(x, axis, combine):
    everything = jax.tree.map(lambda part: lax.all_gather(part, axis), x)
    first = jax.tree.map(lambda part: part[0], everything)

    def step(k, so_far):
        return combine(so_far, jax.tree.map(lambda part: part[k], everything))

    return lax.fori_loop(1, lax.axis_size(axis), step, first)


def inverse_freq(width):
    steps_half = jnp.arange(width // 2, dtype=jnp.float32)
    base_freq = jnp.exp(-(steps_half * (2.0 / width)) * jnp.log(jnp.float32(THETA)))
    wavelength = 2.0 * math.pi / base_freq
    low_wave = INITIAL_CONTEXT / LOW_FACTOR
    high_wave = INITIAL_CONTEXT / HIGH_FACTOR
    smooth = (INITIAL_CONTEXT / wavelength - LOW_FACTOR) / (HIGH_FACTOR - LOW_FACTOR)
    blended = (1.0 - smooth) * base_freq / ROPE_FACTOR + smooth * base_freq
    scaled = jnp.where(wavelength > low_wave, base_freq / ROPE_FACTOR, blended)
    return jnp.where(wavelength < high_wave, base_freq, scaled)


def rotate(values, rot_angle):
    half_width = values.shape[-1] // 2
    first_half = values[..., :half_width]
    second_half = values[..., half_width:]
    cosine = jnp.cos(rot_angle)
    sine_part = jnp.sin(rot_angle)
    return jnp.concatenate(
        [
            first_half * cosine - second_half * sine_part,
            second_half * cosine + first_half * sine_part,
        ],
        axis=-1,
    )


def to_half(values):
    return values.astype(jnp.bfloat16)


def table_lookup(table, index):
    hits = index[..., None] == jnp.arange(table.shape[0], dtype=jnp.int32)
    return jnp.sum(jnp.where(hits, table, 0), axis=-1)


def page_positions(page_store, shards, capacity):
    store_of = page_store[:, 0]
    onehot = (store_of[:, None] == jnp.arange(shards, dtype=jnp.int32)[None, :]).astype(jnp.int32)
    ranks = jnp.sum((jnp.cumsum(onehot, axis=0) - onehot) * onehot, axis=1)
    return store_of * capacity + ranks


def slot_meta(page_store, lengths, offsets, shards, capacity, first_slot, slot_count, page_len):
    positions = page_positions(page_store, shards, capacity)
    wanted = first_slot + jnp.arange(slot_count, dtype=jnp.int32)
    matches = (positions[:, None] == wanted[None, :]).astype(jnp.int32)
    page_ids = jnp.sum(matches * jnp.arange(positions.shape[0], dtype=jnp.int32)[:, None], axis=0)
    filled = jnp.sum(matches, axis=0) > 0
    slot_sess = page_ids // MAXPAGES
    slot_page = page_ids % MAXPAGES
    key_pos = slot_page[:, None] * page_len + jnp.arange(page_len, dtype=jnp.int32)[None, :]
    key_ok = filled[:, None] & (key_pos < table_lookup(lengths, slot_sess)[:, None])
    key_sess = jnp.broadcast_to(slot_sess[:, None], (slot_count, page_len))
    key_off = jnp.broadcast_to(table_lookup(offsets, slot_sess)[:, None], (slot_count, page_len))
    return (key_sess.reshape(-1), key_ok.reshape(-1), key_off.reshape(-1))


def attend(query, key_rows, value_rows, allowed):
    score_scale = 1.0 / query.shape[-1] ** 0.5
    scores = (
        jnp.einsum("tkgd,nkd->tkgn", query, key_rows, preferred_element_type=jnp.float32)
        * score_scale
    )
    wide_mask = allowed[:, None, None, :]
    scores = jnp.where(wide_mask, scores, NEG_FILL)
    row_top = jnp.max(scores, axis=-1)
    weights = jnp.where(wide_mask, jnp.exp(scores - row_top[..., None]), 0.0)
    weight_sum = jnp.sum(weights, axis=-1)
    head_mix = jnp.einsum(
        "tkgn,nkd->tkgd",
        weights.astype(jnp.bfloat16),
        value_rows,
        preferred_element_type=jnp.float32,
    )
    return (row_top, weight_sum, head_mix)


def combine(first_part, second_part):
    new_top = jnp.maximum(first_part[0], second_part[0])
    first_factor = jnp.exp(first_part[0] - new_top)
    second_factor = jnp.exp(second_part[0] - new_top)
    summed = first_part[1] * first_factor + second_part[1] * second_factor
    mixed_sum = first_part[2] * first_factor[..., None] + second_part[2] * second_factor[..., None]
    return (new_top, summed, mixed_sum)


MASK_FILL = -3e30


def hist_kernel(kv0_ref, q_ref, k_ref, v_ref, bias_ref, cos_ref, sin_ref, acc_out, m_out, l_out, m_sc, l_sc, acc_sc, *, scale, blocks):
    j = pl.program_id(1)

    @pl.when(j == 0)
    def _():
        m_sc[...] = jnp.full(m_sc.shape, NEG_FILL, jnp.float32)
        l_sc[...] = jnp.zeros(l_sc.shape, jnp.float32)
        acc_sc[...] = jnp.zeros(acc_sc.shape, jnp.float32)

    pages, page_len, hd = k_ref.shape
    n = pages * page_len
    keys = k_ref[...].reshape(n, hd).astype(jnp.float32)
    vals = v_ref[...].reshape(n, hd)
    keys = (keys * cos_ref[...] + pltpu.roll(keys, hd // 2, 1) * sin_ref[...]).astype(jnp.bfloat16)
    scores = lax.dot_general(
        q_ref[0], keys, (((1,), (1,)), ((), ())), preferred_element_type=jnp.float32
    )
    scores = scores * scale + bias_ref[0]
    m_old = m_sc[...]
    m_new = jnp.maximum(m_old, jnp.max(scores, axis=1, keepdims=True))
    alpha = jnp.exp(m_old - m_new)
    weights = jnp.exp(scores - m_new)
    l_sc[...] = alpha * l_sc[...] + jnp.sum(weights, axis=1, keepdims=True)
    acc_sc[...] = alpha * acc_sc[...] + jnp.dot(
        weights.astype(jnp.bfloat16), vals, preferred_element_type=jnp.float32
    )
    m_sc[...] = m_new

    @pl.when(j == blocks - 1)
    def _():
        acc_out[0] = acc_sc[...]
        m_out[0] = m_sc[...]
        l_out[0] = l_sc[...]


def hist_attend(kv0, q_k, kv_local, bias, cos2, sin2, pb):
    heads, rows, hd = q_k.shape
    slots, page_len, width = kv_local.shape
    kv_heads = width // (2 * hd)
    blocks = slots // pb
    kernel = functools.partial(hist_kernel, scale=1.0 / hd ** 0.5, blocks=blocks)

    def head_of(h, kv0_ref):
        return (kv0_ref[0] + h) % kv_heads

    grid_spec = pltpu.PrefetchScalarGridSpec(
        num_scalar_prefetch=1,
        grid=(heads, blocks),
        in_specs=[
            pl.BlockSpec((1, rows, hd), lambda h, j, r: (h, 0, 0)),
            pl.BlockSpec((pb, page_len, hd), lambda h, j, r: (j, 0, 2 * head_of(h, r))),
            pl.BlockSpec((pb, page_len, hd), lambda h, j, r: (j, 0, 2 * head_of(h, r) + 1)),
            pl.BlockSpec((1, 1, pb * page_len), lambda h, j, r: (j, 0, 0)),
            pl.BlockSpec((1, hd), lambda h, j, r: (0, 0)),
            pl.BlockSpec((1, hd), lambda h, j, r: (0, 0)),
        ],
        out_specs=[
            pl.BlockSpec((1, rows, hd), lambda h, j, r: (h, 0, 0)),
            pl.BlockSpec((1, rows, 1), lambda h, j, r: (h, 0, 0)),
            pl.BlockSpec((1, rows, 1), lambda h, j, r: (h, 0, 0)),
        ],
        scratch_shapes=[
            pltpu.VMEM((rows, 1), jnp.float32),
            pltpu.VMEM((rows, 1), jnp.float32),
            pltpu.VMEM((rows, hd), jnp.float32),
        ],
    )
    return pl.pallas_call(
        kernel,
        grid_spec=grid_spec,
        out_shape=[
            jax.ShapeDtypeStruct((heads, rows, hd), jnp.float32),
            jax.ShapeDtypeStruct((heads, rows, 1), jnp.float32),
            jax.ShapeDtypeStruct((heads, rows, 1), jnp.float32),
        ],
        compiler_params=pltpu.CompilerParams(dimension_semantics=("arbitrary", "arbitrary")),
        cost_estimate=pl.CostEstimate(
            flops=4 * heads * rows * slots * page_len * hd,
            transcendentals=heads * rows * slots * page_len,
            bytes_accessed=heads * (slots * page_len * 2 * hd * 2 + rows * hd * 6),
        ),
    )(jnp.reshape(kv0, (1,)).astype(jnp.int32), q_k, kv_local, kv_local, bias, cos2, sin2)


def axis_reduce(x, axis, op):
    n = lax.axis_size(axis)
    d = 1
    while d < n:
        x = op(x, lax.ppermute(x, axis, perm=[(i, i ^ d) for i in range(n)]))
        d *= 2
    return x


def bit_scatter(block, axis):
    n = lax.axis_size(axis)
    idx = lax.axis_index(axis)
    d = 1
    while d < n:
        bit = (idx // d) % 2
        keep = lax.dynamic_index_in_dim(block, bit, 0, keepdims=False)
        send = lax.dynamic_index_in_dim(block, 1 - bit, 0, keepdims=False)
        block = keep + lax.ppermute(send, axis, perm=[(i, i ^ d) for i in range(n)])
        d *= 2
    return block


def bit_gather(x, axis):
    n = lax.axis_size(axis)
    idx = lax.axis_index(axis)
    dists = []
    d = n // 2
    while d >= 1:
        other = lax.ppermute(x, axis, perm=[(i, i ^ d) for i in range(n)])
        low = (idx // d) % 2 == 0
        x = jnp.stack([jnp.where(low, x, other), jnp.where(low, other, x)])
        dists.insert(0, d)
        d //= 2
    k = len(dists)
    order = sorted(range(k), key=lambda j: -dists[j])
    x = jnp.transpose(x, tuple(order) + tuple(range(k, x.ndim)))
    return x.reshape((n * x.shape[k],) + x.shape[k + 1 :])


def scatter_rows(x, axis):
    n = lax.axis_size(axis)
    if n & (n - 1):
        return lax.psum_scatter(x, axis, scatter_dimension=0, tiled=True)
    bits = n.bit_length() - 1
    x = x.reshape((2,) * bits + (x.shape[0] // n,) + x.shape[1:])
    x = jnp.transpose(x, tuple(range(bits - 1, -1, -1)) + tuple(range(bits, x.ndim)))
    return bit_scatter(x, axis)


def direct_scatter(x, axis):
    n = lax.axis_size(axis)
    idx = lax.axis_index(axis)
    blocks = x.reshape((n, x.shape[0] // n) + x.shape[1:])
    total = lax.dynamic_index_in_dim(blocks, idx, 0, keepdims=False)
    for k in range(1, n):
        piece = lax.dynamic_index_in_dim(blocks, (idx + k) % n, 0, keepdims=False)
        total = total + lax.ppermute(piece, axis, perm=[(i, (i + k) % n) for i in range(n)])
    return total


def direct_gather(x, axis):
    n = lax.axis_size(axis)
    idx = lax.axis_index(axis)
    out = jnp.zeros((n,) + x.shape, x.dtype)
    out = lax.dynamic_update_index_in_dim(out, x, idx, 0)
    for k in range(1, n):
        got = lax.ppermute(x, axis, perm=[(i, (i + k) % n) for i in range(n)])
        out = lax.dynamic_update_index_in_dim(out, got, (idx - k) % n, 0)
    return out.reshape((n * x.shape[0],) + x.shape[1:])


def axis_sum(x, axis):
    n = lax.axis_size(axis)
    if n & (n - 1):
        return lax.psum(x, axis)
    return axis_reduce(x, axis, jnp.add)


def axis_max(x, axes):
    if any(lax.axis_size(a) & (lax.axis_size(a) - 1) for a in axes):
        return jnp.max(lax.all_gather(x, axes), axis=0)
    for a in axes:
        n = lax.axis_size(a)
        others = [lax.ppermute(x, a, perm=[(i, (i + k) % n) for i in range(n)]) for k in range(1, n)]
        for other in others:
            x = jnp.maximum(x, other)
    return x


def body(x_new, kv_pages, w_query, w_keyval, w_out, lengths, page_store, offsets):
    tensors = lax.axis_size("tensor")
    shards = lax.axis_size("store")
    tensor_idx = lax.axis_index("tensor")
    store_idx = lax.axis_index("store")
    tok_count = x_new.shape[0]
    assert tok_count == TURN and lengths.shape[0] == 1
    local_slots = kv_pages.shape[1]
    capacity = local_slots * tensors
    page_len = kv_pages.shape[2]
    kv_heads = kv_pages.shape[3] // (2 * HD)
    group_size = HQ // KVH
    local_heads = w_query.shape[1] // HD
    local_kv = max(1, local_heads // group_size)
    local_group = local_heads // local_kv
    freq_table = inverse_freq(HD)
    kv_first = tensor_idx * local_heads // group_size
    keyval_cols = lax.dynamic_slice_in_dim(w_keyval, kv_first * (2 * HD), local_kv * 2 * HD, 1)
    query_part = jnp.dot(x_new, w_query, preferred_element_type=jnp.float32)
    keyval_part = jnp.dot(x_new, keyval_cols, preferred_element_type=jnp.float32)
    keyval_sum = axis_sum(keyval_part, "store")
    keyval_local = keyval_sum.reshape(tok_count, local_kv, 2, HD)
    tok_ids = jnp.arange(tok_count, dtype=jnp.int32)
    tok_sess = tok_ids // TURN
    tok_pos = table_lookup(lengths, tok_sess) + tok_ids % TURN
    tok_angle = tok_pos.astype(jnp.float32)[:, None, None] * freq_table
    if local_heads % shards == 0 and not shards & (shards - 1):
        s_bits = shards.bit_length() - 1
        heads_major = jnp.transpose(query_part.reshape(tok_count, local_heads, HD), (1, 0, 2))
        block = heads_major.reshape((2,) * s_bits + (local_heads // shards, tok_count, HD))
        block = jnp.transpose(block, tuple(range(s_bits - 1, -1, -1)) + tuple(range(s_bits, s_bits + 3)))
        block = bit_scatter(block, "store")
        block = to_half(rotate(block, jnp.transpose(tok_angle, (1, 0, 2))))
        q_heads = direct_gather(block, "store")
        query_rot = jnp.transpose(q_heads, (1, 0, 2))
        q_all = direct_gather(block, "tensor")
        if tensors & (tensors - 1):
            q_all = None
        else:
            q_all = bit_gather(q_all, "store").reshape((shards, tensors) + block.shape)
            q_all = jnp.transpose(q_all, (1, 0, 2, 3, 4)).reshape((HQ,) + block.shape[1:])
    else:
        query_sum = axis_sum(query_part, "store")
        query_rot = to_half(rotate(query_sum.reshape(tok_count, local_heads, HD), tok_angle))
        q_heads = jnp.transpose(query_rot, (1, 0, 2))
        q_all = None
    key_new = to_half(rotate(keyval_local[:, :, 0], tok_angle))
    value_new = to_half(keyval_local[:, :, 1])

    first_slot = store_idx * capacity + tensor_idx * local_slots
    key_sess, key_ok, key_off = slot_meta(
        page_store, lengths, offsets, shards, capacity, first_slot, local_slots, page_len
    )
    pb = local_slots
    bias = jnp.where(key_ok, 0.0, MASK_FILL).astype(jnp.float32)
    bias = bias.reshape(local_slots // pb, 1, pb * page_len)
    hist_angle = offsets[0].astype(jnp.float32) * freq_table
    kv_local = kv_pages.reshape(local_slots, page_len, kv_pages.shape[3])
    cosine = jnp.cos(hist_angle)
    sine = jnp.sin(hist_angle)
    cos2 = jnp.concatenate([cosine, cosine])[None, :]
    sin2 = jnp.concatenate([-sine, sine])[None, :]

    if q_all is None and tensors & (tensors - 1):
        q_all = lax.all_gather(q_heads, "tensor", axis=0, tiled=True)
    elif q_all is None:
        q_all = bit_gather(q_heads, "tensor")
    q_k = q_all.reshape(kv_heads, group_size * tok_count, HD)
    if local_heads % group_size == 0:
        own = hist_attend(
            kv_first, q_heads.reshape(local_kv, group_size * tok_count, HD), kv_local, bias, cos2, sin2, pb
        )
        rest_first = kv_first + local_kv
        q_rest = lax.dynamic_slice_in_dim(
            jnp.concatenate([q_k, q_k], axis=0), rest_first % kv_heads, kv_heads - local_kv, 0
        )
        rest = hist_attend(rest_first % kv_heads, q_rest, kv_local, bias, cos2, sin2, pb)
        parts = []
        for first, second in zip(own, rest):
            rolled = jnp.concatenate([first, second, first, second], axis=0)
            parts.append(lax.dynamic_slice_in_dim(rolled, kv_heads - kv_first, kv_heads, 0))
        acc, top, total = parts
    else:
        acc, top, total = hist_attend(jnp.int32(0), q_k, kv_local, bias, cos2, sin2, pb)
    acc = acc.reshape(HQ, tok_count, HD)
    top = top.reshape(HQ, tok_count)
    total = total.reshape(HQ, tok_count)

    glob_top = axis_max(top, ("store", "tensor"))
    factor = jnp.exp(top - glob_top)
    packed = jnp.concatenate(
        [(acc * factor[..., None]).reshape(HQ, tok_count * HD), total * factor], axis=1
    )
    new_allowed = (tok_sess[:, None] == tok_sess[None, :]) & (tok_ids[None, :] <= tok_ids[:, None])
    chunk_heads = HQ // (tensors * shards)
    if (
        HQ % (tensors * shards) == 0
        and group_size % chunk_heads == 0
        and not shards & (shards - 1)
        and not tensors & (tensors - 1)
    ):
        width = packed.shape[1]
        s_bits = shards.bit_length() - 1
        t_bits = tensors.bit_length() - 1
        block = packed.reshape((2,) * t_bits + (2,) * s_bits + (chunk_heads, width))
        order = tuple(range(t_bits + s_bits - 1, t_bits - 1, -1)) + tuple(range(t_bits))
        block = jnp.transpose(block, order + (t_bits + s_bits, t_bits + s_bits + 1))
        block = bit_scatter(block, "store")
        block = direct_scatter(block.reshape(tensors * chunk_heads, width), "tensor")
        acc = block[:, : tok_count * HD].reshape(chunk_heads, tok_count, HD)
        total = block[:, tok_count * HD :]
        chunk_first = (tensor_idx * shards + store_idx) * chunk_heads
        loc_top = lax.dynamic_slice_in_dim(glob_top, chunk_first, chunk_heads, 0)
        hist_part = (jnp.transpose(loc_top), jnp.transpose(total), jnp.transpose(acc, (1, 0, 2)))
        in_group = store_idx * chunk_heads
        query_chunk = lax.dynamic_slice_in_dim(query_rot, in_group, chunk_heads, 1)
        kv_idx = in_group // group_size
        key_chunk = lax.dynamic_slice_in_dim(key_new, kv_idx, 1, 1)
        value_chunk = lax.dynamic_slice_in_dim(value_new, kv_idx, 1, 1)
        new_part = attend(
            query_chunk.reshape(tok_count, 1, chunk_heads, HD), key_chunk, value_chunk, new_allowed
        )
        new_flat = (
            new_part[0].reshape(tok_count, chunk_heads),
            new_part[1].reshape(tok_count, chunk_heads),
            new_part[2].reshape(tok_count, chunk_heads, HD),
        )
        combined = combine(hist_part, new_flat)
        attended = (
            (combined[2] / combined[1][..., None])
            .reshape(tok_count, chunk_heads * HD)
            .astype(jnp.bfloat16)
        )
        attended = lax.all_gather(attended, "store", axis=1, tiled=True)
    else:
        packed = lax.psum_scatter(packed, "tensor", scatter_dimension=0, tiled=True)
        packed = axis_sum(packed, "store")
        acc = packed[:, : tok_count * HD].reshape(local_heads, tok_count, HD)
        total = packed[:, tok_count * HD :]
        loc_top = lax.dynamic_slice_in_dim(glob_top, tensor_idx * local_heads, local_heads, 0)
        hist_part = (
            jnp.transpose(loc_top),
            jnp.transpose(total),
            jnp.transpose(acc, (1, 0, 2)),
        )

        query_local = query_rot.reshape(tok_count, local_kv, local_group, HD)
        new_part = attend(query_local, key_new, value_new, new_allowed)
        new_flat = (
            new_part[0].reshape(tok_count, local_heads),
            new_part[1].reshape(tok_count, local_heads),
            new_part[2].reshape(tok_count, local_heads, HD),
        )
        combined = combine(hist_part, new_flat)
        attended = (
            (combined[2] / combined[1][..., None])
            .reshape(tok_count, local_heads * HD)
            .astype(jnp.bfloat16)
        )
    result = direct_scatter(jnp.dot(attended, w_out, preferred_element_type=jnp.float32), "tensor")
    return result.astype(jnp.bfloat16)


def solution(mesh):
    in_specs = (
        P("groups", "store"),
        P(("groups", "store"), "tensor", None, None),
        P("store", "tensor"),
        P("store", None),
        P("tensor", "store"),
        P("groups"),
        P("groups", None),
        P("groups"),
    )
    out_specs = P(("groups", "tensor"), "store")
    return jax.shard_map(body, mesh=mesh, in_specs=in_specs, out_specs=out_specs, check_vma=False)
```
